32 devices in a mesh: lat: 8 (over y, x, core), lon: 4 (over z).
Axes of the slice: x: 2, y: 2, z: 4, core: 2. Of those that a mesh axis runs over, the one named last changes fastest.
Arguments:
- fields: bfloat16 [69, 128, 512], P(None, 'lat', 'lon'), may hold values from -6 to 6
- goal_state: bfloat16 [69, 128, 512], P(None, 'lat', 'lon'), may hold values from -6 to 6
- region_mask: int32 [128, 512], P('lat', 'lon'), may hold values from 0 to 63
- region_class: int32 [64], replicated, may hold values from 0 to 7
- entry_filter_stencil: bfloat16 [9, 128, 69], replicated, may hold values from -0.25 to 0.25
- conv_mid: bfloat16 [9, 128, 128], replicated, may hold values from -0.1875 to 0.1875
- patch_in: bfloat16 [4, 4, 128, 1024], replicated, may hold values from -0.125 to 0.125
- norm_gain: float32 [1024], replicated, may hold values from 0.5 to 1.5
- query_weight: bfloat16 [1024, 1024], replicated, may hold values from -3 to 3
- key_weight: bfloat16 [1024, 1024], replicated, may hold values from -1 to 1
- value_weight: bfloat16 [1024, 1024], replicated, may hold values from -0.1875 to 0.1875
- output_weight: bfloat16 [1024, 1024], replicated, may hold values from -0.1875 to 0.1875
- head_scale: float32 [16], replicated, may hold values from 2 to 5
- patch_out: bfloat16 [1024, 4, 4, 128], replicated, may hold values from -0.1875 to 0.1875
- final_convolution_result: bfloat16 [9, 69, 128], replicated, may hold values from -0.1875 to 0.1875
Outputs:
- prediction: bfloat16 [69, 128, 512], P(None, 'lat', 'lon')
- region_loss: float32 [64], replicated
- class_loss: float32 [8], replicated
The draws below stay inside these ranges and needn't reach their ends.
All inputs are finite; a program needn't handle non-finite values.
Results may differ from the reference program's by a relative error of at most 0.015.
Values may be sent and summed in bfloat16 or wider, within the bound.
No kernel may reach another device: no remote copies, remote signals or barrier semaphores. Data moves between devices by JAX's collectives and lax.ppermute only.
A program may use at most 128 MiB of HBM per device.

```python
import math
import jax
import jax.numpy as jnp
from jax import lax

VARS = 69
CONV = 128
D = 1024
HEADS = 16
HEAD_SIZE = 64
CLASSES = 8
REG_DEV = 2
LAT_DEV = 16
LON_DEV = 128
PARALLEL_COUNT = 128
NLON = 512
TOKENS = 4096
REGIONS = 64


def draw_region_mask(key, part):
    coarse = jax.random.randint(jax.random.fold_in(key, 21), (PARALLEL_COUNT // LAT_DEV, NLON // (LON_DEV // 2)), 0, REGIONS)
    blocky = jnp.repeat(jnp.repeat(coarse, LAT_DEV, axis=0), LON_DEV // 2, axis=1)
    scattered = jax.random.randint(jax.random.fold_in(key, 22), (PARALLEL_COUNT, NLON), 0, REGIONS)
    picker = jax.random.randint(jax.random.fold_in(key, 23), (PARALLEL_COUNT, NLON), 0, 4)
    return jnp.where(picker == 0, scattered, blocky).astype(jnp.int32)


def paired_weights(key):
    key_base = jax.random.normal(jax.random.fold_in(key, 31), (D, D), jnp.float32)
    key_mat = jnp.clip(key_base, -6.0, 6.0) * D ** (-0.5)
    noise = jnp.clip(jax.random.normal(jax.random.fold_in(key, 32), (D, D), jnp.float32), -6.0, 6.0) * D ** (-0.5)
    query_mat = noise
    return (query_mat, key_mat)


def draw_query_weight(key, part):
    query_mat, key_mat = paired_weights(key)
    return query_mat.astype(jnp.bfloat16)


def draw_key_weight(key, part):
    query_mat, key_mat = paired_weights(key)
    return key_mat.astype(jnp.bfloat16)


def plant(drawn, own_key, low, largest):
    shape = drawn.shape
    index_at = [jax.random.randint(jax.random.fold_in(own_key, axis), (), 0, shape[axis]) for axis in range(len(shape))]
    drawn = drawn.at[tuple(index_at)].set(low)
    longest = shape.index(max(shape))
    index_at[longest] = (index_at[longest] + 1) % shape[longest]
    return drawn.at[tuple(index_at)].set(largest)


def steps_of(own_key, extent, shards, smallest, high):
    loudness, own = 1.0, jax.random.fold_in(own_key, 6)
    for position, parts in shards:
        heights = jnp.exp(jax.random.uniform(jax.random.fold_in(own, position), (parts,), jnp.float32, smallest / len(shards), high / len(shards)))
        loudness = loudness * jnp.repeat(heights, extent[position] // parts).reshape([-1 if axis == position else 1 for axis in range(len(extent))])
    return loudness


def centred(stream_key, shape, spread, bound, shards=(), dtype=jnp.bfloat16):
    gain = steps_of(stream_key, shape, shards, -0.22, 0.18) if shards else 1.0
    drawn = jax.random.normal(stream_key, shape, jnp.float32) * spread * gain
    return jnp.minimum(jnp.maximum(drawn, -bound), bound).astype(dtype)


def setup_inputs(seed: int = 0) -> dict:
    keys = jax.random.split(jax.random.key(seed), 16)
    fields = centred(keys[0], (VARS, PARALLEL_COUNT, NLON), 1.0, 6.0, ((1, 8), (2, 4)))
    goal_state = centred(keys[1], (VARS, PARALLEL_COUNT, NLON), 1.0, 6.0, ((1, 8), (2, 4)))
    region_mask = draw_region_mask(jax.random.fold_in(keys[15], 71), 0)
    region_class = plant(jax.random.randint(keys[3], (REGIONS,), 0, CLASSES), jax.random.fold_in(keys[3], 1), 0, CLASSES - 1).astype(jnp.int32)
    entry_filter_stencil = centred(keys[4], (9, CONV, VARS), (9 * VARS) ** -0.5, 0.25)
    conv_mid = centred(keys[5], (9, CONV, CONV), (9 * CONV) ** -0.5, 0.1875)
    patch_in = centred(keys[6], (4, 4, CONV, D), (16 * CONV) ** -0.5, 0.125)
    norm_gain = jnp.clip(1.0 + 0.1 * jax.random.normal(keys[7], (D,), jnp.float32), 0.5, 1.5)
    query_weight = draw_query_weight(jax.random.fold_in(keys[15], 71), 0)
    key_weight = draw_key_weight(jax.random.fold_in(keys[15], 71), 0)
    value_weight = centred(keys[10], (D, D), D ** -0.5, 0.1875)
    output_weight = centred(keys[11], (D, D), D ** -0.5, 0.1875)
    head_scale = jnp.clip(jnp.exp(jax.random.uniform(keys[12], (HEADS,), jnp.float32, math.log(2.0), math.log(5.0))), 2.0, 5.0)
    patch_out = centred(keys[13], (D, 4, 4, CONV), D ** -0.5, 0.1875)
    final_convolution_result = centred(keys[14], (9, VARS, CONV), (9 * CONV) ** -0.5, 0.1875)
    return {"fields": fields, "goal_state": goal_state, "region_mask": region_mask, "region_class": region_class, "entry_filter_stencil": entry_filter_stencil, "conv_mid": conv_mid, "patch_in": patch_in, "norm_gain": norm_gain, "query_weight": query_weight, "key_weight": key_weight, "value_weight": value_weight, "output_weight": output_weight, "head_scale": head_scale, "patch_out": patch_out, "final_convolution_result": final_convolution_result}


def periodic_padding(field):
    padded = jnp.pad(field, ((0, 0), (1, 1), (0, 0)))
    return jnp.concatenate([padded[:, :, -1:], padded, padded[:, :, :1]], axis=2)

def convolution_kernel_taps(padded, weight):
    row_count = padded.shape[1] - 2
    col_count = padded.shape[2] - 2
    result = jnp.zeros((weight.shape[1], row_count, col_count), jnp.float32)
    for tap_index in range(9):
        shift_row = tap_index // 3
        shift_col = tap_index % 3
        window = padded[:, shift_row:shift_row + row_count, shift_col:shift_col + col_count]
        result = result + jnp.einsum('oc,cyx->oyx', weight[tap_index].astype(jnp.float32), window.astype(jnp.float32))
    return result

def meridian_area_factor(rows_total, row_first, row_count):
    row_index = jnp.arange(row_count).astype(jnp.float32) + jnp.asarray(row_first).astype(jnp.float32)
    return jnp.cos(math.pi * ((row_index + 0.5) / rows_total - 0.5))

def attend_head(head_inputs):
    queries, key_rows, value_rows, scale = head_inputs
    block_len = math.gcd(queries.shape[0], 2048)
    query_blocks = queries.reshape(-1, block_len, queries.shape[1])
    factor = scale / math.sqrt(HEAD_SIZE)

    def one_block(query_block):
        scores = jnp.dot(query_block, key_rows.T, preferred_element_type=jnp.float32) * factor
        row_max = lax.optimization_barrier(jnp.max(scores, axis=1, keepdims=True))
        weights = jnp.exp(scores - row_max)
        weighted = jnp.dot(weights.astype(jnp.bfloat16), value_rows, preferred_element_type=jnp.float32)
        return (weighted / lax.optimization_barrier(jnp.sum(weights, axis=1, keepdims=True))).astype(jnp.bfloat16)
    return lax.map(one_block, query_blocks).reshape(queries.shape)

def reference(fields, goal_state, region_mask, region_class, entry_filter_stencil, conv_mid, patch_in, norm_gain, query_weight, key_weight, value_weight, output_weight, head_scale, patch_out, final_convolution_result):
    hidden_one = jax.nn.gelu(convolution_kernel_taps(periodic_padding(fields), entry_filter_stencil)).astype(jnp.bfloat16)
    hidden_two = jax.nn.gelu(convolution_kernel_taps(periodic_padding(hidden_one), conv_mid)).astype(jnp.bfloat16)
    grouped = hidden_two.reshape(CONV, PARALLEL_COUNT // 4, 4, NLON // 4, 4).astype(jnp.float32)
    latent = jnp.einsum('hpaqb,abhd->pqd', grouped, patch_in.astype(jnp.float32)).astype(jnp.bfloat16)
    latent_flat = latent.reshape(TOKENS, D)
    latent_wide = latent_flat.astype(jnp.float32)
    normed = (latent_wide * lax.rsqrt(lax.optimization_barrier(jnp.mean(latent_wide * latent_wide, axis=1, keepdims=True)) + 1e-06) * norm_gain).astype(jnp.bfloat16)
    query_proj = jnp.dot(normed, query_weight, preferred_element_type=jnp.float32).astype(jnp.bfloat16)
    key_proj = jnp.dot(normed, key_weight, preferred_element_type=jnp.float32).astype(jnp.bfloat16)
    value_proj = jnp.dot(normed, value_weight, preferred_element_type=jnp.float32).astype(jnp.bfloat16)

    def by_head(matrix):
        return matrix.reshape(TOKENS, HEADS, HEAD_SIZE).transpose(1, 0, 2)
    head_mixed = lax.map(attend_head, (by_head(query_proj), by_head(key_proj), by_head(value_proj), head_scale))
    attended = head_mixed.transpose(1, 0, 2).reshape(TOKENS, D)
    latent_two = (latent_wide + jnp.dot(attended, output_weight, preferred_element_type=jnp.float32)).astype(jnp.bfloat16)
    latent_grid = latent_two.reshape(PARALLEL_COUNT // 4, NLON // 4, D).astype(jnp.float32)
    decoder_output = jax.nn.gelu(jnp.einsum('pqd,dabh->hpaqb', latent_grid, patch_out.astype(jnp.float32)))
    decoder_output = decoder_output.reshape(CONV, PARALLEL_COUNT, NLON).astype(jnp.bfloat16)
    estimated_maps = fields.astype(jnp.float32) + convolution_kernel_taps(periodic_padding(decoder_output), final_convolution_result)
    prediction = estimated_maps.astype(jnp.bfloat16)
    estimate_misfit = estimated_maps - goal_state.astype(jnp.float32)
    point_mismatch = lax.optimization_barrier(jnp.sum(estimate_misfit * estimate_misfit, axis=0)) * meridian_area_factor(PARALLEL_COUNT, 0, PARALLEL_COUNT)[:, None]
    factor = REG_DEV / (VARS * LAT_DEV * LON_DEV)
    region_loss = jax.ops.segment_sum(point_mismatch.reshape(-1), region_mask.reshape(-1), num_segments=REGIONS) * factor
    class_loss = jax.ops.segment_sum(region_loss, region_class, num_segments=CLASSES)
    return (prediction, region_loss, class_loss)
```

```python
import math

import jax
import jax.numpy as jnp
from jax import lax
from jax.sharding import PartitionSpec as P

HEADS = 16
CLASSES = 8
REG_DEV = 2


def halo_padded(array, width):
    lat_size, lon_size = lax.axis_size("lat"), lax.axis_size("lon")

    def lat_pairs(step):
        return [(i, i + step) for i in range(lat_size) if 0 <= i + step < lat_size]

    def lon_pairs(step):
        return [(j, (j + step) % lon_size) for j in range(lon_size)]

    def both_pairs(lat_step, lon_step):
        return [
            (i * lon_size + j, (i + lat_step) * lon_size + (j + lon_step) % lon_size)
            for i in range(lat_size)
            for j in range(lon_size)
            if 0 <= i + lat_step < lat_size
        ]

    top, bottom = array[:, :width], array[:, -width:]
    left, right = array[:, :, :width], array[:, :, -width:]
    from_above = lax.ppermute(bottom, "lat", lat_pairs(1))
    from_below = lax.ppermute(top, "lat", lat_pairs(-1))
    from_left = lax.ppermute(right, "lon", lon_pairs(1))
    from_right = lax.ppermute(left, "lon", lon_pairs(-1))
    grid = ("lat", "lon")
    top_left = lax.ppermute(bottom[:, :, -width:], grid, both_pairs(1, 1))
    top_right = lax.ppermute(bottom[:, :, :width], grid, both_pairs(1, -1))
    bottom_left = lax.ppermute(top[:, :, -width:], grid, both_pairs(-1, 1))
    bottom_right = lax.ppermute(top[:, :, :width], grid, both_pairs(-1, -1))
    upper = jnp.concatenate([top_left, from_above, top_right], axis=2)
    middle = jnp.concatenate([from_left, array, from_right], axis=2)
    lower = jnp.concatenate([bottom_left, from_below, bottom_right], axis=2)
    return jnp.concatenate([upper, middle, lower], axis=1)


def convolution_kernel_taps(padded, weight):
    row_count = padded.shape[1] - 2
    col_count = padded.shape[2] - 2
    result = jnp.zeros((weight.shape[1], row_count, col_count), jnp.float32)
    for tap_index in range(9):
        shift_row = tap_index // 3
        shift_col = tap_index % 3
        window = padded[:, shift_row : shift_row + row_count, shift_col : shift_col + col_count]
        result = result + jnp.einsum(
            "oc,cyx->oyx", weight[tap_index], window, preferred_element_type=jnp.float32
        )
    return result


def meridian_area_factor(rows_total, row_first, row_count):
    row_index = jnp.arange(row_count).astype(jnp.float32) + jnp.asarray(row_first).astype(
        jnp.float32
    )
    return jnp.cos(math.pi * ((row_index + 0.5) / rows_total - 0.5))


def attention_fold(queries, scales):
    query_count, local_attender_count, head_size = queries.shape

    def fold_keys(fold_state, shard_piece, offset):
        key_rows, value_rows = shard_piece
        block_len = math.gcd(key_rows.shape[0], 2048)
        key_blocks = key_rows.reshape(-1, block_len, local_attender_count, head_size)
        value_blocks = value_rows.reshape(-1, block_len, local_attender_count, head_size)

        def scan_step(running, blocks):
            row_max, weight_sum, weighted = running
            key_block, value_block = blocks
            scores = (
                jnp.einsum("qhd,khd->qhk", queries, key_block, preferred_element_type=jnp.float32)
                * scales[None, :, None]
            )
            new_max = jnp.maximum(row_max, jnp.max(scores, axis=2))
            rescale = jnp.exp(row_max - new_max)
            weights = jnp.exp(scores - new_max[:, :, None])
            weight_sum = weight_sum * rescale + jnp.sum(weights, axis=2)
            weighted = weighted * rescale[:, :, None] + jnp.einsum(
                "qhk,khd->qhd",
                weights.astype(jnp.bfloat16),
                value_block,
                preferred_element_type=jnp.float32,
            )
            return ((new_max, weight_sum, weighted), None)

        running, unused = lax.scan(scan_step, fold_state, (key_blocks, value_blocks))
        return running

    fold_start = (
        jnp.full((query_count, local_attender_count), -1e30, jnp.float32),
        jnp.zeros((query_count, local_attender_count), jnp.float32),
        jnp.zeros((query_count, local_attender_count, head_size), jnp.float32),
    )
    return (fold_keys, fold_start)


def finish_heads(fold_state):
    row_max, weight_sum, weighted = fold_state
    head_mixed = weighted / weight_sum[:, :, None]
    return head_mixed.reshape(weighted.shape[0], -1).astype(jnp.bfloat16)


def on_device(
    fields,
    goal_state,
    region_mask,
    region_class,
    entry_filter_stencil,
    conv_mid,
    patch_in,
    norm_gain,
    query_weight,
    key_weight,
    value_weight,
    output_weight,
    head_scale,
    patch_out,
    final_convolution_result,
):
    var_count, lat_rows, lon_cols = fields.shape
    conv_count = entry_filter_stencil.shape[1]
    model_width = query_weight.shape[0]
    head_size = model_width // HEADS
    row_first = lax.axis_index("lat") * lat_rows
    rows_total = lat_rows * lax.axis_size("lat")
    padded = halo_padded(fields, 2)
    hidden_one = jax.nn.gelu(convolution_kernel_taps(padded, entry_filter_stencil))
    extended_row = row_first - 1 + jnp.arange(lat_rows + 2, dtype=jnp.int32)
    inside = (extended_row >= 0) & (extended_row < rows_total)
    hidden_padded = jnp.where(inside[None, :, None], hidden_one, 0.0).astype(jnp.bfloat16)
    hidden_two = jax.nn.gelu(convolution_kernel_taps(hidden_padded, conv_mid)).astype(jnp.bfloat16)
    grouped = hidden_two.reshape(conv_count, lat_rows // 4, 4, lon_cols // 4, 4)
    latent = jnp.einsum(
        "hpaqb,abhd->pqd", grouped, patch_in, preferred_element_type=jnp.float32
    ).astype(jnp.bfloat16)
    latent_flat = latent.reshape(-1, model_width)
    latent_wide = latent_flat.astype(jnp.float32)
    normed = (
        latent_wide
        * lax.rsqrt(jnp.mean(latent_wide * latent_wide, axis=1, keepdims=True) + 1e-06)
        * norm_gain
    ).astype(jnp.bfloat16)
    projected = jnp.concatenate(
        [
            jnp.dot(normed, query_weight, preferred_element_type=jnp.float32),
            jnp.dot(normed, key_weight, preferred_element_type=jnp.float32),
            jnp.dot(normed, value_weight, preferred_element_type=jnp.float32),
        ],
        axis=1,
    ).astype(jnp.bfloat16)
    lon_size = lax.axis_size("lon")
    projected = projected.reshape(-1, 3, lon_size, model_width // lon_size)
    spread = lax.all_to_all(projected, "lon", split_axis=2, concat_axis=0, tiled=True)
    query_spread, key_spread, value_spread = (spread[:, i, 0] for i in range(3))
    local_attender_count = query_spread.shape[1] // head_size
    head_first = lax.axis_index("lon") * local_attender_count
    scales = lax.dynamic_slice_in_dim(head_scale, head_first, local_attender_count) / math.sqrt(
        head_size
    )
    fold_keys, fold_start = attention_fold(
        query_spread.reshape(-1, local_attender_count, head_size), scales
    )
    fold_state = fold_keys(
        fold_start,
        (
            lax.all_gather(key_spread, "lat", axis=0, tiled=True),
            lax.all_gather(value_spread, "lat", axis=0, tiled=True),
        ),
        jnp.int32(0),
    )
    attended = lax.all_to_all(
        finish_heads(fold_state), "lon", split_axis=0, concat_axis=1, tiled=True
    )
    latent_two = (
        latent_wide + jnp.dot(attended, output_weight, preferred_element_type=jnp.float32)
    ).astype(jnp.bfloat16)
    latent_grid = latent_two.reshape(lat_rows // 4, lon_cols // 4, model_width)
    decoder_output = jax.nn.gelu(
        jnp.einsum("pqd,dabh->hpaqb", latent_grid, patch_out, preferred_element_type=jnp.float32)
    )
    decoder_output = decoder_output.reshape(conv_count, lat_rows, lon_cols).astype(jnp.bfloat16)
    decoder_output_padded = halo_padded(decoder_output, 1)
    estimated_maps = fields.astype(jnp.float32) + convolution_kernel_taps(
        decoder_output_padded, final_convolution_result
    )
    prediction = estimated_maps.astype(jnp.bfloat16)
    estimate_misfit = estimated_maps - goal_state.astype(jnp.float32)
    point_mismatch = (
        jnp.sum(estimate_misfit * estimate_misfit, axis=0)
        * meridian_area_factor(rows_total, row_first, lat_rows)[:, None]
    )
    region_count = region_class.shape[0]
    region_onehot = (
        region_mask.reshape(1, -1) == jnp.arange(region_count, dtype=jnp.int32)[:, None]
    ).astype(jnp.float32)
    factor = REG_DEV / (var_count * lat_rows * lon_cols)
    partial_loss = (
        jnp.dot(region_onehot, point_mismatch.reshape(-1), precision=lax.Precision.HIGHEST) * factor
    )
    region_loss = jnp.sum(lax.all_gather(partial_loss, ("lat", "lon")), axis=0)
    class_onehot = (region_class[None, :] == jnp.arange(CLASSES, dtype=jnp.int32)[:, None]).astype(
        jnp.float32
    )
    class_loss = jnp.dot(class_onehot, region_loss, precision=lax.Precision.HIGHEST)
    return (prediction, region_loss, class_loss)


def solution(mesh):
    return jax.shard_map(
        on_device,
        mesh=mesh,
        in_specs=(
            P(None, "lat", "lon"),
            P(None, "lat", "lon"),
            P("lat", "lon"),
            P(),
            P(),
            P(),
            P(),
            P(),
            P(),
            P(),
            P(),
            P(),
            P(),
            P(),
            P(),
        ),
        out_specs=(P(None, "lat", "lon"), P(), P()),
        check_vma=False,
    )
```

```python
import functools
import math

import jax
import jax.numpy as jnp
from jax import lax
from jax.experimental import pallas as pl
from jax.experimental.pallas import tpu as pltpu
from jax.sharding import PartitionSpec as P

HEADS = 16
CLASSES = 8
REG_DEV = 2


def halo_padded(array, width):
    lat_size, lon_size = lax.axis_size("lat"), lax.axis_size("lon")
    down = [(i, i + 1) for i in range(lat_size - 1)]
    up = [(i + 1, i) for i in range(lat_size - 1)]
    from_above = lax.ppermute(array[:, -width:], "lat", down)
    from_below = lax.ppermute(array[:, :width], "lat", up)
    array = jnp.concatenate([from_above, array, from_below], axis=1)
    right = [(j, (j + 1) % lon_size) for j in range(lon_size)]
    left = [((j + 1) % lon_size, j) for j in range(lon_size)]
    from_left = lax.ppermute(array[:, :, -width:], "lon", right)
    from_right = lax.ppermute(array[:, :, :width], "lon", left)
    return jnp.concatenate([from_left, array, from_right], axis=2)


def butterfly_sum(value, axis):
    size, step = lax.axis_size(axis), 1
    while step < size:
        partner = [(i, i ^ step) for i in range(size) if (i ^ step) < size]
        value = value + lax.ppermute(value, axis, partner)
        step *= 2
    return value


def convolution_kernel_taps(padded, weight):
    row_count = padded.shape[1] - 2
    col_count = padded.shape[2] - 2
    result = jnp.zeros((weight.shape[1], row_count, col_count), jnp.float32)
    for tap_index in range(9):
        shift_row = tap_index // 3
        shift_col = tap_index % 3
        window = padded[:, shift_row : shift_row + row_count, shift_col : shift_col + col_count]
        result = result + jnp.einsum(
            "oc,cyx->oyx", weight[tap_index], window, preferred_element_type=jnp.float32
        )
    return result


def meridian_area_factor(rows_total, row_first, row_count):
    row_index = jnp.arange(row_count).astype(jnp.float32) + jnp.asarray(row_first).astype(
        jnp.float32
    )
    return jnp.cos(math.pi * ((row_index + 0.5) / rows_total - 0.5))


def attention_kernel(scale_ref, q_ref, k_ref, v_ref, o_ref, *, head_size):
    queries = q_ref[...]
    keys = k_ref[...]
    values = v_ref[...]
    column_head = lax.broadcasted_iota(jnp.int32, queries.shape, 1) // head_size
    total = jnp.zeros(queries.shape, jnp.float32)
    for head in range(queries.shape[1] // head_size):
        in_head = column_head == head
        masked = jnp.where(in_head, queries, jnp.zeros_like(queries))
        scores = lax.dot_general(
            masked, keys, (((1,), (1,)), ((), ())), preferred_element_type=jnp.float32
        ) * scale_ref[head]
        row_max = jnp.max(scores, axis=1, keepdims=True)
        weights = jnp.exp(scores - row_max)
        weight_sum = jnp.sum(weights, axis=1, keepdims=True)
        weighted = jnp.dot(
            weights.astype(jnp.bfloat16), values, preferred_element_type=jnp.float32
        )
        total = jnp.where(in_head, weighted / weight_sum, total)
    o_ref[...] = total.astype(o_ref.dtype)


def attend(queries, keys, values, scales, head_size):
    query_count, width = queries.shape
    key_count = keys.shape[0]
    block = math.gcd(query_count, 256)
    heads = width // head_size
    return pl.pallas_call(
        functools.partial(attention_kernel, head_size=head_size),
        out_shape=jax.ShapeDtypeStruct((query_count, width), jnp.bfloat16),
        grid=(query_count // block,),
        in_specs=[
            pl.BlockSpec(memory_space=pltpu.SMEM),
            pl.BlockSpec((block, width), lambda i: (i, 0)),
            pl.BlockSpec((key_count, width), lambda i: (0, 0)),
            pl.BlockSpec((key_count, width), lambda i: (0, 0)),
        ],
        out_specs=pl.BlockSpec((block, width), lambda i: (i, 0)),
        compiler_params=pltpu.CompilerParams(vmem_limit_bytes=48 * 1024 * 1024),
        cost_estimate=pl.CostEstimate(
            flops=4 * query_count * key_count * width,
            transcendentals=query_count * key_count * heads,
            bytes_accessed=2 * (2 * query_count * width + 2 * key_count * width),
        ),
    )(scales, queries, keys, values)


def on_device(
    fields,
    goal_state,
    region_mask,
    region_class,
    entry_filter_stencil,
    conv_mid,
    patch_in,
    norm_gain,
    query_weight,
    key_weight,
    value_weight,
    output_weight,
    head_scale,
    patch_out,
    final_convolution_result,
):
    var_count, lat_rows, lon_cols = fields.shape
    conv_count = entry_filter_stencil.shape[1]
    model_width = query_weight.shape[0]
    head_size = model_width // HEADS
    row_first = lax.axis_index("lat") * lat_rows
    rows_total = lat_rows * lax.axis_size("lat")
    padded = halo_padded(fields, 2)
    hidden_one = jax.nn.gelu(convolution_kernel_taps(padded, entry_filter_stencil))
    extended_row = row_first - 1 + jnp.arange(lat_rows + 2, dtype=jnp.int32)
    inside = (extended_row >= 0) & (extended_row < rows_total)
    hidden_padded = jnp.where(inside[None, :, None], hidden_one, 0.0).astype(jnp.bfloat16)
    hidden_two = jax.nn.gelu(convolution_kernel_taps(hidden_padded, conv_mid)).astype(jnp.bfloat16)
    grouped = hidden_two.reshape(conv_count, lat_rows // 4, 4, lon_cols // 4, 4)
    latent = jnp.einsum(
        "hpaqb,abhd->pqd", grouped, patch_in, preferred_element_type=jnp.float32
    ).astype(jnp.bfloat16)
    latent_flat = latent.reshape(-1, model_width)
    latent_wide = latent_flat.astype(jnp.float32)
    normed = (
        latent_wide
        * lax.rsqrt(jnp.mean(latent_wide * latent_wide, axis=1, keepdims=True) + 1e-06)
        * norm_gain
    ).astype(jnp.bfloat16)
    lon_size = lax.axis_size("lon")
    group_width = model_width // lon_size
    projections = lax.optimization_barrier(
        tuple(
            jnp.dot(normed, weight, preferred_element_type=jnp.float32).astype(jnp.bfloat16)
            for weight in (query_weight, key_weight, value_weight)
        )
    )
    projected = jnp.stack(
        [p.reshape(-1, lon_size, group_width).transpose(1, 0, 2) for p in projections]
    )
    spread = lax.all_to_all(projected, "lon", split_axis=1, concat_axis=2, tiled=True)
    query_spread, key_spread, value_spread = (spread[i, 0] for i in range(3))
    local_attender_count = query_spread.shape[1] // head_size
    head_first = lax.axis_index("lon") * local_attender_count
    scales = lax.dynamic_slice_in_dim(head_scale, head_first, local_attender_count) / math.sqrt(
        head_size
    )
    attended_heads = attend(
        query_spread,
        lax.all_gather(key_spread, "lat", axis=0, tiled=True),
        lax.all_gather(value_spread, "lat", axis=0, tiled=True),
        scales,
        head_size,
    )
    attended = lax.all_to_all(attended_heads, "lon", split_axis=0, concat_axis=1, tiled=True)
    latent_two = (
        latent_wide + jnp.dot(attended, output_weight, preferred_element_type=jnp.float32)
    ).astype(jnp.bfloat16)
    latent_grid = latent_two.reshape(lat_rows // 4, lon_cols // 4, model_width)
    decoder_output = jax.nn.gelu(
        jnp.einsum("pqd,dabh->hpaqb", latent_grid, patch_out, preferred_element_type=jnp.float32)
    )
    decoder_output = decoder_output.reshape(conv_count, lat_rows, lon_cols).astype(jnp.bfloat16)
    decoder_output_padded = halo_padded(decoder_output, 1)
    estimated_maps = fields.astype(jnp.float32) + convolution_kernel_taps(
        decoder_output_padded, final_convolution_result
    )
    prediction = estimated_maps.astype(jnp.bfloat16)
    estimate_misfit = estimated_maps - goal_state.astype(jnp.float32)
    point_mismatch = (
        jnp.sum(estimate_misfit * estimate_misfit, axis=0)
        * meridian_area_factor(rows_total, row_first, lat_rows)[:, None]
    )
    region_count = region_class.shape[0]
    region_onehot = (
        region_mask.reshape(1, -1) == jnp.arange(region_count, dtype=jnp.int32)[:, None]
    ).astype(jnp.float32)
    factor = REG_DEV / (var_count * lat_rows * lon_cols)
    partial_loss = (
        jnp.dot(region_onehot, point_mismatch.reshape(-1), precision=lax.Precision.HIGHEST) * factor
    )
    region_loss = butterfly_sum(butterfly_sum(partial_loss, "lon"), "lat")
    class_onehot = (region_class[None, :] == jnp.arange(CLASSES, dtype=jnp.int32)[:, None]).astype(
        jnp.float32
    )
    class_loss = jnp.dot(class_onehot, region_loss, precision=lax.Precision.HIGHEST)
    return (prediction, region_loss, class_loss)


def solution(mesh):
    return jax.shard_map(
        on_device,
        mesh=mesh,
        in_specs=(
            P(None, "lat", "lon"),
            P(None, "lat", "lon"),
            P("lat", "lon"),
            P(),
            P(),
            P(),
            P(),
            P(),
            P(),
            P(),
            P(),
            P(),
            P(),
            P(),
            P(),
        ),
        out_specs=(P(None, "lat", "lon"), P(), P()),
        check_vma=False,
    )
```

```python
import functools
import math

import jax
import jax.numpy as jnp
from jax import lax
from jax.experimental import pallas as pl
from jax.experimental.pallas import tpu as pltpu
from jax.sharding import PartitionSpec as P

HEADS = 16
CLASSES = 8
REG_DEV = 2


def halo_padded(array, width):
    lat_size, lon_size = lax.axis_size("lat"), lax.axis_size("lon")
    down = [(i, i + 1) for i in range(lat_size - 1)]
    up = [(i + 1, i) for i in range(lat_size - 1)]
    from_above = lax.ppermute(array[:, -width:], "lat", down)
    from_below = lax.ppermute(array[:, :width], "lat", up)
    array = jnp.concatenate([from_above, array, from_below], axis=1)
    right = [(j, (j + 1) % lon_size) for j in range(lon_size)]
    left = [((j + 1) % lon_size, j) for j in range(lon_size)]
    from_left = lax.ppermute(array[:, :, -width:], "lon", right)
    from_right = lax.ppermute(array[:, :, :width], "lon", left)
    return jnp.concatenate([from_left, array, from_right], axis=2)


def butterfly_sum(value, axis):
    size, step = lax.axis_size(axis), 1
    while step < size:
        partner = [(i, i ^ step) for i in range(size) if (i ^ step) < size]
        value = value + lax.ppermute(value, axis, partner)
        step *= 2
    return value


def convolution_kernel_taps(padded, weight):
    row_count = padded.shape[1] - 2
    col_count = padded.shape[2] - 2
    result = jnp.zeros((weight.shape[1], row_count, col_count), jnp.float32)
    for tap_index in range(9):
        shift_row = tap_index // 3
        shift_col = tap_index % 3
        window = padded[:, shift_row : shift_row + row_count, shift_col : shift_col + col_count]
        result = result + jnp.einsum(
            "oc,cyx->oyx", weight[tap_index], window, preferred_element_type=jnp.float32
        )
    return result


def meridian_area_factor(rows_total, row_first, row_count):
    row_index = jnp.arange(row_count).astype(jnp.float32) + jnp.asarray(row_first).astype(
        jnp.float32
    )
    return jnp.cos(math.pi * ((row_index + 0.5) / rows_total - 0.5))


def attention_kernel(scale_ref, q_ref, k_ref, v_ref, o_ref, *, head_size):
    queries = q_ref[...]
    keys = k_ref[...]
    values = v_ref[...]
    column_head = lax.broadcasted_iota(jnp.int32, queries.shape, 1) // head_size
    total = jnp.zeros(queries.shape, jnp.float32)
    for head in range(queries.shape[1] // head_size):
        in_head = column_head == head
        masked = jnp.where(in_head, queries, jnp.zeros_like(queries))
        scores = lax.dot_general(
            masked, keys, (((1,), (1,)), ((), ())), preferred_element_type=jnp.float32
        ) * scale_ref[head]
        row_max = jnp.max(scores, axis=1, keepdims=True)
        weights = jnp.exp(scores - row_max)
        weight_sum = jnp.sum(weights, axis=1, keepdims=True)
        weighted = jnp.dot(
            weights.astype(jnp.bfloat16), values, preferred_element_type=jnp.float32
        )
        total = jnp.where(in_head, weighted / weight_sum, total)
    o_ref[...] = total.astype(o_ref.dtype)


def attend(queries, keys, values, scales, head_size):
    query_count, width = queries.shape
    key_count = keys.shape[0]
    block = math.gcd(query_count, max(8, (1 << 20) // key_count))
    heads = width // head_size
    return pl.pallas_call(
        functools.partial(attention_kernel, head_size=head_size),
        out_shape=jax.ShapeDtypeStruct((query_count, width), jnp.bfloat16),
        grid=(query_count // block,),
        in_specs=[
            pl.BlockSpec(memory_space=pltpu.SMEM),
            pl.BlockSpec((block, width), lambda i: (i, 0)),
            pl.BlockSpec((key_count, width), lambda i: (0, 0)),
            pl.BlockSpec((key_count, width), lambda i: (0, 0)),
        ],
        out_specs=pl.BlockSpec((block, width), lambda i: (i, 0)),
        compiler_params=pltpu.CompilerParams(vmem_limit_bytes=48 * 1024 * 1024),
        cost_estimate=pl.CostEstimate(
            flops=4 * query_count * key_count * width,
            transcendentals=query_count * key_count * heads,
            bytes_accessed=2 * (2 * query_count * width + 2 * key_count * width),
        ),
    )(scales, queries, keys, values)


def on_device(
    fields,
    goal_state,
    region_mask,
    region_class,
    entry_filter_stencil,
    conv_mid,
    patch_in,
    norm_gain,
    query_weight,
    key_weight,
    value_weight,
    output_weight,
    head_scale,
    patch_out,
    final_convolution_result,
):
    var_count, lat_rows, lon_cols = fields.shape
    conv_count = entry_filter_stencil.shape[1]
    model_width = query_weight.shape[0]
    head_size = model_width // HEADS
    row_first = lax.axis_index("lat") * lat_rows
    rows_total = lat_rows * lax.axis_size("lat")
    padded = halo_padded(fields, 2)
    hidden_one = jax.nn.gelu(convolution_kernel_taps(padded, entry_filter_stencil))
    extended_row = row_first - 1 + jnp.arange(lat_rows + 2, dtype=jnp.int32)
    inside = (extended_row >= 0) & (extended_row < rows_total)
    hidden_padded = jnp.where(inside[None, :, None], hidden_one, 0.0).astype(jnp.bfloat16)
    hidden_two = jax.nn.gelu(convolution_kernel_taps(hidden_padded, conv_mid)).astype(jnp.bfloat16)
    grouped = hidden_two.reshape(conv_count, lat_rows // 4, 4, lon_cols // 4, 4)
    latent = jnp.einsum(
        "hpaqb,abhd->pqd", grouped, patch_in, preferred_element_type=jnp.float32
    ).astype(jnp.bfloat16)
    latent_flat = latent.reshape(-1, model_width)
    latent_wide = latent_flat.astype(jnp.float32)
    normed = (
        latent_wide
        * lax.rsqrt(jnp.mean(latent_wide * latent_wide, axis=1, keepdims=True) + 1e-06)
        * norm_gain
    ).astype(jnp.bfloat16)
    lon_size = lax.axis_size("lon")
    group_width = model_width // lon_size
    projections = lax.optimization_barrier(
        tuple(
            jnp.dot(normed, weight, preferred_element_type=jnp.float32).astype(jnp.bfloat16)
            for weight in (query_weight, key_weight, value_weight)
        )
    )
    projected = jnp.stack(
        [p.reshape(-1, lon_size, group_width).transpose(1, 0, 2) for p in projections]
    )
    spread = lax.all_to_all(projected, "lon", split_axis=1, concat_axis=2, tiled=True)
    query_spread, key_spread, value_spread = (spread[i, 0] for i in range(3))
    lat_size = lax.axis_size("lat")
    core = lax.axis_index("lat") % 2
    half = group_width // 2
    stacked = jnp.stack([query_spread, key_spread, value_spread])
    low, high = stacked[..., :half], stacked[..., half:]
    mine = jnp.where(core == 0, low, high)
    theirs = jnp.where(core == 0, high, low)
    partner = [(i, i ^ 1) for i in range(lat_size)]
    pair_tokens = jnp.concatenate([mine, lax.ppermute(theirs, "lat", partner)], axis=1)
    key_value = pair_tokens[1:]
    chunks = [key_value] + [
        lax.ppermute(key_value, "lat", [(i, i ^ (2 * d)) for i in range(lat_size)])
        for d in range(1, lat_size // 2)
    ]
    all_key_value = jnp.concatenate(chunks, axis=1)
    local_heads = half // head_size
    head_first = (lax.axis_index("lon") * 2 + core) * local_heads
    scales = lax.dynamic_slice_in_dim(head_scale, head_first, local_heads) / math.sqrt(head_size)
    pair_attended = attend(
        pair_tokens[0], all_key_value[0], all_key_value[1], scales, head_size
    )
    token_count = query_spread.shape[0]
    own_part = pair_attended[:token_count]
    returned = lax.ppermute(pair_attended[token_count:], "lat", partner)
    attended_heads = jnp.where(
        core == 0,
        jnp.concatenate([own_part, returned], axis=1),
        jnp.concatenate([returned, own_part], axis=1),
    )
    attended = lax.all_to_all(attended_heads, "lon", split_axis=0, concat_axis=1, tiled=True)
    latent_two = (
        latent_wide + jnp.dot(attended, output_weight, preferred_element_type=jnp.float32)
    ).astype(jnp.bfloat16)
    latent_grid = latent_two.reshape(lat_rows // 4, lon_cols // 4, model_width)
    decoder_output = jax.nn.gelu(
        jnp.einsum("pqd,dabh->hpaqb", latent_grid, patch_out, preferred_element_type=jnp.float32)
    )
    decoder_output = decoder_output.reshape(conv_count, lat_rows, lon_cols).astype(jnp.bfloat16)
    decoder_output_padded = halo_padded(decoder_output, 1)
    estimated_maps = fields.astype(jnp.float32) + convolution_kernel_taps(
        decoder_output_padded, final_convolution_result
    )
    prediction = estimated_maps.astype(jnp.bfloat16)
    estimate_misfit = estimated_maps - goal_state.astype(jnp.float32)
    point_mismatch = (
        jnp.sum(estimate_misfit * estimate_misfit, axis=0)
        * meridian_area_factor(rows_total, row_first, lat_rows)[:, None]
    )
    region_count = region_class.shape[0]
    region_onehot = (
        region_mask.reshape(1, -1) == jnp.arange(region_count, dtype=jnp.int32)[:, None]
    ).astype(jnp.float32)
    factor = REG_DEV / (var_count * lat_rows * lon_cols)
    partial_loss = (
        jnp.dot(region_onehot, point_mismatch.reshape(-1), precision=lax.Precision.HIGHEST) * factor
    )
    region_loss = butterfly_sum(butterfly_sum(partial_loss, "lon"), "lat")
    class_onehot = (region_class[None, :] == jnp.arange(CLASSES, dtype=jnp.int32)[:, None]).astype(
        jnp.float32
    )
    class_loss = jnp.dot(class_onehot, region_loss, precision=lax.Precision.HIGHEST)
    return (prediction, region_loss, class_loss)


def solution(mesh):
    return jax.shard_map(
        on_device,
        mesh=mesh,
        in_specs=(
            P(None, "lat", "lon"),
            P(None, "lat", "lon"),
            P("lat", "lon"),
            P(),
            P(),
            P(),
            P(),
            P(),
            P(),
            P(),
            P(),
            P(),
            P(),
            P(),
            P(),
        ),
        out_specs=(P(None, "lat", "lon"), P(), P()),
        check_vma=False,
    )
```

```python
import functools
import math

import jax
import jax.numpy as jnp
from jax import lax
from jax.experimental import pallas as pl
from jax.experimental.pallas import tpu as pltpu
from jax.sharding import PartitionSpec as P

HEADS = 16
CLASSES = 8
REG_DEV = 2


def halo_padded(array, width):
    lat_size, lon_size = lax.axis_size("lat"), lax.axis_size("lon")
    down = [(i, i + 1) for i in range(lat_size - 1)]
    up = [(i + 1, i) for i in range(lat_size - 1)]
    from_above = lax.ppermute(array[:, -width:], "lat", down)
    from_below = lax.ppermute(array[:, :width], "lat", up)
    array = jnp.concatenate([from_above, array, from_below], axis=1)
    right = [(j, (j + 1) % lon_size) for j in range(lon_size)]
    left = [((j + 1) % lon_size, j) for j in range(lon_size)]
    from_left = lax.ppermute(array[:, :, -width:], "lon", right)
    from_right = lax.ppermute(array[:, :, :width], "lon", left)
    return jnp.concatenate([from_left, array, from_right], axis=2)


def butterfly_sum(value, axis):
    size, step = lax.axis_size(axis), 1
    while step < size:
        partner = [(i, i ^ step) for i in range(size) if (i ^ step) < size]
        value = value + lax.ppermute(value, axis, partner)
        step *= 2
    return value


def convolution_kernel_taps(padded, weight):
    row_count = padded.shape[1] - 2
    col_count = padded.shape[2] - 2
    result = jnp.zeros((weight.shape[1], row_count, col_count), jnp.float32)
    for tap_index in range(9):
        shift_row = tap_index // 3
        shift_col = tap_index % 3
        window = padded[:, shift_row : shift_row + row_count, shift_col : shift_col + col_count]
        result = result + jnp.einsum(
            "oc,cyx->oyx", weight[tap_index], window, preferred_element_type=jnp.float32
        )
    return result


def meridian_area_factor(rows_total, row_first, row_count):
    row_index = jnp.arange(row_count).astype(jnp.float32) + jnp.asarray(row_first).astype(
        jnp.float32
    )
    return jnp.cos(math.pi * ((row_index + 0.5) / rows_total - 0.5))


def attention_kernel(scale_ref, q_ref, k_ref, v_ref, o_ref, *, head_size):
    queries = q_ref[...]
    keys = k_ref[...]
    values = v_ref[...]
    column_head = lax.broadcasted_iota(jnp.int32, queries.shape, 1) // head_size
    total = jnp.zeros(queries.shape, jnp.float32)
    for head in range(queries.shape[1] // head_size):
        in_head = column_head == head
        masked = jnp.where(in_head, queries, jnp.zeros_like(queries))
        scores = lax.dot_general(
            masked, keys, (((1,), (1,)), ((), ())), preferred_element_type=jnp.float32
        ) * scale_ref[head]
        row_max = jnp.max(scores, axis=1, keepdims=True)
        weights = jnp.exp(scores - row_max)
        weight_sum = jnp.sum(weights, axis=1, keepdims=True)
        weighted = jnp.dot(
            weights.astype(jnp.bfloat16), values, preferred_element_type=jnp.float32
        )
        total = jnp.where(in_head, weighted / weight_sum, total)
    o_ref[...] = total.astype(o_ref.dtype)


def attend(queries, keys, values, scales, head_size):
    query_count, width = queries.shape
    key_count = keys.shape[0]
    block = math.gcd(query_count, max(8, (1 << 20) // key_count))
    heads = width // head_size
    return pl.pallas_call(
        functools.partial(attention_kernel, head_size=head_size),
        out_shape=jax.ShapeDtypeStruct((query_count, width), jnp.bfloat16),
        grid=(query_count // block,),
        in_specs=[
            pl.BlockSpec(memory_space=pltpu.SMEM),
            pl.BlockSpec((block, width), lambda i: (i, 0)),
            pl.BlockSpec((key_count, width), lambda i: (0, 0)),
            pl.BlockSpec((key_count, width), lambda i: (0, 0)),
        ],
        out_specs=pl.BlockSpec((block, width), lambda i: (i, 0)),
        compiler_params=pltpu.CompilerParams(vmem_limit_bytes=48 * 1024 * 1024),
        cost_estimate=pl.CostEstimate(
            flops=4 * query_count * key_count * width,
            transcendentals=query_count * key_count * heads,
            bytes_accessed=2 * (2 * query_count * width + 2 * key_count * width),
        ),
    )(scales, queries, keys, values)


def on_device(
    fields,
    goal_state,
    region_mask,
    region_class,
    entry_filter_stencil,
    conv_mid,
    patch_in,
    norm_gain,
    query_weight,
    key_weight,
    value_weight,
    output_weight,
    head_scale,
    patch_out,
    final_convolution_result,
):
    var_count, lat_rows, lon_cols = fields.shape
    conv_count = entry_filter_stencil.shape[1]
    model_width = query_weight.shape[0]
    head_size = model_width // HEADS
    row_first = lax.axis_index("lat") * lat_rows
    rows_total = lat_rows * lax.axis_size("lat")
    padded = halo_padded(fields, 2)
    hidden_one = jax.nn.gelu(convolution_kernel_taps(padded, entry_filter_stencil))
    extended_row = row_first - 1 + jnp.arange(lat_rows + 2, dtype=jnp.int32)
    inside = (extended_row >= 0) & (extended_row < rows_total)
    hidden_padded = jnp.where(inside[None, :, None], hidden_one, 0.0).astype(jnp.bfloat16)
    hidden_two = jax.nn.gelu(convolution_kernel_taps(hidden_padded, conv_mid)).astype(jnp.bfloat16)
    grouped = hidden_two.reshape(conv_count, lat_rows // 4, 4, lon_cols // 4, 4)
    latent = jnp.einsum(
        "hpaqb,abhd->pqd", grouped, patch_in, preferred_element_type=jnp.float32
    ).astype(jnp.bfloat16)
    latent_flat = latent.reshape(-1, model_width)
    latent_wide = latent_flat.astype(jnp.float32)
    normed = (
        latent_wide
        * lax.rsqrt(jnp.mean(latent_wide * latent_wide, axis=1, keepdims=True) + 1e-06)
        * norm_gain
    ).astype(jnp.bfloat16)
    lon_size = lax.axis_size("lon")
    group_width = model_width // lon_size
    projections = lax.optimization_barrier(
        tuple(
            jnp.dot(normed, weight, preferred_element_type=jnp.float32).astype(jnp.bfloat16)
            for weight in (query_weight, key_weight, value_weight)
        )
    )
    by_group = [p.reshape(-1, lon_size, group_width).transpose(1, 0, 2) for p in projections]
    key_value_spread = lax.all_to_all(
        jnp.stack(by_group[1:]), "lon", split_axis=1, concat_axis=2, tiled=True
    )
    query_spread = lax.all_to_all(by_group[0], "lon", split_axis=0, concat_axis=1, tiled=True)[0]
    key_spread, value_spread = key_value_spread[0, 0], key_value_spread[1, 0]
    lat_size = lax.axis_size("lat")
    core = lax.axis_index("lat") % 2
    half = group_width // 2
    partner = [(i, i ^ 1) for i in range(lat_size)]

    def with_partner(spread):
        low, high = spread[..., :half], spread[..., half:]
        mine = jnp.where(core == 0, low, high)
        theirs = jnp.where(core == 0, high, low)
        return jnp.concatenate([mine, lax.ppermute(theirs, "lat", partner)], axis=-2)

    key_value = with_partner(jnp.stack([key_spread, value_spread]))
    chunks = [key_value] + [
        lax.ppermute(key_value, "lat", [(i, i ^ (2 * d)) for i in range(lat_size)])
        for d in range(1, lat_size // 2)
    ]
    all_key_value = jnp.concatenate(chunks, axis=1)
    pair_queries = with_partner(query_spread)
    local_heads = half // head_size
    head_first = (lax.axis_index("lon") * 2 + core) * local_heads
    scales = lax.dynamic_slice_in_dim(head_scale, head_first, local_heads) / math.sqrt(head_size)
    pair_attended = attend(
        pair_queries, all_key_value[0], all_key_value[1], scales, head_size
    )
    token_count = query_spread.shape[0]
    own_part = pair_attended[:token_count]
    returned = lax.ppermute(pair_attended[token_count:], "lat", partner)
    attended_heads = jnp.where(
        core == 0,
        jnp.concatenate([own_part, returned], axis=1),
        jnp.concatenate([returned, own_part], axis=1),
    )
    attended = lax.all_to_all(attended_heads, "lon", split_axis=0, concat_axis=1, tiled=True)
    latent_two = (
        latent_wide + jnp.dot(attended, output_weight, preferred_element_type=jnp.float32)
    ).astype(jnp.bfloat16)
    latent_grid = latent_two.reshape(lat_rows // 4, lon_cols // 4, model_width)
    decoder_output = jax.nn.gelu(
        jnp.einsum("pqd,dabh->hpaqb", latent_grid, patch_out, preferred_element_type=jnp.float32)
    )
    decoder_output = decoder_output.reshape(conv_count, lat_rows, lon_cols).astype(jnp.bfloat16)
    decoder_output_padded = halo_padded(decoder_output, 1)
    estimated_maps = fields.astype(jnp.float32) + convolution_kernel_taps(
        decoder_output_padded, final_convolution_result
    )
    prediction = estimated_maps.astype(jnp.bfloat16)
    estimate_misfit = estimated_maps - goal_state.astype(jnp.float32)
    point_mismatch = (
        jnp.sum(estimate_misfit * estimate_misfit, axis=0)
        * meridian_area_factor(rows_total, row_first, lat_rows)[:, None]
    )
    region_count = region_class.shape[0]
    region_onehot = (
        region_mask.reshape(1, -1) == jnp.arange(region_count, dtype=jnp.int32)[:, None]
    ).astype(jnp.float32)
    factor = REG_DEV / (var_count * lat_rows * lon_cols)
    partial_loss = (
        jnp.dot(region_onehot, point_mismatch.reshape(-1), precision=lax.Precision.HIGHEST) * factor
    )
    region_loss = butterfly_sum(butterfly_sum(partial_loss, "lon"), "lat")
    class_onehot = (region_class[None, :] == jnp.arange(CLASSES, dtype=jnp.int32)[:, None]).astype(
        jnp.float32
    )
    class_loss = jnp.dot(class_onehot, region_loss, precision=lax.Precision.HIGHEST)
    return (prediction, region_loss, class_loss)


def solution(mesh):
    return jax.shard_map(
        on_device,
        mesh=mesh,
        in_specs=(
            P(None, "lat", "lon"),
            P(None, "lat", "lon"),
            P("lat", "lon"),
            P(),
            P(),
            P(),
            P(),
            P(),
            P(),
            P(),
            P(),
            P(),
            P(),
            P(),
            P(),
        ),
        out_specs=(P(None, "lat", "lon"), P(), P()),
        check_vma=False,
    )
```

```python
import functools
import math

import jax
import jax.numpy as jnp
from jax import lax
from jax.experimental import pallas as pl
from jax.experimental.pallas import tpu as pltpu
from jax.sharding import PartitionSpec as P

HEADS = 16
CLASSES = 8
REG_DEV = 2


def halo_padded(array, width):
    lat_size, lon_size = lax.axis_size("lat"), lax.axis_size("lon")
    down = [(i, i + 1) for i in range(lat_size - 1)]
    up = [(i + 1, i) for i in range(lat_size - 1)]
    from_above = lax.ppermute(array[:, -width:], "lat", down)
    from_below = lax.ppermute(array[:, :width], "lat", up)
    array = jnp.concatenate([from_above, array, from_below], axis=1)
    right = [(j, (j + 1) % lon_size) for j in range(lon_size)]
    left = [((j + 1) % lon_size, j) for j in range(lon_size)]
    from_left = lax.ppermute(array[:, :, -width:], "lon", right)
    from_right = lax.ppermute(array[:, :, :width], "lon", left)
    return jnp.concatenate([from_left, array, from_right], axis=2)


def butterfly_sum(value, axis):
    size, step = lax.axis_size(axis), 1
    while step < size:
        partner = [(i, i ^ step) for i in range(size) if (i ^ step) < size]
        value = value + lax.ppermute(value, axis, partner)
        step *= 2
    return value


def convolution_kernel_taps(padded, weight):
    row_count = padded.shape[1] - 2
    col_count = padded.shape[2] - 2
    result = jnp.zeros((weight.shape[1], row_count, col_count), jnp.float32)
    for tap_index in range(9):
        shift_row = tap_index // 3
        shift_col = tap_index % 3
        window = padded[:, shift_row : shift_row + row_count, shift_col : shift_col + col_count]
        result = result + jnp.einsum(
            "oc,cyx->oyx", weight[tap_index], window, preferred_element_type=jnp.float32
        )
    return result


def meridian_area_factor(rows_total, row_first, row_count):
    row_index = jnp.arange(row_count).astype(jnp.float32) + jnp.asarray(row_first).astype(
        jnp.float32
    )
    return jnp.cos(math.pi * ((row_index + 0.5) / rows_total - 0.5))


def attention_kernel(scale_ref, q_ref, k_ref, v_ref, o_ref, *, head_size):
    queries = q_ref[...]
    keys = k_ref[...]
    values = v_ref[...]
    column_head = lax.broadcasted_iota(jnp.int32, queries.shape, 1) // head_size
    total = jnp.zeros(queries.shape, jnp.float32)
    for head in range(queries.shape[1] // head_size):
        in_head = column_head == head
        masked = jnp.where(in_head, queries, jnp.zeros_like(queries))
        scores = lax.dot_general(
            masked, keys, (((1,), (1,)), ((), ())), preferred_element_type=jnp.float32
        ) * scale_ref[head]
        row_max = jnp.max(scores, axis=1, keepdims=True)
        weights = jnp.exp(scores - row_max)
        weight_sum = jnp.sum(weights, axis=1, keepdims=True)
        weighted = jnp.dot(
            weights.astype(jnp.bfloat16), values, preferred_element_type=jnp.float32
        )
        total = jnp.where(in_head, weighted / weight_sum, total)
    o_ref[...] = total.astype(o_ref.dtype)


def attend(queries, keys, values, scales, head_size):
    query_count, width = queries.shape
    key_count = keys.shape[0]
    block = math.gcd(query_count, max(8, (1 << 20) // key_count))
    heads = width // head_size
    return pl.pallas_call(
        functools.partial(attention_kernel, head_size=head_size),
        out_shape=jax.ShapeDtypeStruct((query_count, width), jnp.bfloat16),
        grid=(query_count // block,),
        in_specs=[
            pl.BlockSpec(memory_space=pltpu.SMEM),
            pl.BlockSpec((block, width), lambda i: (i, 0)),
            pl.BlockSpec((key_count, width), lambda i: (0, 0)),
            pl.BlockSpec((key_count, width), lambda i: (0, 0)),
        ],
        out_specs=pl.BlockSpec((block, width), lambda i: (i, 0)),
        compiler_params=pltpu.CompilerParams(vmem_limit_bytes=48 * 1024 * 1024),
        cost_estimate=pl.CostEstimate(
            flops=4 * query_count * key_count * width,
            transcendentals=query_count * key_count * heads,
            bytes_accessed=2 * (2 * query_count * width + 2 * key_count * width),
        ),
    )(scales, queries, keys, values)


def on_device(
    fields,
    goal_state,
    region_mask,
    region_class,
    entry_filter_stencil,
    conv_mid,
    patch_in,
    norm_gain,
    query_weight,
    key_weight,
    value_weight,
    output_weight,
    head_scale,
    patch_out,
    final_convolution_result,
):
    var_count, lat_rows, lon_cols = fields.shape
    conv_count = entry_filter_stencil.shape[1]
    model_width = query_weight.shape[0]
    head_size = model_width // HEADS
    row_first = lax.axis_index("lat") * lat_rows
    rows_total = lat_rows * lax.axis_size("lat")
    padded = halo_padded(fields, 2)
    hidden_one = jax.nn.gelu(convolution_kernel_taps(padded, entry_filter_stencil))
    extended_row = row_first - 1 + jnp.arange(lat_rows + 2, dtype=jnp.int32)
    inside = (extended_row >= 0) & (extended_row < rows_total)
    hidden_padded = jnp.where(inside[None, :, None], hidden_one, 0.0).astype(jnp.bfloat16)
    hidden_two = jax.nn.gelu(convolution_kernel_taps(hidden_padded, conv_mid)).astype(jnp.bfloat16)
    grouped = hidden_two.reshape(conv_count, lat_rows // 4, 4, lon_cols // 4, 4)
    latent = jnp.einsum(
        "hpaqb,abhd->pqd", grouped, patch_in, preferred_element_type=jnp.float32
    ).astype(jnp.bfloat16)
    latent_flat = latent.reshape(-1, model_width)
    latent_wide = latent_flat.astype(jnp.float32)
    normed = (
        latent_wide
        * lax.rsqrt(jnp.mean(latent_wide * latent_wide, axis=1, keepdims=True) + 1e-06)
        * norm_gain
    ).astype(jnp.bfloat16)
    lon_size = lax.axis_size("lon")
    group_width = model_width // lon_size
    normed_band = lax.all_gather(normed, "lon", axis=0, tiled=True)
    group_first = lax.axis_index("lon") * group_width

    def group_projection(weight):
        group_weight = lax.dynamic_slice_in_dim(weight, group_first, group_width, axis=1)
        return jnp.dot(normed_band, group_weight, preferred_element_type=jnp.float32).astype(
            jnp.bfloat16
        )

    query_spread, key_spread, value_spread = (
        group_projection(weight) for weight in (query_weight, key_weight, value_weight)
    )
    lat_size = lax.axis_size("lat")
    core = lax.axis_index("lat") % 2
    half = group_width // 2
    partner = [(i, i ^ 1) for i in range(lat_size)]

    def with_partner(spread):
        low, high = spread[..., :half], spread[..., half:]
        mine = jnp.where(core == 0, low, high)
        theirs = jnp.where(core == 0, high, low)
        return jnp.concatenate([mine, lax.ppermute(theirs, "lat", partner)], axis=-2)

    key_value = with_partner(jnp.stack([key_spread, value_spread]))
    chunks = [key_value] + [
        lax.ppermute(key_value, "lat", [(i, i ^ (2 * d)) for i in range(lat_size)])
        for d in range(1, lat_size // 2)
    ]
    all_key_value = jnp.concatenate(chunks, axis=1)
    pair_queries = with_partner(query_spread)
    local_heads = half // head_size
    head_first = (lax.axis_index("lon") * 2 + core) * local_heads
    scales = lax.dynamic_slice_in_dim(head_scale, head_first, local_heads) / math.sqrt(head_size)
    pair_attended = attend(
        pair_queries, all_key_value[0], all_key_value[1], scales, head_size
    )
    token_count = query_spread.shape[0]
    own_part = pair_attended[:token_count]
    returned = lax.ppermute(pair_attended[token_count:], "lat", partner)
    attended_heads = jnp.where(
        core == 0,
        jnp.concatenate([own_part, returned], axis=1),
        jnp.concatenate([returned, own_part], axis=1),
    )
    attended = lax.all_to_all(attended_heads, "lon", split_axis=0, concat_axis=1, tiled=True)
    latent_two = (
        latent_wide + jnp.dot(attended, output_weight, preferred_element_type=jnp.float32)
    ).astype(jnp.bfloat16)
    latent_grid = latent_two.reshape(lat_rows // 4, lon_cols // 4, model_width)
    decoder_output = jax.nn.gelu(
        jnp.einsum("pqd,dabh->hpaqb", latent_grid, patch_out, preferred_element_type=jnp.float32)
    )
    decoder_output = decoder_output.reshape(conv_count, lat_rows, lon_cols).astype(jnp.bfloat16)
    decoder_output_padded = halo_padded(decoder_output, 1)
    estimated_maps = fields.astype(jnp.float32) + convolution_kernel_taps(
        decoder_output_padded, final_convolution_result
    )
    prediction = estimated_maps.astype(jnp.bfloat16)
    estimate_misfit = estimated_maps - goal_state.astype(jnp.float32)
    point_mismatch = (
        jnp.sum(estimate_misfit * estimate_misfit, axis=0)
        * meridian_area_factor(rows_total, row_first, lat_rows)[:, None]
    )
    region_count = region_class.shape[0]
    region_onehot = (
        region_mask.reshape(1, -1) == jnp.arange(region_count, dtype=jnp.int32)[:, None]
    ).astype(jnp.float32)
    factor = REG_DEV / (var_count * lat_rows * lon_cols)
    partial_loss = (
        jnp.dot(region_onehot, point_mismatch.reshape(-1), precision=lax.Precision.HIGHEST) * factor
    )
    region_loss = butterfly_sum(butterfly_sum(partial_loss, "lon"), "lat")
    class_onehot = (region_class[None, :] == jnp.arange(CLASSES, dtype=jnp.int32)[:, None]).astype(
        jnp.float32
    )
    class_loss = jnp.dot(class_onehot, region_loss, precision=lax.Precision.HIGHEST)
    return (prediction, region_loss, class_loss)


def solution(mesh):
    return jax.shard_map(
        on_device,
        mesh=mesh,
        in_specs=(
            P(None, "lat", "lon"),
            P(None, "lat", "lon"),
            P("lat", "lon"),
            P(),
            P(),
            P(),
            P(),
            P(),
            P(),
            P(),
            P(),
            P(),
            P(),
            P(),
            P(),
        ),
        out_specs=(P(None, "lat", "lon"), P(), P()),
        check_vma=False,
    )
```

```python
import functools
import math

import jax
import jax.numpy as jnp
from jax import lax
from jax.experimental import pallas as pl
from jax.experimental.pallas import tpu as pltpu
from jax.sharding import PartitionSpec as P

HEADS = 16
CLASSES = 8
REG_DEV = 2


def halo_padded(array, width):
    lat_size, lon_size = lax.axis_size("lat"), lax.axis_size("lon")
    down = [(i, i + 1) for i in range(lat_size - 1)]
    up = [(i + 1, i) for i in range(lat_size - 1)]
    from_above = lax.ppermute(array[:, -width:], "lat", down)
    from_below = lax.ppermute(array[:, :width], "lat", up)
    array = jnp.concatenate([from_above, array, from_below], axis=1)
    right = [(j, (j + 1) % lon_size) for j in range(lon_size)]
    left = [((j + 1) % lon_size, j) for j in range(lon_size)]
    from_left = lax.ppermute(array[:, :, -width:], "lon", right)
    from_right = lax.ppermute(array[:, :, :width], "lon", left)
    return jnp.concatenate([from_left, array, from_right], axis=2)


def butterfly_sum(value, axis):
    size, step = lax.axis_size(axis), 1
    while step < size:
        partner = [(i, i ^ step) for i in range(size) if (i ^ step) < size]
        value = value + lax.ppermute(value, axis, partner)
        step *= 2
    return value


def convolution_kernel_taps(padded, weight):
    row_count = padded.shape[1] - 2
    col_count = padded.shape[2] - 2
    result = jnp.zeros((weight.shape[1], row_count, col_count), jnp.float32)
    for tap_index in range(9):
        shift_row = tap_index // 3
        shift_col = tap_index % 3
        window = padded[:, shift_row : shift_row + row_count, shift_col : shift_col + col_count]
        result = result + jnp.einsum(
            "oc,cyx->oyx", weight[tap_index], window, preferred_element_type=jnp.float32
        )
    return result


def meridian_area_factor(rows_total, row_first, row_count):
    row_index = jnp.arange(row_count).astype(jnp.float32) + jnp.asarray(row_first).astype(
        jnp.float32
    )
    return jnp.cos(math.pi * ((row_index + 0.5) / rows_total - 0.5))


def attention_kernel(scale_ref, q_ref, k_ref, v_ref, o_ref, *, head_size):
    queries = q_ref[...]
    keys = k_ref[...]
    values = v_ref[...]
    column_head = lax.broadcasted_iota(jnp.int32, queries.shape, 1) // head_size
    total = jnp.zeros(queries.shape, jnp.float32)
    for head in range(queries.shape[1] // head_size):
        in_head = column_head == head
        masked = jnp.where(in_head, queries, jnp.zeros_like(queries))
        scores = lax.dot_general(
            masked, keys, (((1,), (1,)), ((), ())), preferred_element_type=jnp.float32
        ) * scale_ref[head]
        row_max = jnp.max(scores, axis=1, keepdims=True)
        weights = jnp.exp(scores - row_max)
        weight_sum = jnp.sum(weights, axis=1, keepdims=True)
        weighted = jnp.dot(
            weights.astype(jnp.bfloat16), values, preferred_element_type=jnp.float32
        )
        total = jnp.where(in_head, weighted / weight_sum, total)
    o_ref[...] = total.astype(o_ref.dtype)


def attend(queries, keys, values, scales, head_size):
    query_count, width = queries.shape
    key_count = keys.shape[0]
    block = math.gcd(query_count, max(8, (1 << 20) // key_count))
    heads = width // head_size
    return pl.pallas_call(
        functools.partial(attention_kernel, head_size=head_size),
        out_shape=jax.ShapeDtypeStruct((query_count, width), jnp.bfloat16),
        grid=(query_count // block,),
        in_specs=[
            pl.BlockSpec(memory_space=pltpu.SMEM),
            pl.BlockSpec((block, width), lambda i: (i, 0)),
            pl.BlockSpec((key_count, width), lambda i: (0, 0)),
            pl.BlockSpec((key_count, width), lambda i: (0, 0)),
        ],
        out_specs=pl.BlockSpec((block, width), lambda i: (i, 0)),
        compiler_params=pltpu.CompilerParams(vmem_limit_bytes=48 * 1024 * 1024),
        cost_estimate=pl.CostEstimate(
            flops=4 * query_count * key_count * width,
            transcendentals=query_count * key_count * heads,
            bytes_accessed=2 * (2 * query_count * width + 2 * key_count * width),
        ),
    )(scales, queries, keys, values)


def exchange_blocks(blocks, axis):
    size, index = lax.axis_size(axis), lax.axis_index(axis)
    received = [lax.dynamic_index_in_dim(blocks, index, 0, keepdims=False)]
    for shift in range(1, size):
        outgoing = lax.dynamic_index_in_dim(blocks, (index + shift) % size, 0, keepdims=False)
        received.append(
            lax.ppermute(outgoing, axis, [(i, (i + shift) % size) for i in range(size)])
        )
    return received


def return_blocks(blocks, axis):
    size, index = lax.axis_size(axis), lax.axis_index(axis)
    received = [blocks[0]] + [
        lax.ppermute(blocks[shift], axis, [((i + shift) % size, i) for i in range(size)])
        for shift in range(1, size)
    ]
    rotated = jnp.stack(received + received)
    return lax.dynamic_slice_in_dim(rotated, size - index, size, axis=0)


def on_device(
    fields,
    goal_state,
    region_mask,
    region_class,
    entry_filter_stencil,
    conv_mid,
    patch_in,
    norm_gain,
    query_weight,
    key_weight,
    value_weight,
    output_weight,
    head_scale,
    patch_out,
    final_convolution_result,
):
    var_count, lat_rows, lon_cols = fields.shape
    conv_count = entry_filter_stencil.shape[1]
    model_width = query_weight.shape[0]
    head_size = model_width // HEADS
    row_first = lax.axis_index("lat") * lat_rows
    rows_total = lat_rows * lax.axis_size("lat")
    padded = halo_padded(fields, 2)
    hidden_one = jax.nn.gelu(convolution_kernel_taps(padded, entry_filter_stencil))
    extended_row = row_first - 1 + jnp.arange(lat_rows + 2, dtype=jnp.int32)
    inside = (extended_row >= 0) & (extended_row < rows_total)
    hidden_padded = jnp.where(inside[None, :, None], hidden_one, 0.0).astype(jnp.bfloat16)
    hidden_two = jax.nn.gelu(convolution_kernel_taps(hidden_padded, conv_mid)).astype(jnp.bfloat16)
    grouped = hidden_two.reshape(conv_count, lat_rows // 4, 4, lon_cols // 4, 4)
    latent = jnp.einsum(
        "hpaqb,abhd->pqd", grouped, patch_in, preferred_element_type=jnp.float32
    ).astype(jnp.bfloat16)
    latent_flat = latent.reshape(-1, model_width)
    latent_wide = latent_flat.astype(jnp.float32)
    normed = (
        latent_wide
        * lax.rsqrt(jnp.mean(latent_wide * latent_wide, axis=1, keepdims=True) + 1e-06)
        * norm_gain
    ).astype(jnp.bfloat16)
    lon_size = lax.axis_size("lon")
    group_width = model_width // lon_size
    projections = lax.optimization_barrier(
        tuple(
            jnp.dot(normed, weight, preferred_element_type=jnp.float32).astype(jnp.bfloat16)
            for weight in (query_weight, key_weight, value_weight)
        )
    )
    by_group = [p.reshape(-1, lon_size, group_width).transpose(1, 0, 2) for p in projections]
    key_value_spread = jnp.concatenate(
        exchange_blocks(jnp.stack(by_group[1:], axis=1), "lon"), axis=1
    )
    query_spread = jnp.concatenate(exchange_blocks(by_group[0], "lon"), axis=0)
    key_spread, value_spread = key_value_spread[0], key_value_spread[1]
    lat_size = lax.axis_size("lat")
    core = lax.axis_index("lat") % 2
    half = group_width // 2
    partner = [(i, i ^ 1) for i in range(lat_size)]

    def with_partner(spread):
        low, high = spread[..., :half], spread[..., half:]
        mine = jnp.where(core == 0, low, high)
        theirs = jnp.where(core == 0, high, low)
        return jnp.concatenate([mine, lax.ppermute(theirs, "lat", partner)], axis=-2)

    key_value = with_partner(jnp.stack([key_spread, value_spread]))
    chunks = [key_value] + [
        lax.ppermute(key_value, "lat", [(i, i ^ (2 * d)) for i in range(lat_size)])
        for d in range(1, lat_size // 2)
    ]
    all_key_value = jnp.concatenate(chunks, axis=1)
    pair_queries = with_partner(query_spread)
    local_heads = half // head_size
    head_first = (lax.axis_index("lon") * 2 + core) * local_heads
    scales = lax.dynamic_slice_in_dim(head_scale, head_first, local_heads) / math.sqrt(head_size)
    pair_attended = attend(
        pair_queries, all_key_value[0], all_key_value[1], scales, head_size
    )
    token_count = query_spread.shape[0]
    own_part = pair_attended[:token_count]
    returned = lax.ppermute(pair_attended[token_count:], "lat", partner)
    attended_heads = jnp.where(
        core == 0,
        jnp.concatenate([own_part, returned], axis=1),
        jnp.concatenate([returned, own_part], axis=1),
    )
    token_block = attended_heads.shape[0] // lon_size
    attended = return_blocks(
        [attended_heads[d * token_block : (d + 1) * token_block] for d in range(lon_size)], "lon"
    )
    attended = attended.transpose(1, 0, 2).reshape(token_block, model_width)
    latent_two = (
        latent_wide + jnp.dot(attended, output_weight, preferred_element_type=jnp.float32)
    ).astype(jnp.bfloat16)
    latent_grid = latent_two.reshape(lat_rows // 4, lon_cols // 4, model_width)
    decoder_output = jax.nn.gelu(
        jnp.einsum("pqd,dabh->hpaqb", latent_grid, patch_out, preferred_element_type=jnp.float32)
    )
    decoder_output = decoder_output.reshape(conv_count, lat_rows, lon_cols).astype(jnp.bfloat16)
    decoder_output_padded = halo_padded(decoder_output, 1)
    estimated_maps = fields.astype(jnp.float32) + convolution_kernel_taps(
        decoder_output_padded, final_convolution_result
    )
    prediction = estimated_maps.astype(jnp.bfloat16)
    estimate_misfit = estimated_maps - goal_state.astype(jnp.float32)
    point_mismatch = (
        jnp.sum(estimate_misfit * estimate_misfit, axis=0)
        * meridian_area_factor(rows_total, row_first, lat_rows)[:, None]
    )
    region_count = region_class.shape[0]
    region_onehot = (
        region_mask.reshape(1, -1) == jnp.arange(region_count, dtype=jnp.int32)[:, None]
    ).astype(jnp.float32)
    factor = REG_DEV / (var_count * lat_rows * lon_cols)
    partial_loss = (
        jnp.dot(region_onehot, point_mismatch.reshape(-1), precision=lax.Precision.HIGHEST) * factor
    )
    region_loss = butterfly_sum(butterfly_sum(partial_loss, "lon"), "lat")
    class_onehot = (region_class[None, :] == jnp.arange(CLASSES, dtype=jnp.int32)[:, None]).astype(
        jnp.float32
    )
    class_loss = jnp.dot(class_onehot, region_loss, precision=lax.Precision.HIGHEST)
    return (prediction, region_loss, class_loss)


def solution(mesh):
    return jax.shard_map(
        on_device,
        mesh=mesh,
        in_specs=(
            P(None, "lat", "lon"),
            P(None, "lat", "lon"),
            P("lat", "lon"),
            P(),
            P(),
            P(),
            P(),
            P(),
            P(),
            P(),
            P(),
            P(),
            P(),
            P(),
            P(),
        ),
        out_specs=(P(None, "lat", "lon"), P(), P()),
        check_vma=False,
    )
```

```python
import functools
import math

import jax
import jax.numpy as jnp
from jax import lax
from jax.experimental import pallas as pl
from jax.experimental.pallas import tpu as pltpu
from jax.sharding import PartitionSpec as P

HEADS = 16
CLASSES = 8
REG_DEV = 2


def halo_padded(array, width):
    lat_size, lon_size = lax.axis_size("lat"), lax.axis_size("lon")
    down = [(i, i + 1) for i in range(lat_size - 1)]
    up = [(i + 1, i) for i in range(lat_size - 1)]
    from_above = lax.ppermute(array[:, -width:], "lat", down)
    from_below = lax.ppermute(array[:, :width], "lat", up)
    array = jnp.concatenate([from_above, array, from_below], axis=1)
    right = [(j, (j + 1) % lon_size) for j in range(lon_size)]
    left = [((j + 1) % lon_size, j) for j in range(lon_size)]
    from_left = lax.ppermute(array[:, :, -width:], "lon", right)
    from_right = lax.ppermute(array[:, :, :width], "lon", left)
    return jnp.concatenate([from_left, array, from_right], axis=2)


def butterfly_sum(value, axis):
    size, step = lax.axis_size(axis), 1
    while step < size:
        partner = [(i, i ^ step) for i in range(size) if (i ^ step) < size]
        value = value + lax.ppermute(value, axis, partner)
        step *= 2
    return value


def convolution_kernel_taps(padded, weight):
    row_count = padded.shape[1] - 2
    col_count = padded.shape[2] - 2
    result = jnp.zeros((weight.shape[1], row_count, col_count), jnp.float32)
    for tap_index in range(9):
        shift_row = tap_index // 3
        shift_col = tap_index % 3
        window = padded[:, shift_row : shift_row + row_count, shift_col : shift_col + col_count]
        result = result + jnp.einsum(
            "oc,cyx->oyx", weight[tap_index], window, preferred_element_type=jnp.float32
        )
    return result


def meridian_area_factor(rows_total, row_first, row_count):
    row_index = jnp.arange(row_count).astype(jnp.float32) + jnp.asarray(row_first).astype(
        jnp.float32
    )
    return jnp.cos(math.pi * ((row_index + 0.5) / rows_total - 0.5))


def attention_kernel(scale_ref, q_ref, *refs, head_size, chunk_count):
    key_refs, value_refs = refs[:chunk_count], refs[chunk_count : 2 * chunk_count]
    o_ref, m_ref, l_ref = refs[2 * chunk_count :]
    queries = q_ref[...]
    column_head = lax.broadcasted_iota(jnp.int32, queries.shape, 1) // head_size
    total = jnp.zeros(queries.shape, jnp.float32)
    maxima = jnp.zeros(queries.shape, jnp.float32)
    sums = jnp.zeros(queries.shape, jnp.float32)
    for head in range(queries.shape[1] // head_size):
        in_head = column_head == head
        masked = jnp.where(in_head, queries, jnp.zeros_like(queries))
        scores = [
            lax.dot_general(
                masked, key_ref[...], (((1,), (1,)), ((), ())), preferred_element_type=jnp.float32
            )
            * scale_ref[head]
            for key_ref in key_refs
        ]
        row_max = functools.reduce(
            jnp.maximum, [jnp.max(score, axis=1, keepdims=True) for score in scores]
        )
        weighted = None
        weight_sum = None
        for score, value_ref in zip(scores, value_refs):
            weights = jnp.exp(score - row_max)
            chunk_sum = jnp.sum(weights, axis=1, keepdims=True)
            chunk_weighted = jnp.dot(
                weights.astype(jnp.bfloat16), value_ref[...], preferred_element_type=jnp.float32
            )
            weight_sum = chunk_sum if weight_sum is None else weight_sum + chunk_sum
            weighted = chunk_weighted if weighted is None else weighted + chunk_weighted
        total = jnp.where(in_head, weighted, total)
        maxima = jnp.where(in_head, row_max, maxima)
        sums = jnp.where(in_head, weight_sum, sums)
    o_ref[...] = total
    m_ref[...] = maxima
    l_ref[...] = sums


def attend_part(queries, key_chunks, value_chunks, scales, head_size):
    query_count, width = queries.shape
    key_count = sum(chunk.shape[0] for chunk in key_chunks)
    cap = 1 << (max(8, (1 << 20) // key_count).bit_length() - 1)
    block = math.gcd(query_count, cap)
    heads = width // head_size
    part = jax.ShapeDtypeStruct((query_count, width), jnp.float32)
    part_spec = pl.BlockSpec((block, width), lambda i: (i, 0))
    chunk_specs = [
        pl.BlockSpec((chunk.shape[0], width), lambda i: (0, 0))
        for chunk in list(key_chunks) + list(value_chunks)
    ]
    return pl.pallas_call(
        functools.partial(attention_kernel, head_size=head_size, chunk_count=len(key_chunks)),
        out_shape=(part, part, part),
        grid=(query_count // block,),
        in_specs=[
            pl.BlockSpec(memory_space=pltpu.SMEM),
            pl.BlockSpec((block, width), lambda i: (i, 0)),
        ]
        + chunk_specs,
        out_specs=(part_spec, part_spec, part_spec),
        compiler_params=pltpu.CompilerParams(vmem_limit_bytes=48 * 1024 * 1024),
        cost_estimate=pl.CostEstimate(
            flops=4 * query_count * key_count * width,
            transcendentals=query_count * key_count * heads,
            bytes_accessed=2 * (query_count * width + 2 * key_count * width)
            + 12 * query_count * width,
        ),
    )(scales, queries, *key_chunks, *value_chunks)


def merge_parts(first, second):
    total_a, max_a, sum_a = first
    total_b, max_b, sum_b = second
    joint = jnp.maximum(max_a, max_b)
    rescale_a, rescale_b = jnp.exp(max_a - joint), jnp.exp(max_b - joint)
    total = total_a * rescale_a + total_b * rescale_b
    return (total / (sum_a * rescale_a + sum_b * rescale_b)).astype(jnp.bfloat16)


def exchange_blocks(blocks, axis):
    size, index = lax.axis_size(axis), lax.axis_index(axis)
    received = [lax.dynamic_index_in_dim(blocks, index, 0, keepdims=False)]
    for shift in range(1, size):
        outgoing = lax.dynamic_index_in_dim(blocks, (index + shift) % size, 0, keepdims=False)
        received.append(
            lax.ppermute(outgoing, axis, [(i, (i + shift) % size) for i in range(size)])
        )
    return received


def return_blocks(blocks, axis):
    size, index = lax.axis_size(axis), lax.axis_index(axis)
    received = [blocks[0]] + [
        lax.ppermute(blocks[shift], axis, [((i + shift) % size, i) for i in range(size)])
        for shift in range(1, size)
    ]
    rotated = jnp.stack(received + received)
    return lax.dynamic_slice_in_dim(rotated, size - index, size, axis=0)


def on_device(
    fields,
    goal_state,
    region_mask,
    region_class,
    entry_filter_stencil,
    conv_mid,
    patch_in,
    norm_gain,
    query_weight,
    key_weight,
    value_weight,
    output_weight,
    head_scale,
    patch_out,
    final_convolution_result,
):
    var_count, lat_rows, lon_cols = fields.shape
    conv_count = entry_filter_stencil.shape[1]
    model_width = query_weight.shape[0]
    head_size = model_width // HEADS
    row_first = lax.axis_index("lat") * lat_rows
    rows_total = lat_rows * lax.axis_size("lat")
    padded = halo_padded(fields, 2)
    hidden_one = jax.nn.gelu(convolution_kernel_taps(padded, entry_filter_stencil))
    extended_row = row_first - 1 + jnp.arange(lat_rows + 2, dtype=jnp.int32)
    inside = (extended_row >= 0) & (extended_row < rows_total)
    hidden_padded = jnp.where(inside[None, :, None], hidden_one, 0.0).astype(jnp.bfloat16)
    hidden_two = jax.nn.gelu(convolution_kernel_taps(hidden_padded, conv_mid)).astype(jnp.bfloat16)
    grouped = hidden_two.reshape(conv_count, lat_rows // 4, 4, lon_cols // 4, 4)
    latent = jnp.einsum(
        "hpaqb,abhd->pqd", grouped, patch_in, preferred_element_type=jnp.float32
    ).astype(jnp.bfloat16)
    latent_flat = latent.reshape(-1, model_width)
    latent_wide = latent_flat.astype(jnp.float32)
    normed = (
        latent_wide
        * lax.rsqrt(jnp.mean(latent_wide * latent_wide, axis=1, keepdims=True) + 1e-06)
        * norm_gain
    ).astype(jnp.bfloat16)
    lon_size = lax.axis_size("lon")
    group_width = model_width // lon_size
    projections = lax.optimization_barrier(
        tuple(
            jnp.dot(normed, weight, preferred_element_type=jnp.float32).astype(jnp.bfloat16)
            for weight in (query_weight, key_weight, value_weight)
        )
    )
    by_group = [p.reshape(-1, lon_size, group_width).transpose(1, 0, 2) for p in projections]
    key_value_spread = jnp.concatenate(
        exchange_blocks(jnp.stack(by_group[1:], axis=1), "lon"), axis=1
    )
    query_spread = jnp.concatenate(exchange_blocks(by_group[0], "lon"), axis=0)
    key_spread, value_spread = key_value_spread[0], key_value_spread[1]
    lat_size = lax.axis_size("lat")
    core = lax.axis_index("lat") % 2
    half = group_width // 2
    partner = [(i, i ^ 1) for i in range(lat_size)]

    def with_partner(spread):
        low, high = spread[..., :half], spread[..., half:]
        mine = jnp.where(core == 0, low, high)
        theirs = jnp.where(core == 0, high, low)
        return jnp.concatenate([mine, lax.ppermute(theirs, "lat", partner)], axis=-2)

    key_value = with_partner(jnp.stack([key_spread, value_spread]))
    remote_chunks = [
        lax.ppermute(key_value, "lat", [(i, i ^ (2 * d)) for i in range(lat_size)])
        for d in range(1, lat_size // 2)
    ]
    pair_queries = with_partner(query_spread)
    local_heads = half // head_size
    head_first = (lax.axis_index("lon") * 2 + core) * local_heads
    scales = lax.dynamic_slice_in_dim(head_scale, head_first, local_heads) / math.sqrt(head_size)
    pair_attended = merge_parts(
        attend_part(pair_queries, [key_value[0]], [key_value[1]], scales, head_size),
        attend_part(
            pair_queries,
            [chunk[0] for chunk in remote_chunks],
            [chunk[1] for chunk in remote_chunks],
            scales,
            head_size,
        ),
    )
    token_count = query_spread.shape[0]
    own_part = pair_attended[:token_count]
    returned = lax.ppermute(pair_attended[token_count:], "lat", partner)
    attended_heads = jnp.where(
        core == 0,
        jnp.concatenate([own_part, returned], axis=1),
        jnp.concatenate([returned, own_part], axis=1),
    )
    token_block = attended_heads.shape[0] // lon_size
    attended = return_blocks(
        [attended_heads[d * token_block : (d + 1) * token_block] for d in range(lon_size)], "lon"
    )
    attended = attended.transpose(1, 0, 2).reshape(token_block, model_width)
    latent_two = (
        latent_wide + jnp.dot(attended, output_weight, preferred_element_type=jnp.float32)
    ).astype(jnp.bfloat16)
    latent_grid = latent_two.reshape(lat_rows // 4, lon_cols // 4, model_width)
    decoder_output = jax.nn.gelu(
        jnp.einsum("pqd,dabh->hpaqb", latent_grid, patch_out, preferred_element_type=jnp.float32)
    )
    decoder_output = decoder_output.reshape(conv_count, lat_rows, lon_cols).astype(jnp.bfloat16)
    decoder_output_padded = halo_padded(decoder_output, 1)
    estimated_maps = fields.astype(jnp.float32) + convolution_kernel_taps(
        decoder_output_padded, final_convolution_result
    )
    prediction = estimated_maps.astype(jnp.bfloat16)
    estimate_misfit = estimated_maps - goal_state.astype(jnp.float32)
    point_mismatch = (
        jnp.sum(estimate_misfit * estimate_misfit, axis=0)
        * meridian_area_factor(rows_total, row_first, lat_rows)[:, None]
    )
    region_count = region_class.shape[0]
    region_onehot = (
        region_mask.reshape(1, -1) == jnp.arange(region_count, dtype=jnp.int32)[:, None]
    ).astype(jnp.float32)
    factor = REG_DEV / (var_count * lat_rows * lon_cols)
    partial_loss = (
        jnp.dot(region_onehot, point_mismatch.reshape(-1), precision=lax.Precision.HIGHEST) * factor
    )
    region_loss = butterfly_sum(butterfly_sum(partial_loss, "lon"), "lat")
    class_onehot = (region_class[None, :] == jnp.arange(CLASSES, dtype=jnp.int32)[:, None]).astype(
        jnp.float32
    )
    class_loss = jnp.dot(class_onehot, region_loss, precision=lax.Precision.HIGHEST)
    return (prediction, region_loss, class_loss)


def solution(mesh):
    return jax.shard_map(
        on_device,
        mesh=mesh,
        in_specs=(
            P(None, "lat", "lon"),
            P(None, "lat", "lon"),
            P("lat", "lon"),
            P(),
            P(),
            P(),
            P(),
            P(),
            P(),
            P(),
            P(),
            P(),
            P(),
            P(),
            P(),
        ),
        out_specs=(P(None, "lat", "lon"), P(), P()),
        check_vma=False,
    )
```

```python
import functools
import math

import jax
import jax.numpy as jnp
from jax import lax
from jax.experimental import pallas as pl
from jax.experimental.pallas import tpu as pltpu
from jax.sharding import PartitionSpec as P

HEADS = 16
CLASSES = 8
REG_DEV = 2


def halo_padded(array, width):
    lat_size, lon_size = lax.axis_size("lat"), lax.axis_size("lon")
    down = [(i, i + 1) for i in range(lat_size - 1)]
    up = [(i + 1, i) for i in range(lat_size - 1)]
    from_above = lax.ppermute(array[:, -width:], "lat", down)
    from_below = lax.ppermute(array[:, :width], "lat", up)
    array = jnp.concatenate([from_above, array, from_below], axis=1)
    right = [(j, (j + 1) % lon_size) for j in range(lon_size)]
    left = [((j + 1) % lon_size, j) for j in range(lon_size)]
    from_left = lax.ppermute(array[:, :, -width:], "lon", right)
    from_right = lax.ppermute(array[:, :, :width], "lon", left)
    return jnp.concatenate([from_left, array, from_right], axis=2)


def butterfly_sum(value, axis):
    size, step = lax.axis_size(axis), 1
    while step < size:
        partner = [(i, i ^ step) for i in range(size) if (i ^ step) < size]
        value = value + lax.ppermute(value, axis, partner)
        step *= 2
    return value


def convolution_kernel_taps(padded, weight):
    row_count = padded.shape[1] - 2
    col_count = padded.shape[2] - 2
    result = jnp.zeros((weight.shape[1], row_count, col_count), jnp.float32)
    for tap_index in range(9):
        shift_row = tap_index // 3
        shift_col = tap_index % 3
        window = padded[:, shift_row : shift_row + row_count, shift_col : shift_col + col_count]
        result = result + jnp.einsum(
            "oc,cyx->oyx", weight[tap_index], window, preferred_element_type=jnp.float32
        )
    return result


def meridian_area_factor(rows_total, row_first, row_count):
    row_index = jnp.arange(row_count).astype(jnp.float32) + jnp.asarray(row_first).astype(
        jnp.float32
    )
    return jnp.cos(math.pi * ((row_index + 0.5) / rows_total - 0.5))


def attention_kernel(scale_ref, q_ref, *refs, head_size, chunk_count):
    key_refs, value_refs = refs[:chunk_count], refs[chunk_count : 2 * chunk_count]
    o_ref, m_ref, l_ref = refs[2 * chunk_count :]
    queries = q_ref[...]
    column_head = lax.broadcasted_iota(jnp.int32, queries.shape, 1) // head_size
    total = jnp.zeros(queries.shape, jnp.float32)
    maxima = jnp.zeros(queries.shape, jnp.float32)
    sums = jnp.zeros(queries.shape, jnp.float32)
    for head in range(queries.shape[1] // head_size):
        in_head = column_head == head
        masked = jnp.where(in_head, queries, jnp.zeros_like(queries))
        scores = [
            lax.dot_general(
                masked, key_ref[...], (((1,), (1,)), ((), ())), preferred_element_type=jnp.float32
            )
            * scale_ref[head]
            for key_ref in key_refs
        ]
        row_max = functools.reduce(
            jnp.maximum, [jnp.max(score, axis=1, keepdims=True) for score in scores]
        )
        weighted = None
        weight_sum = None
        for score, value_ref in zip(scores, value_refs):
            weights = jnp.exp(score - row_max)
            chunk_sum = jnp.sum(weights, axis=1, keepdims=True)
            chunk_weighted = jnp.dot(
                weights.astype(jnp.bfloat16), value_ref[...], preferred_element_type=jnp.float32
            )
            weight_sum = chunk_sum if weight_sum is None else weight_sum + chunk_sum
            weighted = chunk_weighted if weighted is None else weighted + chunk_weighted
        total = jnp.where(in_head, weighted, total)
        maxima = jnp.where(in_head, row_max, maxima)
        sums = jnp.where(in_head, weight_sum, sums)
    o_ref[...] = total
    m_ref[...] = maxima
    l_ref[...] = sums


def attend_part(queries, key_chunks, value_chunks, scales, head_size):
    query_count, width = queries.shape
    key_count = sum(chunk.shape[0] for chunk in key_chunks)
    cap = 1 << (max(8, (1 << 20) // key_count).bit_length() - 1)
    block = math.gcd(query_count, cap)
    heads = width // head_size
    part = jax.ShapeDtypeStruct((query_count, width), jnp.float32)
    part_spec = pl.BlockSpec((block, width), lambda i: (i, 0))
    chunk_specs = [
        pl.BlockSpec((chunk.shape[0], width), lambda i: (0, 0))
        for chunk in list(key_chunks) + list(value_chunks)
    ]
    return pl.pallas_call(
        functools.partial(attention_kernel, head_size=head_size, chunk_count=len(key_chunks)),
        out_shape=(part, part, part),
        grid=(query_count // block,),
        in_specs=[
            pl.BlockSpec(memory_space=pltpu.SMEM),
            pl.BlockSpec((block, width), lambda i: (i, 0)),
        ]
        + chunk_specs,
        out_specs=(part_spec, part_spec, part_spec),
        compiler_params=pltpu.CompilerParams(vmem_limit_bytes=48 * 1024 * 1024),
        cost_estimate=pl.CostEstimate(
            flops=4 * query_count * key_count * width,
            transcendentals=query_count * key_count * heads,
            bytes_accessed=2 * (query_count * width + 2 * key_count * width)
            + 12 * query_count * width,
        ),
    )(scales, queries, *key_chunks, *value_chunks)


def merge_parts(parts):
    joint = functools.reduce(jnp.maximum, [maxima for total, maxima, sums in parts])
    rescales = [jnp.exp(maxima - joint) for total, maxima, sums in parts]
    total = sum(part[0] * rescale for part, rescale in zip(parts, rescales))
    weight_sum = sum(part[2] * rescale for part, rescale in zip(parts, rescales))
    return (total / weight_sum).astype(jnp.bfloat16)


def exchange_blocks(blocks, axis):
    size, index = lax.axis_size(axis), lax.axis_index(axis)
    received = [lax.dynamic_index_in_dim(blocks, index, 0, keepdims=False)]
    for shift in range(1, size):
        outgoing = lax.dynamic_index_in_dim(blocks, (index + shift) % size, 0, keepdims=False)
        received.append(
            lax.ppermute(outgoing, axis, [(i, (i + shift) % size) for i in range(size)])
        )
    return received


def return_blocks(blocks, axis):
    size, index = lax.axis_size(axis), lax.axis_index(axis)
    received = [blocks[0]] + [
        lax.ppermute(blocks[shift], axis, [((i + shift) % size, i) for i in range(size)])
        for shift in range(1, size)
    ]
    rotated = jnp.stack(received + received)
    return lax.dynamic_slice_in_dim(rotated, size - index, size, axis=0)


def on_device(
    fields,
    goal_state,
    region_mask,
    region_class,
    entry_filter_stencil,
    conv_mid,
    patch_in,
    norm_gain,
    query_weight,
    key_weight,
    value_weight,
    output_weight,
    head_scale,
    patch_out,
    final_convolution_result,
):
    var_count, lat_rows, lon_cols = fields.shape
    conv_count = entry_filter_stencil.shape[1]
    model_width = query_weight.shape[0]
    head_size = model_width // HEADS
    row_first = lax.axis_index("lat") * lat_rows
    rows_total = lat_rows * lax.axis_size("lat")
    padded = halo_padded(fields, 2)
    hidden_one = jax.nn.gelu(convolution_kernel_taps(padded, entry_filter_stencil))
    extended_row = row_first - 1 + jnp.arange(lat_rows + 2, dtype=jnp.int32)
    inside = (extended_row >= 0) & (extended_row < rows_total)
    hidden_padded = jnp.where(inside[None, :, None], hidden_one, 0.0).astype(jnp.bfloat16)
    hidden_two = jax.nn.gelu(convolution_kernel_taps(hidden_padded, conv_mid)).astype(jnp.bfloat16)
    grouped = hidden_two.reshape(conv_count, lat_rows // 4, 4, lon_cols // 4, 4)
    latent = jnp.einsum(
        "hpaqb,abhd->pqd", grouped, patch_in, preferred_element_type=jnp.float32
    ).astype(jnp.bfloat16)
    latent_flat = latent.reshape(-1, model_width)
    latent_wide = latent_flat.astype(jnp.float32)
    normed = (
        latent_wide
        * lax.rsqrt(jnp.mean(latent_wide * latent_wide, axis=1, keepdims=True) + 1e-06)
        * norm_gain
    ).astype(jnp.bfloat16)
    lon_size = lax.axis_size("lon")
    group_width = model_width // lon_size
    projections = lax.optimization_barrier(
        tuple(
            jnp.dot(normed, weight, preferred_element_type=jnp.float32).astype(jnp.bfloat16)
            for weight in (query_weight, key_weight, value_weight)
        )
    )
    by_group = [p.reshape(-1, lon_size, group_width).transpose(1, 0, 2) for p in projections]
    spread = jnp.concatenate(exchange_blocks(jnp.stack(by_group, axis=1), "lon"), axis=1)
    lat_size = lax.axis_size("lat")
    core = lax.axis_index("lat") % 2
    half = group_width // 2
    partner = [(i, i ^ 1) for i in range(lat_size)]

    def with_partner(spread):
        low, high = spread[..., :half], spread[..., half:]
        mine = jnp.where(core == 0, low, high)
        theirs = jnp.where(core == 0, high, low)
        return jnp.concatenate([mine, lax.ppermute(theirs, "lat", partner)], axis=-2)

    pair_spread = with_partner(spread)
    pair_queries, key_value = pair_spread[0], pair_spread[1:]
    remote_chunks = [
        lax.ppermute(key_value, "lat", [(i, i ^ (2 * d)) for i in range(lat_size)])
        for d in range(1, lat_size // 2)
    ]
    local_heads = half // head_size
    head_first = (lax.axis_index("lon") * 2 + core) * local_heads
    scales = lax.dynamic_slice_in_dim(head_scale, head_first, local_heads) / math.sqrt(head_size)
    key_groups = [[key_value], remote_chunks[:1], remote_chunks[1:]]
    parts = [
        attend_part(
            pair_queries,
            [chunk[0] for chunk in group],
            [chunk[1] for chunk in group],
            scales,
            head_size,
        )
        for group in key_groups
        if group
    ]
    pair_attended = merge_parts(parts)
    token_count = spread.shape[1]
    own_part = pair_attended[:token_count]
    returned = lax.ppermute(pair_attended[token_count:], "lat", partner)
    attended_heads = jnp.where(
        core == 0,
        jnp.concatenate([own_part, returned], axis=1),
        jnp.concatenate([returned, own_part], axis=1),
    )
    token_block = attended_heads.shape[0] // lon_size
    attended = return_blocks(
        [attended_heads[d * token_block : (d + 1) * token_block] for d in range(lon_size)], "lon"
    )
    attended = attended.transpose(1, 0, 2).reshape(token_block, model_width)
    latent_two = (
        latent_wide + jnp.dot(attended, output_weight, preferred_element_type=jnp.float32)
    ).astype(jnp.bfloat16)
    latent_grid = latent_two.reshape(lat_rows // 4, lon_cols // 4, model_width)
    decoder_output = jax.nn.gelu(
        jnp.einsum("pqd,dabh->hpaqb", latent_grid, patch_out, preferred_element_type=jnp.float32)
    )
    decoder_output = decoder_output.reshape(conv_count, lat_rows, lon_cols).astype(jnp.bfloat16)
    decoder_output_padded = halo_padded(decoder_output, 1)
    estimated_maps = fields.astype(jnp.float32) + convolution_kernel_taps(
        decoder_output_padded, final_convolution_result
    )
    prediction = estimated_maps.astype(jnp.bfloat16)
    estimate_misfit = estimated_maps - goal_state.astype(jnp.float32)
    point_mismatch = (
        jnp.sum(estimate_misfit * estimate_misfit, axis=0)
        * meridian_area_factor(rows_total, row_first, lat_rows)[:, None]
    )
    region_count = region_class.shape[0]
    region_onehot = (
        region_mask.reshape(1, -1) == jnp.arange(region_count, dtype=jnp.int32)[:, None]
    ).astype(jnp.float32)
    factor = REG_DEV / (var_count * lat_rows * lon_cols)
    partial_loss = (
        jnp.dot(region_onehot, point_mismatch.reshape(-1), precision=lax.Precision.HIGHEST) * factor
    )
    region_loss = butterfly_sum(butterfly_sum(partial_loss, "lon"), "lat")
    class_onehot = (region_class[None, :] == jnp.arange(CLASSES, dtype=jnp.int32)[:, None]).astype(
        jnp.float32
    )
    class_loss = jnp.dot(class_onehot, region_loss, precision=lax.Precision.HIGHEST)
    return (prediction, region_loss, class_loss)


def solution(mesh):
    return jax.shard_map(
        on_device,
        mesh=mesh,
        in_specs=(
            P(None, "lat", "lon"),
            P(None, "lat", "lon"),
            P("lat", "lon"),
            P(),
            P(),
            P(),
            P(),
            P(),
            P(),
            P(),
            P(),
            P(),
            P(),
            P(),
            P(),
        ),
        out_specs=(P(None, "lat", "lon"), P(), P()),
        check_vma=False,
    )
```

```python
import functools
import math

import jax
import jax.numpy as jnp
from jax import lax
from jax.experimental import pallas as pl
from jax.experimental.pallas import tpu as pltpu
from jax.sharding import PartitionSpec as P

HEADS = 16
CLASSES = 8
REG_DEV = 2


def halo_padded(array, width):
    lat_size, lon_size = lax.axis_size("lat"), lax.axis_size("lon")
    down = [(i, i + 1) for i in range(lat_size - 1)]
    up = [(i + 1, i) for i in range(lat_size - 1)]
    from_above = lax.ppermute(array[:, -width:], "lat", down)
    from_below = lax.ppermute(array[:, :width], "lat", up)
    array = jnp.concatenate([from_above, array, from_below], axis=1)
    right = [(j, (j + 1) % lon_size) for j in range(lon_size)]
    left = [((j + 1) % lon_size, j) for j in range(lon_size)]
    from_left = lax.ppermute(array[:, :, -width:], "lon", right)
    from_right = lax.ppermute(array[:, :, :width], "lon", left)
    return jnp.concatenate([from_left, array, from_right], axis=2)


def butterfly_sum(value, axis):
    size, step = lax.axis_size(axis), 1
    while step < size:
        partner = [(i, i ^ step) for i in range(size) if (i ^ step) < size]
        value = value + lax.ppermute(value, axis, partner)
        step *= 2
    return value


def convolution_kernel_taps(padded, weight):
    row_count = padded.shape[1] - 2
    col_count = padded.shape[2] - 2
    result = jnp.zeros((weight.shape[1], row_count, col_count), jnp.float32)
    for tap_index in range(9):
        shift_row = tap_index // 3
        shift_col = tap_index % 3
        window = padded[:, shift_row : shift_row + row_count, shift_col : shift_col + col_count]
        result = result + jnp.einsum(
            "oc,cyx->oyx", weight[tap_index], window, preferred_element_type=jnp.float32
        )
    return result


def meridian_area_factor(rows_total, row_first, row_count):
    row_index = jnp.arange(row_count).astype(jnp.float32) + jnp.asarray(row_first).astype(
        jnp.float32
    )
    return jnp.cos(math.pi * ((row_index + 0.5) / rows_total - 0.5))


def attention_kernel(scale_ref, q_ref, *refs, head_size, chunk_count):
    key_refs, value_refs = refs[:chunk_count], refs[chunk_count : 2 * chunk_count]
    o_ref, m_ref, l_ref = refs[2 * chunk_count :]
    queries = q_ref[...]
    column_head = lax.broadcasted_iota(jnp.int32, queries.shape, 1) // head_size
    total = jnp.zeros(queries.shape, jnp.float32)
    maxima = jnp.zeros(queries.shape, jnp.float32)
    sums = jnp.zeros(queries.shape, jnp.float32)
    for head in range(queries.shape[1] // head_size):
        in_head = column_head == head
        masked = jnp.where(in_head, queries, jnp.zeros_like(queries))
        scores = [
            lax.dot_general(
                masked, key_ref[...], (((1,), (1,)), ((), ())), preferred_element_type=jnp.float32
            )
            * scale_ref[head]
            for key_ref in key_refs
        ]
        row_max = functools.reduce(
            jnp.maximum, [jnp.max(score, axis=1, keepdims=True) for score in scores]
        )
        weighted = None
        weight_sum = None
        for score, value_ref in zip(scores, value_refs):
            weights = jnp.exp(score - row_max)
            chunk_sum = jnp.sum(weights, axis=1, keepdims=True)
            chunk_weighted = jnp.dot(
                weights.astype(jnp.bfloat16), value_ref[...], preferred_element_type=jnp.float32
            )
            weight_sum = chunk_sum if weight_sum is None else weight_sum + chunk_sum
            weighted = chunk_weighted if weighted is None else weighted + chunk_weighted
        total = jnp.where(in_head, weighted, total)
        maxima = jnp.where(in_head, row_max, maxima)
        sums = jnp.where(in_head, weight_sum, sums)
    o_ref[...] = total
    m_ref[...] = maxima
    l_ref[...] = sums


def attend_part(queries, key_chunks, value_chunks, scales, head_size):
    query_count, width = queries.shape
    key_count = sum(chunk.shape[0] for chunk in key_chunks)
    cap = 1 << (max(8, (1 << 20) // key_count).bit_length() - 1)
    block = math.gcd(query_count, cap)
    heads = width // head_size
    part = jax.ShapeDtypeStruct((query_count, width), jnp.float32)
    part_spec = pl.BlockSpec((block, width), lambda i: (i, 0))
    chunk_specs = [
        pl.BlockSpec((chunk.shape[0], width), lambda i: (0, 0))
        for chunk in list(key_chunks) + list(value_chunks)
    ]
    return pl.pallas_call(
        functools.partial(attention_kernel, head_size=head_size, chunk_count=len(key_chunks)),
        out_shape=(part, part, part),
        grid=(query_count // block,),
        in_specs=[
            pl.BlockSpec(memory_space=pltpu.SMEM),
            pl.BlockSpec((block, width), lambda i: (i, 0)),
        ]
        + chunk_specs,
        out_specs=(part_spec, part_spec, part_spec),
        compiler_params=pltpu.CompilerParams(vmem_limit_bytes=48 * 1024 * 1024),
        cost_estimate=pl.CostEstimate(
            flops=4 * query_count * key_count * width,
            transcendentals=query_count * key_count * heads,
            bytes_accessed=2 * (query_count * width + 2 * key_count * width)
            + 12 * query_count * width,
        ),
    )(scales, queries, *key_chunks, *value_chunks)


def merge_parts(parts):
    joint = functools.reduce(jnp.maximum, [maxima for total, maxima, sums in parts])
    rescales = [jnp.exp(maxima - joint) for total, maxima, sums in parts]
    total = sum(part[0] * rescale for part, rescale in zip(parts, rescales))
    weight_sum = sum(part[2] * rescale for part, rescale in zip(parts, rescales))
    return (total / weight_sum).astype(jnp.bfloat16)


def exchange_blocks(blocks, axis):
    size, index = lax.axis_size(axis), lax.axis_index(axis)
    received = [lax.dynamic_index_in_dim(blocks, index, 0, keepdims=False)]
    for shift in range(1, size):
        outgoing = lax.dynamic_index_in_dim(blocks, (index + shift) % size, 0, keepdims=False)
        received.append(
            lax.ppermute(outgoing, axis, [(i, (i + shift) % size) for i in range(size)])
        )
    return received


def return_blocks(blocks, axis):
    size, index = lax.axis_size(axis), lax.axis_index(axis)
    received = [blocks[0]] + [
        lax.ppermute(blocks[shift], axis, [((i + shift) % size, i) for i in range(size)])
        for shift in range(1, size)
    ]
    rotated = jnp.stack(received + received)
    return lax.dynamic_slice_in_dim(rotated, size - index, size, axis=0)


def on_device(
    fields,
    goal_state,
    region_mask,
    region_class,
    entry_filter_stencil,
    conv_mid,
    patch_in,
    norm_gain,
    query_weight,
    key_weight,
    value_weight,
    output_weight,
    head_scale,
    patch_out,
    final_convolution_result,
):
    var_count, lat_rows, lon_cols = fields.shape
    conv_count = entry_filter_stencil.shape[1]
    model_width = query_weight.shape[0]
    head_size = model_width // HEADS
    row_first = lax.axis_index("lat") * lat_rows
    rows_total = lat_rows * lax.axis_size("lat")
    padded = halo_padded(fields, 2)
    hidden_one = jax.nn.gelu(convolution_kernel_taps(padded, entry_filter_stencil))
    extended_row = row_first - 1 + jnp.arange(lat_rows + 2, dtype=jnp.int32)
    inside = (extended_row >= 0) & (extended_row < rows_total)
    hidden_padded = jnp.where(inside[None, :, None], hidden_one, 0.0).astype(jnp.bfloat16)
    hidden_two = jax.nn.gelu(convolution_kernel_taps(hidden_padded, conv_mid)).astype(jnp.bfloat16)
    grouped = hidden_two.reshape(conv_count, lat_rows // 4, 4, lon_cols // 4, 4)
    latent = jnp.einsum(
        "hpaqb,abhd->pqd", grouped, patch_in, preferred_element_type=jnp.float32
    ).astype(jnp.bfloat16)
    latent_flat = latent.reshape(-1, model_width)
    latent_wide = latent_flat.astype(jnp.float32)
    normed = (
        latent_wide
        * lax.rsqrt(jnp.mean(latent_wide * latent_wide, axis=1, keepdims=True) + 1e-06)
        * norm_gain
    ).astype(jnp.bfloat16)
    lon_size = lax.axis_size("lon")
    group_width = model_width // lon_size
    projections = lax.optimization_barrier(
        tuple(
            jnp.dot(normed, weight, preferred_element_type=jnp.float32).astype(jnp.bfloat16)
            for weight in (query_weight, key_weight, value_weight)
        )
    )
    by_group = [p.reshape(-1, lon_size, group_width).transpose(1, 0, 2) for p in projections]
    spread = jnp.concatenate(exchange_blocks(jnp.stack(by_group, axis=1), "lon"), axis=1)
    lat_size = lax.axis_size("lat")
    core = lax.axis_index("lat") % 2
    half = group_width // 2
    partner = [(i, i ^ 1) for i in range(lat_size)]

    def with_partner(spread):
        low, high = spread[..., :half], spread[..., half:]
        mine = jnp.where(core == 0, low, high)
        theirs = jnp.where(core == 0, high, low)
        return jnp.concatenate([mine, lax.ppermute(theirs, "lat", partner)], axis=-2)

    pair_spread = with_partner(spread)
    pair_queries, key_value = pair_spread[0], pair_spread[1:]
    remote_chunks = [
        lax.ppermute(key_value, "lat", [(i, i ^ (2 * d)) for i in range(lat_size)])
        for d in range(1, lat_size // 2)
    ]
    local_heads = half // head_size
    head_first = (lax.axis_index("lon") * 2 + core) * local_heads
    scales = lax.dynamic_slice_in_dim(head_scale, head_first, local_heads) / math.sqrt(head_size)
    key_groups = [[key_value]] + [[chunk] for chunk in remote_chunks]
    parts = [
        attend_part(
            pair_queries,
            [chunk[0] for chunk in group],
            [chunk[1] for chunk in group],
            scales,
            head_size,
        )
        for group in key_groups
        if group
    ]
    pair_attended = merge_parts(parts)
    token_count = spread.shape[1]
    own_part = pair_attended[:token_count]
    returned = lax.ppermute(pair_attended[token_count:], "lat", partner)
    attended_heads = jnp.where(
        core == 0,
        jnp.concatenate([own_part, returned], axis=1),
        jnp.concatenate([returned, own_part], axis=1),
    )
    token_block = attended_heads.shape[0] // lon_size
    attended = return_blocks(
        [attended_heads[d * token_block : (d + 1) * token_block] for d in range(lon_size)], "lon"
    )
    attended = attended.transpose(1, 0, 2).reshape(token_block, model_width)
    latent_two = (
        latent_wide + jnp.dot(attended, output_weight, preferred_element_type=jnp.float32)
    ).astype(jnp.bfloat16)
    latent_grid = latent_two.reshape(lat_rows // 4, lon_cols // 4, model_width)
    decoder_output = jax.nn.gelu(
        jnp.einsum("pqd,dabh->hpaqb", latent_grid, patch_out, preferred_element_type=jnp.float32)
    )
    decoder_output = decoder_output.reshape(conv_count, lat_rows, lon_cols).astype(jnp.bfloat16)
    decoder_output_padded = halo_padded(decoder_output, 1)
    estimated_maps = fields.astype(jnp.float32) + convolution_kernel_taps(
        decoder_output_padded, final_convolution_result
    )
    prediction = estimated_maps.astype(jnp.bfloat16)
    estimate_misfit = estimated_maps - goal_state.astype(jnp.float32)
    point_mismatch = (
        jnp.sum(estimate_misfit * estimate_misfit, axis=0)
        * meridian_area_factor(rows_total, row_first, lat_rows)[:, None]
    )
    region_count = region_class.shape[0]
    region_onehot = (
        region_mask.reshape(1, -1) == jnp.arange(region_count, dtype=jnp.int32)[:, None]
    ).astype(jnp.float32)
    factor = REG_DEV / (var_count * lat_rows * lon_cols)
    partial_loss = (
        jnp.dot(region_onehot, point_mismatch.reshape(-1), precision=lax.Precision.HIGHEST) * factor
    )
    region_loss = butterfly_sum(butterfly_sum(partial_loss, "lon"), "lat")
    class_onehot = (region_class[None, :] == jnp.arange(CLASSES, dtype=jnp.int32)[:, None]).astype(
        jnp.float32
    )
    class_loss = jnp.dot(class_onehot, region_loss, precision=lax.Precision.HIGHEST)
    return (prediction, region_loss, class_loss)


def solution(mesh):
    return jax.shard_map(
        on_device,
        mesh=mesh,
        in_specs=(
            P(None, "lat", "lon"),
            P(None, "lat", "lon"),
            P("lat", "lon"),
            P(),
            P(),
            P(),
            P(),
            P(),
            P(),
            P(),
            P(),
            P(),
            P(),
            P(),
            P(),
        ),
        out_specs=(P(None, "lat", "lon"), P(), P()),
        check_vma=False,
    )
```

```python
import functools
import math

import jax
import jax.numpy as jnp
from jax import lax
from jax.experimental import pallas as pl
from jax.experimental.pallas import tpu as pltpu
from jax.sharding import PartitionSpec as P

HEADS = 16
CLASSES = 8
REG_DEV = 2


def halo_padded(array, width):
    lat_size, lon_size = lax.axis_size("lat"), lax.axis_size("lon")
    down = [(i, i + 1) for i in range(lat_size - 1)]
    up = [(i + 1, i) for i in range(lat_size - 1)]
    from_above = lax.ppermute(array[:, -width:], "lat", down)
    from_below = lax.ppermute(array[:, :width], "lat", up)
    array = jnp.concatenate([from_above, array, from_below], axis=1)
    right = [(j, (j + 1) % lon_size) for j in range(lon_size)]
    left = [((j + 1) % lon_size, j) for j in range(lon_size)]
    from_left = lax.ppermute(array[:, :, -width:], "lon", right)
    from_right = lax.ppermute(array[:, :, :width], "lon", left)
    return jnp.concatenate([from_left, array, from_right], axis=2)


def butterfly_sum(value, axis):
    size, step = lax.axis_size(axis), 1
    while step < size:
        partner = [(i, i ^ step) for i in range(size) if (i ^ step) < size]
        value = value + lax.ppermute(value, axis, partner)
        step *= 2
    return value


def convolution_kernel_taps(padded, weight):
    row_count = padded.shape[1] - 2
    col_count = padded.shape[2] - 2
    result = jnp.zeros((weight.shape[1], row_count, col_count), jnp.float32)
    for tap_index in range(9):
        shift_row = tap_index // 3
        shift_col = tap_index % 3
        window = padded[:, shift_row : shift_row + row_count, shift_col : shift_col + col_count]
        result = result + jnp.einsum(
            "oc,cyx->oyx", weight[tap_index], window, preferred_element_type=jnp.float32
        )
    return result


def meridian_area_factor(rows_total, row_first, row_count):
    row_index = jnp.arange(row_count).astype(jnp.float32) + jnp.asarray(row_first).astype(
        jnp.float32
    )
    return jnp.cos(math.pi * ((row_index + 0.5) / rows_total - 0.5))


def attention_kernel(scale_ref, q_ref, *refs, head_size, chunk_count):
    key_refs, value_refs = refs[:chunk_count], refs[chunk_count : 2 * chunk_count]
    o_ref, m_ref, l_ref = refs[2 * chunk_count :]
    queries = q_ref[...]
    column_head = lax.broadcasted_iota(jnp.int32, queries.shape, 1) // head_size
    total = jnp.zeros(queries.shape, jnp.float32)
    maxima = jnp.zeros(queries.shape, jnp.float32)
    sums = jnp.zeros(queries.shape, jnp.float32)
    for head in range(queries.shape[1] // head_size):
        in_head = column_head == head
        masked = jnp.where(in_head, queries, jnp.zeros_like(queries))
        scores = [
            lax.dot_general(
                masked, key_ref[...], (((1,), (1,)), ((), ())), preferred_element_type=jnp.float32
            )
            * scale_ref[head]
            for key_ref in key_refs
        ]
        row_max = functools.reduce(
            jnp.maximum, [jnp.max(score, axis=1, keepdims=True) for score in scores]
        )
        weighted = None
        weight_sum = None
        for score, value_ref in zip(scores, value_refs):
            weights = jnp.exp(score - row_max)
            chunk_sum = jnp.sum(weights, axis=1, keepdims=True)
            chunk_weighted = jnp.dot(
                weights.astype(jnp.bfloat16), value_ref[...], preferred_element_type=jnp.float32
            )
            weight_sum = chunk_sum if weight_sum is None else weight_sum + chunk_sum
            weighted = chunk_weighted if weighted is None else weighted + chunk_weighted
        total = jnp.where(in_head, weighted, total)
        maxima = jnp.where(in_head, row_max, maxima)
        sums = jnp.where(in_head, weight_sum, sums)
    o_ref[...] = total
    m_ref[...] = maxima
    l_ref[...] = sums


def attend_part(queries, key_chunks, value_chunks, scales, head_size):
    query_count, width = queries.shape
    key_count = sum(chunk.shape[0] for chunk in key_chunks)
    cap = 1 << (max(8, (1 << 18) // key_count).bit_length() - 1)
    block = math.gcd(query_count, cap)
    heads = width // head_size
    part = jax.ShapeDtypeStruct((query_count, width), jnp.float32)
    part_spec = pl.BlockSpec((block, width), lambda i: (i, 0))
    chunk_specs = [
        pl.BlockSpec((chunk.shape[0], width), lambda i: (0, 0))
        for chunk in list(key_chunks) + list(value_chunks)
    ]
    return pl.pallas_call(
        functools.partial(attention_kernel, head_size=head_size, chunk_count=len(key_chunks)),
        out_shape=(part, part, part),
        grid=(query_count // block,),
        in_specs=[
            pl.BlockSpec(memory_space=pltpu.SMEM),
            pl.BlockSpec((block, width), lambda i: (i, 0)),
        ]
        + chunk_specs,
        out_specs=(part_spec, part_spec, part_spec),
        compiler_params=pltpu.CompilerParams(vmem_limit_bytes=48 * 1024 * 1024),
        cost_estimate=pl.CostEstimate(
            flops=4 * query_count * key_count * width,
            transcendentals=query_count * key_count * heads,
            bytes_accessed=2 * (query_count * width + 2 * key_count * width)
            + 12 * query_count * width,
        ),
    )(scales, queries, *key_chunks, *value_chunks)


def merge_parts(parts):
    joint = functools.reduce(jnp.maximum, [maxima for total, maxima, sums in parts])
    rescales = [jnp.exp(maxima - joint) for total, maxima, sums in parts]
    total = sum(part[0] * rescale for part, rescale in zip(parts, rescales))
    weight_sum = sum(part[2] * rescale for part, rescale in zip(parts, rescales))
    return (total / weight_sum).astype(jnp.bfloat16)


def exchange_blocks(blocks, axis):
    size, index = lax.axis_size(axis), lax.axis_index(axis)
    received = [lax.dynamic_index_in_dim(blocks, index, 0, keepdims=False)]
    for shift in range(1, size):
        outgoing = lax.dynamic_index_in_dim(blocks, (index + shift) % size, 0, keepdims=False)
        received.append(
            lax.ppermute(outgoing, axis, [(i, (i + shift) % size) for i in range(size)])
        )
    return received


def return_blocks(blocks, axis):
    size, index = lax.axis_size(axis), lax.axis_index(axis)
    received = [blocks[0]] + [
        lax.ppermute(blocks[shift], axis, [((i + shift) % size, i) for i in range(size)])
        for shift in range(1, size)
    ]
    rotated = jnp.stack(received + received)
    return lax.dynamic_slice_in_dim(rotated, size - index, size, axis=0)


def on_device(
    fields,
    goal_state,
    region_mask,
    region_class,
    entry_filter_stencil,
    conv_mid,
    patch_in,
    norm_gain,
    query_weight,
    key_weight,
    value_weight,
    output_weight,
    head_scale,
    patch_out,
    final_convolution_result,
):
    var_count, lat_rows, lon_cols = fields.shape
    conv_count = entry_filter_stencil.shape[1]
    model_width = query_weight.shape[0]
    head_size = model_width // HEADS
    row_first = lax.axis_index("lat") * lat_rows
    rows_total = lat_rows * lax.axis_size("lat")
    padded = halo_padded(fields, 2)
    hidden_one = jax.nn.gelu(convolution_kernel_taps(padded, entry_filter_stencil))
    extended_row = row_first - 1 + jnp.arange(lat_rows + 2, dtype=jnp.int32)
    inside = (extended_row >= 0) & (extended_row < rows_total)
    hidden_padded = jnp.where(inside[None, :, None], hidden_one, 0.0).astype(jnp.bfloat16)
    hidden_two = jax.nn.gelu(convolution_kernel_taps(hidden_padded, conv_mid)).astype(jnp.bfloat16)
    grouped = hidden_two.reshape(conv_count, lat_rows // 4, 4, lon_cols // 4, 4)
    latent = jnp.einsum(
        "hpaqb,abhd->pqd", grouped, patch_in, preferred_element_type=jnp.float32
    ).astype(jnp.bfloat16)
    latent_flat = latent.reshape(-1, model_width)
    latent_wide = latent_flat.astype(jnp.float32)
    normed = (
        latent_wide
        * lax.rsqrt(jnp.mean(latent_wide * latent_wide, axis=1, keepdims=True) + 1e-06)
        * norm_gain
    ).astype(jnp.bfloat16)
    lon_size = lax.axis_size("lon")
    group_width = model_width // lon_size
    projections = lax.optimization_barrier(
        tuple(
            jnp.dot(normed, weight, preferred_element_type=jnp.float32).astype(jnp.bfloat16)
            for weight in (query_weight, key_weight, value_weight)
        )
    )
    by_group = [p.reshape(-1, lon_size, group_width).transpose(1, 0, 2) for p in projections]
    spread = jnp.concatenate(exchange_blocks(jnp.stack(by_group, axis=1), "lon"), axis=1)
    lat_size = lax.axis_size("lat")
    core = lax.axis_index("lat") % 2
    half = group_width // 2
    partner = [(i, i ^ 1) for i in range(lat_size)]

    def with_partner(spread):
        low, high = spread[..., :half], spread[..., half:]
        mine = jnp.where(core == 0, low, high)
        theirs = jnp.where(core == 0, high, low)
        return jnp.concatenate([mine, lax.ppermute(theirs, "lat", partner)], axis=-2)

    pair_spread = with_partner(spread)
    pair_queries, key_value = pair_spread[0], pair_spread[1:]
    remote_chunks = [
        lax.ppermute(key_value, "lat", [(i, i ^ (2 * d)) for i in range(lat_size)])
        for d in range(1, lat_size // 2)
    ]
    local_heads = half // head_size
    head_first = (lax.axis_index("lon") * 2 + core) * local_heads
    scales = lax.dynamic_slice_in_dim(head_scale, head_first, local_heads) / math.sqrt(head_size)
    key_groups = [[key_value]] + [[chunk] for chunk in remote_chunks]
    parts = [
        attend_part(
            pair_queries,
            [chunk[0] for chunk in group],
            [chunk[1] for chunk in group],
            scales,
            head_size,
        )
        for group in key_groups
        if group
    ]
    pair_attended = merge_parts(parts)
    token_count = spread.shape[1]
    own_part = pair_attended[:token_count]
    returned = lax.ppermute(pair_attended[token_count:], "lat", partner)
    attended_heads = jnp.where(
        core == 0,
        jnp.concatenate([own_part, returned], axis=1),
        jnp.concatenate([returned, own_part], axis=1),
    )
    token_block = attended_heads.shape[0] // lon_size
    attended = return_blocks(
        [attended_heads[d * token_block : (d + 1) * token_block] for d in range(lon_size)], "lon"
    )
    attended = attended.transpose(1, 0, 2).reshape(token_block, model_width)
    latent_two = (
        latent_wide + jnp.dot(attended, output_weight, preferred_element_type=jnp.float32)
    ).astype(jnp.bfloat16)
    latent_grid = latent_two.reshape(lat_rows // 4, lon_cols // 4, model_width)
    decoder_output = jax.nn.gelu(
        jnp.einsum("pqd,dabh->hpaqb", latent_grid, patch_out, preferred_element_type=jnp.float32)
    )
    decoder_output = decoder_output.reshape(conv_count, lat_rows, lon_cols).astype(jnp.bfloat16)
    decoder_output_padded = halo_padded(decoder_output, 1)
    estimated_maps = fields.astype(jnp.float32) + convolution_kernel_taps(
        decoder_output_padded, final_convolution_result
    )
    prediction = estimated_maps.astype(jnp.bfloat16)
    estimate_misfit = estimated_maps - goal_state.astype(jnp.float32)
    point_mismatch = (
        jnp.sum(estimate_misfit * estimate_misfit, axis=0)
        * meridian_area_factor(rows_total, row_first, lat_rows)[:, None]
    )
    region_count = region_class.shape[0]
    region_onehot = (
        region_mask.reshape(1, -1) == jnp.arange(region_count, dtype=jnp.int32)[:, None]
    ).astype(jnp.float32)
    factor = REG_DEV / (var_count * lat_rows * lon_cols)
    partial_loss = (
        jnp.dot(region_onehot, point_mismatch.reshape(-1), precision=lax.Precision.HIGHEST) * factor
    )
    region_loss = butterfly_sum(butterfly_sum(partial_loss, "lon"), "lat")
    class_onehot = (region_class[None, :] == jnp.arange(CLASSES, dtype=jnp.int32)[:, None]).astype(
        jnp.float32
    )
    class_loss = jnp.dot(class_onehot, region_loss, precision=lax.Precision.HIGHEST)
    return (prediction, region_loss, class_loss)


def solution(mesh):
    return jax.shard_map(
        on_device,
        mesh=mesh,
        in_specs=(
            P(None, "lat", "lon"),
            P(None, "lat", "lon"),
            P("lat", "lon"),
            P(),
            P(),
            P(),
            P(),
            P(),
            P(),
            P(),
            P(),
            P(),
            P(),
            P(),
            P(),
        ),
        out_specs=(P(None, "lat", "lon"), P(), P()),
        check_vma=False,
    )
```

```python
import functools
import math

import jax
import jax.numpy as jnp
from jax import lax
from jax.experimental import pallas as pl
from jax.experimental.pallas import tpu as pltpu
from jax.sharding import PartitionSpec as P

HEADS = 16
CLASSES = 8
REG_DEV = 2


def halo_padded(array, width):
    lat_size, lon_size = lax.axis_size("lat"), lax.axis_size("lon")
    down = [(i, i + 1) for i in range(lat_size - 1)]
    up = [(i + 1, i) for i in range(lat_size - 1)]
    from_above = lax.ppermute(array[:, -width:], "lat", down)
    from_below = lax.ppermute(array[:, :width], "lat", up)
    array = jnp.concatenate([from_above, array, from_below], axis=1)
    right = [(j, (j + 1) % lon_size) for j in range(lon_size)]
    left = [((j + 1) % lon_size, j) for j in range(lon_size)]
    from_left = lax.ppermute(array[:, :, -width:], "lon", right)
    from_right = lax.ppermute(array[:, :, :width], "lon", left)
    return jnp.concatenate([from_left, array, from_right], axis=2)


def butterfly_sum(value, axis):
    size, step = lax.axis_size(axis), 1
    while step < size:
        partner = [(i, i ^ step) for i in range(size) if (i ^ step) < size]
        value = value + lax.ppermute(value, axis, partner)
        step *= 2
    return value


def convolution_kernel_taps(padded, weight):
    row_count = padded.shape[1] - 2
    col_count = padded.shape[2] - 2
    result = jnp.zeros((weight.shape[1], row_count, col_count), jnp.float32)
    for tap_index in range(9):
        shift_row = tap_index // 3
        shift_col = tap_index % 3
        window = padded[:, shift_row : shift_row + row_count, shift_col : shift_col + col_count]
        result = result + jnp.einsum(
            "oc,cyx->oyx", weight[tap_index], window, preferred_element_type=jnp.float32
        )
    return result


def meridian_area_factor(rows_total, row_first, row_count):
    row_index = jnp.arange(row_count).astype(jnp.float32) + jnp.asarray(row_first).astype(
        jnp.float32
    )
    return jnp.cos(math.pi * ((row_index + 0.5) / rows_total - 0.5))


def attention_kernel(scale_ref, q_ref, *refs, head_size, chunk_count):
    key_refs, value_refs = refs[:chunk_count], refs[chunk_count : 2 * chunk_count]
    o_ref, m_ref, l_ref = refs[2 * chunk_count :]
    queries = q_ref[...]
    column_head = lax.broadcasted_iota(jnp.int32, queries.shape, 1) // head_size
    total = jnp.zeros(queries.shape, jnp.float32)
    maxima = jnp.zeros(queries.shape, jnp.float32)
    sums = jnp.zeros(queries.shape, jnp.float32)
    for head in range(queries.shape[1] // head_size):
        in_head = column_head == head
        masked = jnp.where(in_head, queries, jnp.zeros_like(queries))
        scores = [
            lax.dot_general(
                masked, key_ref[...], (((1,), (1,)), ((), ())), preferred_element_type=jnp.float32
            )
            * scale_ref[head]
            for key_ref in key_refs
        ]
        row_max = functools.reduce(
            jnp.maximum, [jnp.max(score, axis=1, keepdims=True) for score in scores]
        )
        weighted = None
        weight_sum = None
        for score, value_ref in zip(scores, value_refs):
            weights = jnp.exp(score - row_max)
            chunk_sum = jnp.sum(weights, axis=1, keepdims=True)
            chunk_weighted = jnp.dot(
                weights.astype(jnp.bfloat16), value_ref[...], preferred_element_type=jnp.float32
            )
            weight_sum = chunk_sum if weight_sum is None else weight_sum + chunk_sum
            weighted = chunk_weighted if weighted is None else weighted + chunk_weighted
        total = jnp.where(in_head, weighted, total)
        maxima = jnp.where(in_head, row_max, maxima)
        sums = jnp.where(in_head, weight_sum, sums)
    o_ref[...] = total
    m_ref[...] = maxima
    l_ref[...] = sums


def attend_part(queries, key_chunks, value_chunks, scales, head_size):
    query_count, width = queries.shape
    key_count = sum(chunk.shape[0] for chunk in key_chunks)
    cap = 1 << (max(8, (1 << 20) // key_count).bit_length() - 1)
    block = math.gcd(query_count, cap)
    heads = width // head_size
    part = jax.ShapeDtypeStruct((query_count, width), jnp.float32)
    part_spec = pl.BlockSpec((block, width), lambda i: (i, 0))
    chunk_specs = [
        pl.BlockSpec((chunk.shape[0], width), lambda i: (0, 0))
        for chunk in list(key_chunks) + list(value_chunks)
    ]
    return pl.pallas_call(
        functools.partial(attention_kernel, head_size=head_size, chunk_count=len(key_chunks)),
        out_shape=(part, part, part),
        grid=(query_count // block,),
        in_specs=[
            pl.BlockSpec(memory_space=pltpu.SMEM),
            pl.BlockSpec((block, width), lambda i: (i, 0)),
        ]
        + chunk_specs,
        out_specs=(part_spec, part_spec, part_spec),
        compiler_params=pltpu.CompilerParams(vmem_limit_bytes=48 * 1024 * 1024),
        cost_estimate=pl.CostEstimate(
            flops=4 * query_count * key_count * width,
            transcendentals=query_count * key_count * heads,
            bytes_accessed=2 * (query_count * width + 2 * key_count * width)
            + 12 * query_count * width,
        ),
    )(scales, queries, *key_chunks, *value_chunks)


def merge_parts(parts):
    joint = functools.reduce(jnp.maximum, [maxima for total, maxima, sums in parts])
    rescales = [jnp.exp(maxima - joint) for total, maxima, sums in parts]
    total = sum(part[0] * rescale for part, rescale in zip(parts, rescales))
    weight_sum = sum(part[2] * rescale for part, rescale in zip(parts, rescales))
    return (total / weight_sum).astype(jnp.bfloat16)


def exchange_blocks(blocks, axis):
    size, index = lax.axis_size(axis), lax.axis_index(axis)
    received = [lax.dynamic_index_in_dim(blocks, index, 0, keepdims=False)]
    for shift in range(1, size):
        outgoing = lax.dynamic_index_in_dim(blocks, (index + shift) % size, 0, keepdims=False)
        received.append(
            lax.ppermute(outgoing, axis, [(i, (i + shift) % size) for i in range(size)])
        )
    return received


def return_blocks(blocks, axis):
    size, index = lax.axis_size(axis), lax.axis_index(axis)
    received = [blocks[0]] + [
        lax.ppermute(blocks[shift], axis, [((i + shift) % size, i) for i in range(size)])
        for shift in range(1, size)
    ]
    rotated = jnp.stack(received + received)
    return lax.dynamic_slice_in_dim(rotated, size - index, size, axis=0)


def on_device(
    fields,
    goal_state,
    region_mask,
    region_class,
    entry_filter_stencil,
    conv_mid,
    patch_in,
    norm_gain,
    query_weight,
    key_weight,
    value_weight,
    output_weight,
    head_scale,
    patch_out,
    final_convolution_result,
):
    var_count, lat_rows, lon_cols = fields.shape
    conv_count = entry_filter_stencil.shape[1]
    model_width = query_weight.shape[0]
    head_size = model_width // HEADS
    row_first = lax.axis_index("lat") * lat_rows
    rows_total = lat_rows * lax.axis_size("lat")
    padded = halo_padded(fields, 2)
    hidden_one = jax.nn.gelu(convolution_kernel_taps(padded, entry_filter_stencil))
    extended_row = row_first - 1 + jnp.arange(lat_rows + 2, dtype=jnp.int32)
    inside = (extended_row >= 0) & (extended_row < rows_total)
    hidden_padded = jnp.where(inside[None, :, None], hidden_one, 0.0).astype(jnp.bfloat16)
    hidden_two = jax.nn.gelu(convolution_kernel_taps(hidden_padded, conv_mid)).astype(jnp.bfloat16)
    grouped = hidden_two.reshape(conv_count, lat_rows // 4, 4, lon_cols // 4, 4)
    latent = jnp.einsum(
        "hpaqb,abhd->pqd", grouped, patch_in, preferred_element_type=jnp.float32
    ).astype(jnp.bfloat16)
    latent_flat = latent.reshape(-1, model_width)
    latent_wide = latent_flat.astype(jnp.float32)
    normed = (
        latent_wide
        * lax.rsqrt(jnp.mean(latent_wide * latent_wide, axis=1, keepdims=True) + 1e-06)
        * norm_gain
    ).astype(jnp.bfloat16)
    lon_size = lax.axis_size("lon")
    group_width = model_width // lon_size
    projections = lax.optimization_barrier(
        tuple(
            jnp.dot(normed, weight, preferred_element_type=jnp.float32).astype(jnp.bfloat16)
            for weight in (query_weight, key_weight, value_weight)
        )
    )
    by_group = [p.reshape(-1, lon_size, group_width).transpose(1, 0, 2) for p in projections]
    spread = jnp.concatenate(exchange_blocks(jnp.stack(by_group, axis=1), "lon"), axis=1)
    lat_size = lax.axis_size("lat")
    core = lax.axis_index("lat") % 2
    half = group_width // 2
    partner = [(i, i ^ 1) for i in range(lat_size)]

    def with_partner(spread):
        low, high = spread[..., :half], spread[..., half:]
        mine = jnp.where(core == 0, low, high)
        theirs = jnp.where(core == 0, high, low)
        return jnp.concatenate([mine, lax.ppermute(theirs, "lat", partner)], axis=-2)

    pair_spread = with_partner(spread)
    pair_queries, key_value = pair_spread[0], pair_spread[1:]
    remote_chunks = [
        lax.ppermute(key_value, "lat", [(i, i ^ (2 * d)) for i in range(lat_size)])
        for d in range(1, lat_size // 2)
    ]
    local_heads = half // head_size
    head_first = (lax.axis_index("lon") * 2 + core) * local_heads
    scales = lax.dynamic_slice_in_dim(head_scale, head_first, local_heads) / math.sqrt(head_size)
    key_groups = [[key_value]] + [[chunk] for chunk in remote_chunks]
    parts = [
        attend_part(
            pair_queries,
            [chunk[0] for chunk in group],
            [chunk[1] for chunk in group],
            scales,
            head_size,
        )
        for group in key_groups
        if group
    ]
    pair_attended = merge_parts(parts)
    token_count = spread.shape[1]
    own_part = pair_attended[:token_count]
    returned = lax.ppermute(pair_attended[token_count:], "lat", partner)
    attended_heads = jnp.where(
        core == 0,
        jnp.concatenate([own_part, returned], axis=1),
        jnp.concatenate([returned, own_part], axis=1),
    )
    token_block = attended_heads.shape[0] // lon_size
    attended = return_blocks(
        [attended_heads[d * token_block : (d + 1) * token_block] for d in range(lon_size)], "lon"
    )
    attended = attended.transpose(1, 0, 2).reshape(token_block, model_width)
    latent_two = (
        latent_wide + jnp.dot(attended, output_weight, preferred_element_type=jnp.float32)
    ).astype(jnp.bfloat16)
    latent_grid = latent_two.reshape(lat_rows // 4, lon_cols // 4, model_width)

    def decode(token_grid):
        decoded = jax.nn.gelu(
            jnp.einsum(
                "pqd,dabh->hpaqb", token_grid, patch_out, preferred_element_type=jnp.float32
            )
        )
        return decoded.reshape(conv_count, lat_rows, -1).astype(jnp.bfloat16)

    lon_size = lax.axis_size("lon")
    first_column = decode(latent_grid[:, :1])[:, :, :1]
    last_column = decode(latent_grid[:, -1:])[:, :, -1:]
    from_left = lax.ppermute(last_column, "lon", [(j, (j + 1) % lon_size) for j in range(lon_size)])
    from_right = lax.ppermute(first_column, "lon", [((j + 1) % lon_size, j) for j in range(lon_size)])
    decoder_output = jnp.concatenate([from_left, decode(latent_grid), from_right], axis=2)
    down = [(i, i + 1) for i in range(lat_size - 1)]
    up = [(i + 1, i) for i in range(lat_size - 1)]
    decoder_output_padded = jnp.concatenate(
        [
            lax.ppermute(decoder_output[:, -1:], "lat", down),
            decoder_output,
            lax.ppermute(decoder_output[:, :1], "lat", up),
        ],
        axis=1,
    )
    estimated_maps = fields.astype(jnp.float32) + convolution_kernel_taps(
        decoder_output_padded, final_convolution_result
    )
    prediction = estimated_maps.astype(jnp.bfloat16)
    estimate_misfit = estimated_maps - goal_state.astype(jnp.float32)
    point_mismatch = (
        jnp.sum(estimate_misfit * estimate_misfit, axis=0)
        * meridian_area_factor(rows_total, row_first, lat_rows)[:, None]
    )
    region_count = region_class.shape[0]
    region_onehot = (
        region_mask.reshape(1, -1) == jnp.arange(region_count, dtype=jnp.int32)[:, None]
    ).astype(jnp.float32)
    factor = REG_DEV / (var_count * lat_rows * lon_cols)
    partial_loss = (
        jnp.dot(region_onehot, point_mismatch.reshape(-1), precision=lax.Precision.HIGHEST) * factor
    )
    region_loss = butterfly_sum(butterfly_sum(partial_loss, "lon"), "lat")
    class_onehot = (region_class[None, :] == jnp.arange(CLASSES, dtype=jnp.int32)[:, None]).astype(
        jnp.float32
    )
    class_loss = jnp.dot(class_onehot, region_loss, precision=lax.Precision.HIGHEST)
    return (prediction, region_loss, class_loss)


def solution(mesh):
    return jax.shard_map(
        on_device,
        mesh=mesh,
        in_specs=(
            P(None, "lat", "lon"),
            P(None, "lat", "lon"),
            P("lat", "lon"),
            P(),
            P(),
            P(),
            P(),
            P(),
            P(),
            P(),
            P(),
            P(),
            P(),
            P(),
            P(),
        ),
        out_specs=(P(None, "lat", "lon"), P(), P()),
        check_vma=False,
    )
```

```python
import functools
import math

import jax
import jax.numpy as jnp
from jax import lax
from jax.experimental import pallas as pl
from jax.experimental.pallas import tpu as pltpu
from jax.sharding import PartitionSpec as P

HEADS = 16
CLASSES = 8
REG_DEV = 2


def halo_padded(array, width):
    lat_size, lon_size = lax.axis_size("lat"), lax.axis_size("lon")
    down = [(i, i + 1) for i in range(lat_size - 1)]
    up = [(i + 1, i) for i in range(lat_size - 1)]
    from_above = lax.ppermute(array[:, -width:], "lat", down)
    from_below = lax.ppermute(array[:, :width], "lat", up)
    array = jnp.concatenate([from_above, array, from_below], axis=1)
    right = [(j, (j + 1) % lon_size) for j in range(lon_size)]
    left = [((j + 1) % lon_size, j) for j in range(lon_size)]
    from_left = lax.ppermute(array[:, :, -width:], "lon", right)
    from_right = lax.ppermute(array[:, :, :width], "lon", left)
    return jnp.concatenate([from_left, array, from_right], axis=2)


def butterfly_sum(value, axis):
    size, step = lax.axis_size(axis), 1
    while step < size:
        partner = [(i, i ^ step) for i in range(size) if (i ^ step) < size]
        value = value + lax.ppermute(value, axis, partner)
        step *= 2
    return value


def convolution_kernel_taps(padded, weight):
    row_count = padded.shape[1] - 2
    col_count = padded.shape[2] - 2
    result = jnp.zeros((weight.shape[1], row_count, col_count), jnp.float32)
    for tap_index in range(9):
        shift_row = tap_index // 3
        shift_col = tap_index % 3
        window = padded[:, shift_row : shift_row + row_count, shift_col : shift_col + col_count]
        result = result + jnp.einsum(
            "oc,cyx->oyx", weight[tap_index], window, preferred_element_type=jnp.float32
        )
    return result


def meridian_area_factor(rows_total, row_first, row_count):
    row_index = jnp.arange(row_count).astype(jnp.float32) + jnp.asarray(row_first).astype(
        jnp.float32
    )
    return jnp.cos(math.pi * ((row_index + 0.5) / rows_total - 0.5))


def attention_kernel(scale_ref, q_ref, *refs, head_size, chunk_count):
    key_refs, value_refs = refs[:chunk_count], refs[chunk_count : 2 * chunk_count]
    o_ref, m_ref, l_ref = refs[2 * chunk_count :]
    queries = q_ref[...]
    column_head = lax.broadcasted_iota(jnp.int32, queries.shape, 1) // head_size
    total = jnp.zeros(queries.shape, jnp.float32)
    maxima = jnp.zeros(queries.shape, jnp.float32)
    sums = jnp.zeros(queries.shape, jnp.float32)
    for head in range(queries.shape[1] // head_size):
        in_head = column_head == head
        masked = jnp.where(in_head, queries, jnp.zeros_like(queries))
        scores = [
            lax.dot_general(
                masked, key_ref[...], (((1,), (1,)), ((), ())), preferred_element_type=jnp.float32
            )
            * scale_ref[head]
            for key_ref in key_refs
        ]
        row_max = functools.reduce(
            jnp.maximum, [jnp.max(score, axis=1, keepdims=True) for score in scores]
        )
        weighted = None
        weight_sum = None
        for score, value_ref in zip(scores, value_refs):
            weights = jnp.exp(score - row_max)
            chunk_sum = jnp.sum(weights, axis=1, keepdims=True)
            chunk_weighted = jnp.dot(
                weights.astype(jnp.bfloat16), value_ref[...], preferred_element_type=jnp.float32
            )
            weight_sum = chunk_sum if weight_sum is None else weight_sum + chunk_sum
            weighted = chunk_weighted if weighted is None else weighted + chunk_weighted
        total = jnp.where(in_head, weighted, total)
        maxima = jnp.where(in_head, row_max, maxima)
        sums = jnp.where(in_head, weight_sum, sums)
    o_ref[...] = total
    m_ref[...] = maxima
    l_ref[...] = sums


def attend_part(queries, key_chunks, value_chunks, scales, head_size):
    query_count, width = queries.shape
    key_count = sum(chunk.shape[0] for chunk in key_chunks)
    cap = 1 << (max(8, (1 << 20) // key_count).bit_length() - 1)
    block = math.gcd(query_count, cap)
    heads = width // head_size
    part = jax.ShapeDtypeStruct((query_count, width), jnp.float32)
    part_spec = pl.BlockSpec((block, width), lambda i: (i, 0))
    chunk_specs = [
        pl.BlockSpec((chunk.shape[0], width), lambda i: (0, 0))
        for chunk in list(key_chunks) + list(value_chunks)
    ]
    return pl.pallas_call(
        functools.partial(attention_kernel, head_size=head_size, chunk_count=len(key_chunks)),
        out_shape=(part, part, part),
        grid=(query_count // block,),
        in_specs=[
            pl.BlockSpec(memory_space=pltpu.SMEM),
            pl.BlockSpec((block, width), lambda i: (i, 0)),
        ]
        + chunk_specs,
        out_specs=(part_spec, part_spec, part_spec),
        compiler_params=pltpu.CompilerParams(vmem_limit_bytes=48 * 1024 * 1024),
        cost_estimate=pl.CostEstimate(
            flops=4 * query_count * key_count * width,
            transcendentals=query_count * key_count * heads,
            bytes_accessed=2 * (query_count * width + 2 * key_count * width)
            + 12 * query_count * width,
        ),
    )(scales, queries, *key_chunks, *value_chunks)


def merge_parts(parts):
    joint = functools.reduce(jnp.maximum, [maxima for total, maxima, sums in parts])
    rescales = [jnp.exp(maxima - joint) for total, maxima, sums in parts]
    total = sum(part[0] * rescale for part, rescale in zip(parts, rescales))
    weight_sum = sum(part[2] * rescale for part, rescale in zip(parts, rescales))
    return (total / weight_sum).astype(jnp.bfloat16)


def exchange_blocks(blocks, axis):
    size, index = lax.axis_size(axis), lax.axis_index(axis)
    received = [lax.dynamic_index_in_dim(blocks, index, 0, keepdims=False)]
    for shift in range(1, size):
        outgoing = lax.dynamic_index_in_dim(blocks, (index + shift) % size, 0, keepdims=False)
        received.append(
            lax.ppermute(outgoing, axis, [(i, (i + shift) % size) for i in range(size)])
        )
    return received


def return_blocks(blocks, axis):
    size, index = lax.axis_size(axis), lax.axis_index(axis)
    received = [blocks[0]] + [
        lax.ppermute(blocks[shift], axis, [((i + shift) % size, i) for i in range(size)])
        for shift in range(1, size)
    ]
    rotated = jnp.stack(received + received)
    return lax.dynamic_slice_in_dim(rotated, size - index, size, axis=0)


def on_device(
    fields,
    goal_state,
    region_mask,
    region_class,
    entry_filter_stencil,
    conv_mid,
    patch_in,
    norm_gain,
    query_weight,
    key_weight,
    value_weight,
    output_weight,
    head_scale,
    patch_out,
    final_convolution_result,
):
    var_count, lat_rows, lon_cols = fields.shape
    conv_count = entry_filter_stencil.shape[1]
    model_width = query_weight.shape[0]
    head_size = model_width // HEADS
    row_first = lax.axis_index("lat") * lat_rows
    rows_total = lat_rows * lax.axis_size("lat")
    padded = halo_padded(fields, 2)
    hidden_one = jax.nn.gelu(convolution_kernel_taps(padded, entry_filter_stencil))
    extended_row = row_first - 1 + jnp.arange(lat_rows + 2, dtype=jnp.int32)
    inside = (extended_row >= 0) & (extended_row < rows_total)
    hidden_padded = jnp.where(inside[None, :, None], hidden_one, 0.0).astype(jnp.bfloat16)
    hidden_two = jax.nn.gelu(convolution_kernel_taps(hidden_padded, conv_mid)).astype(jnp.bfloat16)
    grouped = hidden_two.reshape(conv_count, lat_rows // 4, 4, lon_cols // 4, 4)
    latent = jnp.einsum(
        "hpaqb,abhd->pqd", grouped, patch_in, preferred_element_type=jnp.float32
    ).astype(jnp.bfloat16)
    latent_flat = latent.reshape(-1, model_width)
    latent_wide = latent_flat.astype(jnp.float32)
    normed = (
        latent_wide
        * lax.rsqrt(jnp.mean(latent_wide * latent_wide, axis=1, keepdims=True) + 1e-06)
        * norm_gain
    ).astype(jnp.bfloat16)
    lon_size = lax.axis_size("lon")
    group_width = model_width // lon_size
    projections = lax.optimization_barrier(
        tuple(
            jnp.dot(normed, weight, preferred_element_type=jnp.float32).astype(jnp.bfloat16)
            for weight in (query_weight, key_weight, value_weight)
        )
    )
    by_group = [p.reshape(-1, lon_size, group_width).transpose(1, 0, 2) for p in projections]
    spread = jnp.concatenate(exchange_blocks(jnp.stack(by_group, axis=1), "lon"), axis=1)
    lat_size = lax.axis_size("lat")
    core = lax.axis_index("lat") % 2
    half = group_width // 2
    partner = [(i, i ^ 1) for i in range(lat_size)]

    def with_partner(spread):
        low, high = spread[..., :half], spread[..., half:]
        mine = jnp.where(core == 0, low, high)
        theirs = jnp.where(core == 0, high, low)
        return jnp.concatenate([mine, lax.ppermute(theirs, "lat", partner)], axis=-2)

    pair_spread = with_partner(spread)
    pair_queries, key_value = pair_spread[0], pair_spread[1:]
    if lat_size == 8:
        across_x = [(i, i ^ 2) for i in range(lat_size)]
        across_y = [(i, i ^ 4) for i in range(lat_size)]
        from_x = lax.ppermute(key_value, "lat", across_x)
        from_y = lax.ppermute(key_value, "lat", across_y)
        middle = key_value.shape[1] // 2
        diagonal_low = lax.ppermute(from_y[:, :middle], "lat", across_x)
        diagonal_high = lax.ppermute(from_x[:, middle:], "lat", across_y)
        key_groups = [[key_value], [from_x], [from_y], [diagonal_low, diagonal_high]]
    else:
        remote_chunks = [
            lax.ppermute(key_value, "lat", [(i, i ^ (2 * d)) for i in range(lat_size)])
            for d in range(1, lat_size // 2)
        ]
        key_groups = [[key_value]] + [[chunk] for chunk in remote_chunks]
    local_heads = half // head_size
    head_first = (lax.axis_index("lon") * 2 + core) * local_heads
    scales = lax.dynamic_slice_in_dim(head_scale, head_first, local_heads) / math.sqrt(head_size)
    parts = [
        attend_part(
            pair_queries,
            [chunk[0] for chunk in group],
            [chunk[1] for chunk in group],
            scales,
            head_size,
        )
        for group in key_groups
        if group
    ]
    pair_attended = merge_parts(parts)
    token_count = spread.shape[1]
    own_part = pair_attended[:token_count]
    returned = lax.ppermute(pair_attended[token_count:], "lat", partner)
    attended_heads = jnp.where(
        core == 0,
        jnp.concatenate([own_part, returned], axis=1),
        jnp.concatenate([returned, own_part], axis=1),
    )
    token_block = attended_heads.shape[0] // lon_size
    attended = return_blocks(
        [attended_heads[d * token_block : (d + 1) * token_block] for d in range(lon_size)], "lon"
    )
    attended = attended.transpose(1, 0, 2).reshape(token_block, model_width)
    latent_two = (
        latent_wide + jnp.dot(attended, output_weight, preferred_element_type=jnp.float32)
    ).astype(jnp.bfloat16)
    latent_grid = latent_two.reshape(lat_rows // 4, lon_cols // 4, model_width)
    decoder_output = jax.nn.gelu(
        jnp.einsum("pqd,dabh->hpaqb", latent_grid, patch_out, preferred_element_type=jnp.float32)
    )
    decoder_output = decoder_output.reshape(conv_count, lat_rows, lon_cols).astype(jnp.bfloat16)
    decoder_output_padded = halo_padded(decoder_output, 1)
    estimated_maps = fields.astype(jnp.float32) + convolution_kernel_taps(
        decoder_output_padded, final_convolution_result
    )
    prediction = estimated_maps.astype(jnp.bfloat16)
    estimate_misfit = estimated_maps - goal_state.astype(jnp.float32)
    point_mismatch = (
        jnp.sum(estimate_misfit * estimate_misfit, axis=0)
        * meridian_area_factor(rows_total, row_first, lat_rows)[:, None]
    )
    region_count = region_class.shape[0]
    region_onehot = (
        region_mask.reshape(1, -1) == jnp.arange(region_count, dtype=jnp.int32)[:, None]
    ).astype(jnp.float32)
    factor = REG_DEV / (var_count * lat_rows * lon_cols)
    partial_loss = (
        jnp.dot(region_onehot, point_mismatch.reshape(-1), precision=lax.Precision.HIGHEST) * factor
    )
    region_loss = butterfly_sum(butterfly_sum(partial_loss, "lon"), "lat")
    class_onehot = (region_class[None, :] == jnp.arange(CLASSES, dtype=jnp.int32)[:, None]).astype(
        jnp.float32
    )
    class_loss = jnp.dot(class_onehot, region_loss, precision=lax.Precision.HIGHEST)
    return (prediction, region_loss, class_loss)


def solution(mesh):
    return jax.shard_map(
        on_device,
        mesh=mesh,
        in_specs=(
            P(None, "lat", "lon"),
            P(None, "lat", "lon"),
            P("lat", "lon"),
            P(),
            P(),
            P(),
            P(),
            P(),
            P(),
            P(),
            P(),
            P(),
            P(),
            P(),
            P(),
        ),
        out_specs=(P(None, "lat", "lon"), P(), P()),
        check_vma=False,
    )
```

```python
import functools
import math

import jax
import jax.numpy as jnp
from jax import lax
from jax.experimental import pallas as pl
from jax.experimental.pallas import tpu as pltpu
from jax.sharding import PartitionSpec as P

HEADS = 16
CLASSES = 8
REG_DEV = 2


def halo_padded(array, width):
    lat_size, lon_size = lax.axis_size("lat"), lax.axis_size("lon")
    down = [(i, i + 1) for i in range(lat_size - 1)]
    up = [(i + 1, i) for i in range(lat_size - 1)]
    from_above = lax.ppermute(array[:, -width:], "lat", down)
    from_below = lax.ppermute(array[:, :width], "lat", up)
    array = jnp.concatenate([from_above, array, from_below], axis=1)
    right = [(j, (j + 1) % lon_size) for j in range(lon_size)]
    left = [((j + 1) % lon_size, j) for j in range(lon_size)]
    from_left = lax.ppermute(array[:, :, -width:], "lon", right)
    from_right = lax.ppermute(array[:, :, :width], "lon", left)
    return jnp.concatenate([from_left, array, from_right], axis=2)


def butterfly_sum(value, axis):
    size, step = lax.axis_size(axis), 1
    while step < size:
        partner = [(i, i ^ step) for i in range(size) if (i ^ step) < size]
        value = value + lax.ppermute(value, axis, partner)
        step *= 2
    return value


def convolution_kernel_taps(padded, weight):
    row_count = padded.shape[1] - 2
    col_count = padded.shape[2] - 2
    result = jnp.zeros((weight.shape[1], row_count, col_count), jnp.float32)
    for tap_index in range(9):
        shift_row = tap_index // 3
        shift_col = tap_index % 3
        window = padded[:, shift_row : shift_row + row_count, shift_col : shift_col + col_count]
        result = result + jnp.einsum(
            "oc,cyx->oyx", weight[tap_index], window, preferred_element_type=jnp.float32
        )
    return result


def meridian_area_factor(rows_total, row_first, row_count):
    row_index = jnp.arange(row_count).astype(jnp.float32) + jnp.asarray(row_first).astype(
        jnp.float32
    )
    return jnp.cos(math.pi * ((row_index + 0.5) / rows_total - 0.5))


def attention_kernel(scale_ref, q_ref, *refs, head_size, chunk_count):
    key_refs, value_refs = refs[:chunk_count], refs[chunk_count : 2 * chunk_count]
    o_ref, m_ref, l_ref = refs[2 * chunk_count :]
    queries = q_ref[...]
    column_head = lax.broadcasted_iota(jnp.int32, queries.shape, 1) // head_size
    total = jnp.zeros(queries.shape, jnp.float32)
    for head in range(queries.shape[1] // head_size):
        in_head = column_head == head
        masked = jnp.where(in_head, queries, jnp.zeros_like(queries))
        scores = [
            lax.dot_general(
                masked, key_ref[...], (((1,), (1,)), ((), ())), preferred_element_type=jnp.float32
            )
            * scale_ref[head]
            for key_ref in key_refs
        ]
        row_max = functools.reduce(
            jnp.maximum, [jnp.max(score, axis=1, keepdims=True) for score in scores]
        )
        weighted = None
        weight_sum = None
        for score, value_ref in zip(scores, value_refs):
            weights = jnp.exp(score - row_max)
            chunk_sum = jnp.sum(weights, axis=1, keepdims=True)
            chunk_weighted = jnp.dot(
                weights.astype(jnp.bfloat16), value_ref[...], preferred_element_type=jnp.float32
            )
            weight_sum = chunk_sum if weight_sum is None else weight_sum + chunk_sum
            weighted = chunk_weighted if weighted is None else weighted + chunk_weighted
        total = jnp.where(in_head, weighted, total)
        m_ref[:, head : head + 1] = row_max
        l_ref[:, head : head + 1] = weight_sum
    o_ref[...] = total


def attend_part(queries, key_chunks, value_chunks, scales, head_size):
    query_count, width = queries.shape
    key_count = sum(chunk.shape[0] for chunk in key_chunks)
    cap = 1 << (max(8, (1 << 20) // key_count).bit_length() - 1)
    block = math.gcd(query_count, cap)
    heads = width // head_size
    part = jax.ShapeDtypeStruct((query_count, width), jnp.float32)
    part_spec = pl.BlockSpec((block, width), lambda i: (i, 0))
    stat = jax.ShapeDtypeStruct((query_count, heads), jnp.float32)
    stat_spec = pl.BlockSpec((block, heads), lambda i: (i, 0))
    chunk_specs = [
        pl.BlockSpec((chunk.shape[0], width), lambda i: (0, 0))
        for chunk in list(key_chunks) + list(value_chunks)
    ]
    return pl.pallas_call(
        functools.partial(attention_kernel, head_size=head_size, chunk_count=len(key_chunks)),
        out_shape=(part, stat, stat),
        grid=(query_count // block,),
        in_specs=[
            pl.BlockSpec(memory_space=pltpu.SMEM),
            pl.BlockSpec((block, width), lambda i: (i, 0)),
        ]
        + chunk_specs,
        out_specs=(part_spec, stat_spec, stat_spec),
        compiler_params=pltpu.CompilerParams(vmem_limit_bytes=48 * 1024 * 1024),
        cost_estimate=pl.CostEstimate(
            flops=4 * query_count * key_count * width,
            transcendentals=query_count * key_count * heads,
            bytes_accessed=2 * (query_count * width + 2 * key_count * width)
            + 4 * query_count * (width + 2 * heads),
        ),
    )(scales, queries, *key_chunks, *value_chunks)


def merge_parts(parts, head_size):
    parts = [
        (total, jnp.repeat(maxima, head_size, axis=1), jnp.repeat(sums, head_size, axis=1))
        for total, maxima, sums in parts
    ]
    joint = functools.reduce(jnp.maximum, [maxima for total, maxima, sums in parts])
    rescales = [jnp.exp(maxima - joint) for total, maxima, sums in parts]
    total = sum(part[0] * rescale for part, rescale in zip(parts, rescales))
    weight_sum = sum(part[2] * rescale for part, rescale in zip(parts, rescales))
    return (total / weight_sum).astype(jnp.bfloat16)


def exchange_blocks(blocks, axis):
    size, index = lax.axis_size(axis), lax.axis_index(axis)
    received = [lax.dynamic_index_in_dim(blocks, index, 0, keepdims=False)]
    for shift in range(1, size):
        outgoing = lax.dynamic_index_in_dim(blocks, (index + shift) % size, 0, keepdims=False)
        received.append(
            lax.ppermute(outgoing, axis, [(i, (i + shift) % size) for i in range(size)])
        )
    return received


def return_blocks(blocks, axis):
    size, index = lax.axis_size(axis), lax.axis_index(axis)
    received = [blocks[0]] + [
        lax.ppermute(blocks[shift], axis, [((i + shift) % size, i) for i in range(size)])
        for shift in range(1, size)
    ]
    rotated = jnp.stack(received + received)
    return lax.dynamic_slice_in_dim(rotated, size - index, size, axis=0)


def on_device(
    fields,
    goal_state,
    region_mask,
    region_class,
    entry_filter_stencil,
    conv_mid,
    patch_in,
    norm_gain,
    query_weight,
    key_weight,
    value_weight,
    output_weight,
    head_scale,
    patch_out,
    final_convolution_result,
):
    var_count, lat_rows, lon_cols = fields.shape
    conv_count = entry_filter_stencil.shape[1]
    model_width = query_weight.shape[0]
    head_size = model_width // HEADS
    row_first = lax.axis_index("lat") * lat_rows
    rows_total = lat_rows * lax.axis_size("lat")
    padded = halo_padded(fields, 2)
    hidden_one = jax.nn.gelu(convolution_kernel_taps(padded, entry_filter_stencil))
    extended_row = row_first - 1 + jnp.arange(lat_rows + 2, dtype=jnp.int32)
    inside = (extended_row >= 0) & (extended_row < rows_total)
    hidden_padded = jnp.where(inside[None, :, None], hidden_one, 0.0).astype(jnp.bfloat16)
    hidden_two = jax.nn.gelu(convolution_kernel_taps(hidden_padded, conv_mid)).astype(jnp.bfloat16)
    grouped = hidden_two.reshape(conv_count, lat_rows // 4, 4, lon_cols // 4, 4)
    latent = jnp.einsum(
        "hpaqb,abhd->pqd", grouped, patch_in, preferred_element_type=jnp.float32
    ).astype(jnp.bfloat16)
    latent_flat = latent.reshape(-1, model_width)
    latent_wide = latent_flat.astype(jnp.float32)
    normed = (
        latent_wide
        * lax.rsqrt(jnp.mean(latent_wide * latent_wide, axis=1, keepdims=True) + 1e-06)
        * norm_gain
    ).astype(jnp.bfloat16)
    lon_size = lax.axis_size("lon")
    group_width = model_width // lon_size
    projections = lax.optimization_barrier(
        tuple(
            jnp.dot(normed, weight, preferred_element_type=jnp.float32).astype(jnp.bfloat16)
            for weight in (query_weight, key_weight, value_weight)
        )
    )
    by_group = [p.reshape(-1, lon_size, group_width).transpose(1, 0, 2) for p in projections]
    spread = jnp.concatenate(exchange_blocks(jnp.stack(by_group, axis=1), "lon"), axis=1)
    lat_size = lax.axis_size("lat")
    core = lax.axis_index("lat") % 2
    half = group_width // 2
    partner = [(i, i ^ 1) for i in range(lat_size)]

    def with_partner(spread):
        low, high = spread[..., :half], spread[..., half:]
        mine = jnp.where(core == 0, low, high)
        theirs = jnp.where(core == 0, high, low)
        return jnp.concatenate([mine, lax.ppermute(theirs, "lat", partner)], axis=-2)

    pair_spread = with_partner(spread)
    pair_queries, key_value = pair_spread[0], pair_spread[1:]
    if lat_size == 8:
        across_x = [(i, i ^ 2) for i in range(lat_size)]
        across_y = [(i, i ^ 4) for i in range(lat_size)]
        from_x = lax.ppermute(key_value, "lat", across_x)
        from_y = lax.ppermute(key_value, "lat", across_y)
        middle = key_value.shape[1] // 2
        diagonal_low = lax.ppermute(from_y[:, :middle], "lat", across_x)
        diagonal_high = lax.ppermute(from_x[:, middle:], "lat", across_y)
        key_groups = [[key_value], [from_x], [from_y], [diagonal_low, diagonal_high]]
    else:
        remote_chunks = [
            lax.ppermute(key_value, "lat", [(i, i ^ (2 * d)) for i in range(lat_size)])
            for d in range(1, lat_size // 2)
        ]
        key_groups = [[key_value]] + [[chunk] for chunk in remote_chunks]
    local_heads = half // head_size
    head_first = (lax.axis_index("lon") * 2 + core) * local_heads
    scales = lax.dynamic_slice_in_dim(head_scale, head_first, local_heads) / math.sqrt(head_size)
    parts = [
        attend_part(
            pair_queries,
            [chunk[0] for chunk in group],
            [chunk[1] for chunk in group],
            scales,
            head_size,
        )
        for group in key_groups
        if group
    ]
    pair_attended = merge_parts(parts, head_size)
    token_count = spread.shape[1]
    own_part = pair_attended[:token_count]
    returned = lax.ppermute(pair_attended[token_count:], "lat", partner)
    attended_heads = jnp.where(
        core == 0,
        jnp.concatenate([own_part, returned], axis=1),
        jnp.concatenate([returned, own_part], axis=1),
    )
    token_block = attended_heads.shape[0] // lon_size
    attended = return_blocks(
        [attended_heads[d * token_block : (d + 1) * token_block] for d in range(lon_size)], "lon"
    )
    attended = attended.transpose(1, 0, 2).reshape(token_block, model_width)
    latent_two = (
        latent_wide + jnp.dot(attended, output_weight, preferred_element_type=jnp.float32)
    ).astype(jnp.bfloat16)
    latent_grid = latent_two.reshape(lat_rows // 4, lon_cols // 4, model_width)
    decoder_output = jax.nn.gelu(
        jnp.einsum("pqd,dabh->hpaqb", latent_grid, patch_out, preferred_element_type=jnp.float32)
    )
    decoder_output = decoder_output.reshape(conv_count, lat_rows, lon_cols).astype(jnp.bfloat16)
    decoder_output_padded = halo_padded(decoder_output, 1)
    estimated_maps = fields.astype(jnp.float32) + convolution_kernel_taps(
        decoder_output_padded, final_convolution_result
    )
    prediction = estimated_maps.astype(jnp.bfloat16)
    estimate_misfit = estimated_maps - goal_state.astype(jnp.float32)
    point_mismatch = (
        jnp.sum(estimate_misfit * estimate_misfit, axis=0)
        * meridian_area_factor(rows_total, row_first, lat_rows)[:, None]
    )
    region_count = region_class.shape[0]
    region_onehot = (
        region_mask.reshape(1, -1) == jnp.arange(region_count, dtype=jnp.int32)[:, None]
    ).astype(jnp.float32)
    factor = REG_DEV / (var_count * lat_rows * lon_cols)
    partial_loss = (
        jnp.dot(region_onehot, point_mismatch.reshape(-1), precision=lax.Precision.HIGHEST) * factor
    )
    region_loss = butterfly_sum(butterfly_sum(partial_loss, "lon"), "lat")
    class_onehot = (region_class[None, :] == jnp.arange(CLASSES, dtype=jnp.int32)[:, None]).astype(
        jnp.float32
    )
    class_loss = jnp.dot(class_onehot, region_loss, precision=lax.Precision.HIGHEST)
    return (prediction, region_loss, class_loss)


def solution(mesh):
    return jax.shard_map(
        on_device,
        mesh=mesh,
        in_specs=(
            P(None, "lat", "lon"),
            P(None, "lat", "lon"),
            P("lat", "lon"),
            P(),
            P(),
            P(),
            P(),
            P(),
            P(),
            P(),
            P(),
            P(),
            P(),
            P(),
            P(),
        ),
        out_specs=(P(None, "lat", "lon"), P(), P()),
        check_vma=False,
    )
```

```python
import functools
import math

import jax
import jax.numpy as jnp
from jax import lax
from jax.experimental import pallas as pl
from jax.experimental.pallas import tpu as pltpu
from jax.sharding import PartitionSpec as P

HEADS = 16
CLASSES = 8
REG_DEV = 2


def halo_padded(array, width):
    lat_size, lon_size = lax.axis_size("lat"), lax.axis_size("lon")
    down = [(i, i + 1) for i in range(lat_size - 1)]
    up = [(i + 1, i) for i in range(lat_size - 1)]
    from_above = lax.ppermute(array[:, -width:], "lat", down)
    from_below = lax.ppermute(array[:, :width], "lat", up)
    array = jnp.concatenate([from_above, array, from_below], axis=1)
    right = [(j, (j + 1) % lon_size) for j in range(lon_size)]
    left = [((j + 1) % lon_size, j) for j in range(lon_size)]
    from_left = lax.ppermute(array[:, :, -width:], "lon", right)
    from_right = lax.ppermute(array[:, :, :width], "lon", left)
    return jnp.concatenate([from_left, array, from_right], axis=2)


def butterfly_sum(value, axis):
    size, step = lax.axis_size(axis), 1
    while step < size:
        partner = [(i, i ^ step) for i in range(size) if (i ^ step) < size]
        value = value + lax.ppermute(value, axis, partner)
        step *= 2
    return value


def convolution_kernel_taps(padded, weight):
    row_count = padded.shape[1] - 2
    col_count = padded.shape[2] - 2
    result = jnp.zeros((weight.shape[1], row_count, col_count), jnp.float32)
    for tap_index in range(9):
        shift_row = tap_index // 3
        shift_col = tap_index % 3
        window = padded[:, shift_row : shift_row + row_count, shift_col : shift_col + col_count]
        result = result + jnp.einsum(
            "oc,cyx->oyx", weight[tap_index], window, preferred_element_type=jnp.float32
        )
    return result


def meridian_area_factor(rows_total, row_first, row_count):
    row_index = jnp.arange(row_count).astype(jnp.float32) + jnp.asarray(row_first).astype(
        jnp.float32
    )
    return jnp.cos(math.pi * ((row_index + 0.5) / rows_total - 0.5))


def attention_kernel(scale_ref, q_ref, *refs, head_size, chunk_count):
    key_refs, value_refs = refs[:chunk_count], refs[chunk_count : 2 * chunk_count]
    o_ref, m_ref, l_ref = refs[2 * chunk_count :]
    queries = q_ref[...]
    column_head = lax.broadcasted_iota(jnp.int32, queries.shape, 1) // head_size
    total = jnp.zeros(queries.shape, jnp.float32)
    maxima = jnp.zeros(queries.shape, jnp.float32)
    sums = jnp.zeros(queries.shape, jnp.float32)
    for head in range(queries.shape[1] // head_size):
        in_head = column_head == head
        masked = jnp.where(in_head, queries, jnp.zeros_like(queries))
        scores = [
            lax.dot_general(
                masked, key_ref[...], (((1,), (1,)), ((), ())), preferred_element_type=jnp.float32
            )
            * scale_ref[head]
            for key_ref in key_refs
        ]
        row_max = functools.reduce(
            jnp.maximum, [jnp.max(score, axis=1, keepdims=True) for score in scores]
        )
        weighted = None
        weight_sum = None
        for score, value_ref in zip(scores, value_refs):
            weights = jnp.exp(score - row_max)
            chunk_sum = jnp.sum(weights, axis=1, keepdims=True)
            chunk_weighted = jnp.dot(
                weights.astype(jnp.bfloat16), value_ref[...], preferred_element_type=jnp.float32
            )
            weight_sum = chunk_sum if weight_sum is None else weight_sum + chunk_sum
            weighted = chunk_weighted if weighted is None else weighted + chunk_weighted
        total = jnp.where(in_head, weighted, total)
        maxima = jnp.where(in_head, row_max, maxima)
        sums = jnp.where(in_head, weight_sum, sums)
    o_ref[...] = total
    m_ref[...] = maxima
    l_ref[...] = sums


def attend_part(queries, key_chunks, value_chunks, scales, head_size):
    query_count, width = queries.shape
    key_count = sum(chunk.shape[0] for chunk in key_chunks)
    cap = 1 << (max(8, (1 << 20) // key_count).bit_length() - 1)
    block = math.gcd(query_count, cap)
    heads = width // head_size
    part = jax.ShapeDtypeStruct((query_count, width), jnp.float32)
    part_spec = pl.BlockSpec((block, width), lambda i: (i, 0))
    chunk_specs = [
        pl.BlockSpec((chunk.shape[0], width), lambda i: (0, 0))
        for chunk in list(key_chunks) + list(value_chunks)
    ]
    return pl.pallas_call(
        functools.partial(attention_kernel, head_size=head_size, chunk_count=len(key_chunks)),
        out_shape=(part, part, part),
        grid=(query_count // block,),
        in_specs=[
            pl.BlockSpec(memory_space=pltpu.SMEM),
            pl.BlockSpec((block, width), lambda i: (i, 0)),
        ]
        + chunk_specs,
        out_specs=(part_spec, part_spec, part_spec),
        compiler_params=pltpu.CompilerParams(vmem_limit_bytes=48 * 1024 * 1024),
        cost_estimate=pl.CostEstimate(
            flops=4 * query_count * key_count * width,
            transcendentals=query_count * key_count * heads,
            bytes_accessed=2 * (query_count * width + 2 * key_count * width)
            + 12 * query_count * width,
        ),
    )(scales, queries, *key_chunks, *value_chunks)


def merge_parts(parts):
    joint = functools.reduce(jnp.maximum, [maxima for total, maxima, sums in parts])
    rescales = [jnp.exp(maxima - joint) for total, maxima, sums in parts]
    total = sum(part[0] * rescale for part, rescale in zip(parts, rescales))
    weight_sum = sum(part[2] * rescale for part, rescale in zip(parts, rescales))
    return (total / weight_sum).astype(jnp.bfloat16)


def exchange_blocks(blocks, axis):
    size, index = lax.axis_size(axis), lax.axis_index(axis)
    received = [lax.dynamic_index_in_dim(blocks, index, 0, keepdims=False)]
    for shift in range(1, size):
        outgoing = lax.dynamic_index_in_dim(blocks, (index + shift) % size, 0, keepdims=False)
        received.append(
            lax.ppermute(outgoing, axis, [(i, (i + shift) % size) for i in range(size)])
        )
    return received


def return_blocks(blocks, axis):
    size, index = lax.axis_size(axis), lax.axis_index(axis)
    received = [blocks[0]] + [
        lax.ppermute(blocks[shift], axis, [((i + shift) % size, i) for i in range(size)])
        for shift in range(1, size)
    ]
    rotated = jnp.stack(received + received)
    return lax.dynamic_slice_in_dim(rotated, size - index, size, axis=0)


def on_device(
    fields,
    goal_state,
    region_mask,
    region_class,
    entry_filter_stencil,
    conv_mid,
    patch_in,
    norm_gain,
    query_weight,
    key_weight,
    value_weight,
    output_weight,
    head_scale,
    patch_out,
    final_convolution_result,
):
    var_count, lat_rows, lon_cols = fields.shape
    conv_count = entry_filter_stencil.shape[1]
    model_width = query_weight.shape[0]
    head_size = model_width // HEADS
    row_first = lax.axis_index("lat") * lat_rows
    rows_total = lat_rows * lax.axis_size("lat")
    padded = halo_padded(fields, 2)
    hidden_one = jax.nn.gelu(convolution_kernel_taps(padded, entry_filter_stencil))
    extended_row = row_first - 1 + jnp.arange(lat_rows + 2, dtype=jnp.int32)
    inside = (extended_row >= 0) & (extended_row < rows_total)
    hidden_padded = jnp.where(inside[None, :, None], hidden_one, 0.0).astype(jnp.bfloat16)
    hidden_two = jax.nn.gelu(convolution_kernel_taps(hidden_padded, conv_mid)).astype(jnp.bfloat16)
    grouped = hidden_two.reshape(conv_count, lat_rows // 4, 4, lon_cols // 4, 4)
    latent = jnp.einsum(
        "hpaqb,abhd->pqd", grouped, patch_in, preferred_element_type=jnp.float32
    ).astype(jnp.bfloat16)
    latent_flat = latent.reshape(-1, model_width)
    latent_wide = latent_flat.astype(jnp.float32)
    normed = (
        latent_wide
        * lax.rsqrt(jnp.mean(latent_wide * latent_wide, axis=1, keepdims=True) + 1e-06)
        * norm_gain
    ).astype(jnp.bfloat16)
    lon_size = lax.axis_size("lon")
    group_width = model_width // lon_size
    projections = lax.optimization_barrier(
        tuple(
            jnp.dot(normed, weight, preferred_element_type=jnp.float32).astype(jnp.bfloat16)
            for weight in (query_weight, key_weight, value_weight)
        )
    )
    by_group = [p.reshape(-1, lon_size, group_width).transpose(1, 0, 2) for p in projections]
    spread = jnp.concatenate(exchange_blocks(jnp.stack(by_group, axis=1), "lon"), axis=1)
    lat_size = lax.axis_size("lat")
    core = lax.axis_index("lat") % 2
    half = group_width // 2
    partner = [(i, i ^ 1) for i in range(lat_size)]

    def with_partner(spread):
        low, high = spread[..., :half], spread[..., half:]
        mine = jnp.where(core == 0, low, high)
        theirs = jnp.where(core == 0, high, low)
        return jnp.concatenate([mine, lax.ppermute(theirs, "lat", partner)], axis=-2)

    pair_spread = with_partner(spread)
    pair_queries, key_value = pair_spread[0], pair_spread[1:]
    if lat_size == 8:
        across_x = [(i, i ^ 2) for i in range(lat_size)]
        across_y = [(i, i ^ 4) for i in range(lat_size)]
        from_x = lax.ppermute(key_value, "lat", across_x)
        from_y = lax.ppermute(key_value, "lat", across_y)
        middle = key_value.shape[1] // 2
        diagonal_low = lax.ppermute(from_y[:, :middle], "lat", across_x)
        diagonal_high = lax.ppermute(from_x[:, middle:], "lat", across_y)
        key_groups = [[key_value], [from_x, from_y], [diagonal_low, diagonal_high]]
    else:
        remote_chunks = [
            lax.ppermute(key_value, "lat", [(i, i ^ (2 * d)) for i in range(lat_size)])
            for d in range(1, lat_size // 2)
        ]
        key_groups = [[key_value]] + [[chunk] for chunk in remote_chunks]
    local_heads = half // head_size
    head_first = (lax.axis_index("lon") * 2 + core) * local_heads
    scales = lax.dynamic_slice_in_dim(head_scale, head_first, local_heads) / math.sqrt(head_size)
    parts = [
        attend_part(
            pair_queries,
            [chunk[0] for chunk in group],
            [chunk[1] for chunk in group],
            scales,
            head_size,
        )
        for group in key_groups
        if group
    ]
    pair_attended = merge_parts(parts)
    token_count = spread.shape[1]
    own_part = pair_attended[:token_count]
    returned = lax.ppermute(pair_attended[token_count:], "lat", partner)
    attended_heads = jnp.where(
        core == 0,
        jnp.concatenate([own_part, returned], axis=1),
        jnp.concatenate([returned, own_part], axis=1),
    )
    token_block = attended_heads.shape[0] // lon_size
    attended = return_blocks(
        [attended_heads[d * token_block : (d + 1) * token_block] for d in range(lon_size)], "lon"
    )
    attended = attended.transpose(1, 0, 2).reshape(token_block, model_width)
    latent_two = (
        latent_wide + jnp.dot(attended, output_weight, preferred_element_type=jnp.float32)
    ).astype(jnp.bfloat16)
    latent_grid = latent_two.reshape(lat_rows // 4, lon_cols // 4, model_width)
    decoder_output = jax.nn.gelu(
        jnp.einsum("pqd,dabh->hpaqb", latent_grid, patch_out, preferred_element_type=jnp.float32)
    )
    decoder_output = decoder_output.reshape(conv_count, lat_rows, lon_cols).astype(jnp.bfloat16)
    decoder_output_padded = halo_padded(decoder_output, 1)
    estimated_maps = fields.astype(jnp.float32) + convolution_kernel_taps(
        decoder_output_padded, final_convolution_result
    )
    prediction = estimated_maps.astype(jnp.bfloat16)
    estimate_misfit = estimated_maps - goal_state.astype(jnp.float32)
    point_mismatch = (
        jnp.sum(estimate_misfit * estimate_misfit, axis=0)
        * meridian_area_factor(rows_total, row_first, lat_rows)[:, None]
    )
    region_count = region_class.shape[0]
    region_onehot = (
        region_mask.reshape(1, -1) == jnp.arange(region_count, dtype=jnp.int32)[:, None]
    ).astype(jnp.float32)
    factor = REG_DEV / (var_count * lat_rows * lon_cols)
    partial_loss = (
        jnp.dot(region_onehot, point_mismatch.reshape(-1), precision=lax.Precision.HIGHEST) * factor
    )
    region_loss = butterfly_sum(butterfly_sum(partial_loss, "lon"), "lat")
    class_onehot = (region_class[None, :] == jnp.arange(CLASSES, dtype=jnp.int32)[:, None]).astype(
        jnp.float32
    )
    class_loss = jnp.dot(class_onehot, region_loss, precision=lax.Precision.HIGHEST)
    return (prediction, region_loss, class_loss)


def solution(mesh):
    return jax.shard_map(
        on_device,
        mesh=mesh,
        in_specs=(
            P(None, "lat", "lon"),
            P(None, "lat", "lon"),
            P("lat", "lon"),
            P(),
            P(),
            P(),
            P(),
            P(),
            P(),
            P(),
            P(),
            P(),
            P(),
            P(),
            P(),
        ),
        out_specs=(P(None, "lat", "lon"), P(), P()),
        check_vma=False,
    )
```

```python
import functools
import math

import jax
import jax.numpy as jnp
from jax import lax
from jax.experimental import pallas as pl
from jax.experimental.pallas import tpu as pltpu
from jax.sharding import PartitionSpec as P

HEADS = 16
CLASSES = 8
REG_DEV = 2


def halo_padded(array, width):
    lat_size, lon_size = lax.axis_size("lat"), lax.axis_size("lon")
    down = [(i, i + 1) for i in range(lat_size - 1)]
    up = [(i + 1, i) for i in range(lat_size - 1)]
    from_above = lax.ppermute(array[:, -width:], "lat", down)
    from_below = lax.ppermute(array[:, :width], "lat", up)
    array = jnp.concatenate([from_above, array, from_below], axis=1)
    right = [(j, (j + 1) % lon_size) for j in range(lon_size)]
    left = [((j + 1) % lon_size, j) for j in range(lon_size)]
    from_left = lax.ppermute(array[:, :, -width:], "lon", right)
    from_right = lax.ppermute(array[:, :, :width], "lon", left)
    return jnp.concatenate([from_left, array, from_right], axis=2)


def butterfly_sum(value, axis):
    size, step = lax.axis_size(axis), 1
    while step < size:
        partner = [(i, i ^ step) for i in range(size) if (i ^ step) < size]
        value = value + lax.ppermute(value, axis, partner)
        step *= 2
    return value


def convolution_kernel_taps(padded, weight):
    row_count = padded.shape[1] - 2
    col_count = padded.shape[2] - 2
    result = jnp.zeros((weight.shape[1], row_count, col_count), jnp.float32)
    for tap_index in range(9):
        shift_row = tap_index // 3
        shift_col = tap_index % 3
        window = padded[:, shift_row : shift_row + row_count, shift_col : shift_col + col_count]
        result = result + jnp.einsum(
            "oc,cyx->oyx", weight[tap_index], window, preferred_element_type=jnp.float32
        )
    return result


def meridian_area_factor(rows_total, row_first, row_count):
    row_index = jnp.arange(row_count).astype(jnp.float32) + jnp.asarray(row_first).astype(
        jnp.float32
    )
    return jnp.cos(math.pi * ((row_index + 0.5) / rows_total - 0.5))


def attention_kernel(scale_ref, q_ref, *refs, head_size, chunk_count):
    key_refs, value_refs = refs[:chunk_count], refs[chunk_count : 2 * chunk_count]
    o_ref, m_ref, l_ref = refs[2 * chunk_count :]
    queries = q_ref[...]
    column_head = lax.broadcasted_iota(jnp.int32, queries.shape, 1) // head_size
    total = jnp.zeros(queries.shape, jnp.float32)
    maxima = jnp.zeros(queries.shape, jnp.float32)
    sums = jnp.zeros(queries.shape, jnp.float32)
    for head in range(queries.shape[1] // head_size):
        in_head = column_head == head
        masked = jnp.where(in_head, queries, jnp.zeros_like(queries))
        scores = [
            lax.dot_general(
                masked, key_ref[...], (((1,), (1,)), ((), ())), preferred_element_type=jnp.float32
            )
            * scale_ref[head]
            for key_ref in key_refs
        ]
        row_max = functools.reduce(
            jnp.maximum, [jnp.max(score, axis=1, keepdims=True) for score in scores]
        )
        weighted = None
        weight_sum = None
        for score, value_ref in zip(scores, value_refs):
            weights = jnp.exp(score - row_max)
            chunk_sum = jnp.sum(weights, axis=1, keepdims=True)
            chunk_weighted = jnp.dot(
                weights.astype(jnp.bfloat16), value_ref[...], preferred_element_type=jnp.float32
            )
            weight_sum = chunk_sum if weight_sum is None else weight_sum + chunk_sum
            weighted = chunk_weighted if weighted is None else weighted + chunk_weighted
        total = jnp.where(in_head, weighted, total)
        maxima = jnp.where(in_head, row_max, maxima)
        sums = jnp.where(in_head, weight_sum, sums)
    o_ref[...] = total
    m_ref[...] = maxima
    l_ref[...] = sums


def attend_part(queries, chunks, scales, head_size):
    query_count, width = queries.shape
    key_count = sum(chunk.shape[1] for chunk in chunks)
    cap = 1 << (max(8, (1 << 20) // key_count).bit_length() - 1)
    block = math.gcd(query_count, cap)
    heads = width // head_size
    part = jax.ShapeDtypeStruct((query_count, width), jnp.float32)
    part_spec = pl.BlockSpec((block, width), lambda i: (i, 0))
    chunk_specs = [
        pl.BlockSpec((None, chunk.shape[1], width), lambda i, part=part: (part, 0, 0))
        for part in (0, 1)
        for chunk in chunks
    ]
    return pl.pallas_call(
        functools.partial(attention_kernel, head_size=head_size, chunk_count=len(chunks)),
        out_shape=(part, part, part),
        grid=(query_count // block,),
        in_specs=[
            pl.BlockSpec(memory_space=pltpu.SMEM),
            pl.BlockSpec((block, width), lambda i: (i, 0)),
        ]
        + chunk_specs,
        out_specs=(part_spec, part_spec, part_spec),
        compiler_params=pltpu.CompilerParams(vmem_limit_bytes=48 * 1024 * 1024),
        cost_estimate=pl.CostEstimate(
            flops=4 * query_count * key_count * width,
            transcendentals=query_count * key_count * heads,
            bytes_accessed=2 * (query_count * width + 2 * key_count * width)
            + 12 * query_count * width,
        ),
    )(scales, queries, *chunks, *chunks)


def merge_parts(parts):
    joint = functools.reduce(jnp.maximum, [maxima for total, maxima, sums in parts])
    rescales = [jnp.exp(maxima - joint) for total, maxima, sums in parts]
    total = sum(part[0] * rescale for part, rescale in zip(parts, rescales))
    weight_sum = sum(part[2] * rescale for part, rescale in zip(parts, rescales))
    return (total / weight_sum).astype(jnp.bfloat16)


def exchange_blocks(blocks, axis):
    size, index = lax.axis_size(axis), lax.axis_index(axis)
    received = [lax.dynamic_index_in_dim(blocks, index, 0, keepdims=False)]
    for shift in range(1, size):
        outgoing = lax.dynamic_index_in_dim(blocks, (index + shift) % size, 0, keepdims=False)
        received.append(
            lax.ppermute(outgoing, axis, [(i, (i + shift) % size) for i in range(size)])
        )
    return received


def return_blocks(blocks, axis):
    size, index = lax.axis_size(axis), lax.axis_index(axis)
    received = [blocks[0]] + [
        lax.ppermute(blocks[shift], axis, [((i + shift) % size, i) for i in range(size)])
        for shift in range(1, size)
    ]
    rotated = jnp.stack(received + received)
    return lax.dynamic_slice_in_dim(rotated, size - index, size, axis=0)


def on_device(
    fields,
    goal_state,
    region_mask,
    region_class,
    entry_filter_stencil,
    conv_mid,
    patch_in,
    norm_gain,
    query_weight,
    key_weight,
    value_weight,
    output_weight,
    head_scale,
    patch_out,
    final_convolution_result,
):
    var_count, lat_rows, lon_cols = fields.shape
    conv_count = entry_filter_stencil.shape[1]
    model_width = query_weight.shape[0]
    head_size = model_width // HEADS
    row_first = lax.axis_index("lat") * lat_rows
    rows_total = lat_rows * lax.axis_size("lat")
    padded = halo_padded(fields, 2)
    hidden_one = jax.nn.gelu(convolution_kernel_taps(padded, entry_filter_stencil))
    extended_row = row_first - 1 + jnp.arange(lat_rows + 2, dtype=jnp.int32)
    inside = (extended_row >= 0) & (extended_row < rows_total)
    hidden_padded = jnp.where(inside[None, :, None], hidden_one, 0.0).astype(jnp.bfloat16)
    hidden_two = jax.nn.gelu(convolution_kernel_taps(hidden_padded, conv_mid)).astype(jnp.bfloat16)
    grouped = hidden_two.reshape(conv_count, lat_rows // 4, 4, lon_cols // 4, 4)
    latent = jnp.einsum(
        "hpaqb,abhd->pqd", grouped, patch_in, preferred_element_type=jnp.float32
    ).astype(jnp.bfloat16)
    latent_flat = latent.reshape(-1, model_width)
    latent_wide = latent_flat.astype(jnp.float32)
    normed = (
        latent_wide
        * lax.rsqrt(jnp.mean(latent_wide * latent_wide, axis=1, keepdims=True) + 1e-06)
        * norm_gain
    ).astype(jnp.bfloat16)
    lon_size = lax.axis_size("lon")
    group_width = model_width // lon_size
    projections = lax.optimization_barrier(
        tuple(
            jnp.dot(normed, weight, preferred_element_type=jnp.float32).astype(jnp.bfloat16)
            for weight in (query_weight, key_weight, value_weight)
        )
    )
    by_group = [p.reshape(-1, lon_size, group_width).transpose(1, 0, 2) for p in projections]
    spread = jnp.concatenate(exchange_blocks(jnp.stack(by_group, axis=1), "lon"), axis=1)
    lat_size = lax.axis_size("lat")
    core = lax.axis_index("lat") % 2
    half = group_width // 2
    partner = [(i, i ^ 1) for i in range(lat_size)]

    def with_partner(spread):
        low, high = spread[..., :half], spread[..., half:]
        mine = jnp.where(core == 0, low, high)
        theirs = jnp.where(core == 0, high, low)
        return jnp.concatenate([mine, lax.ppermute(theirs, "lat", partner)], axis=-2)

    pair_spread = with_partner(spread)
    pair_queries, key_value = pair_spread[0], pair_spread[1:]
    if lat_size == 8:
        across_x = [(i, i ^ 2) for i in range(lat_size)]
        across_y = [(i, i ^ 4) for i in range(lat_size)]
        from_x = lax.ppermute(key_value, "lat", across_x)
        from_y = lax.ppermute(key_value, "lat", across_y)
        middle = key_value.shape[1] // 2
        diagonal_low = lax.ppermute(from_y[:, :middle], "lat", across_x)
        diagonal_high = lax.ppermute(from_x[:, middle:], "lat", across_y)
        key_groups = [[key_value], [from_x, from_y], [diagonal_low, diagonal_high]]
    else:
        remote_chunks = [
            lax.ppermute(key_value, "lat", [(i, i ^ (2 * d)) for i in range(lat_size)])
            for d in range(1, lat_size // 2)
        ]
        key_groups = [[key_value]] + [[chunk] for chunk in remote_chunks]
    local_heads = half // head_size
    head_first = (lax.axis_index("lon") * 2 + core) * local_heads
    scales = lax.dynamic_slice_in_dim(head_scale, head_first, local_heads) / math.sqrt(head_size)
    parts = [
        attend_part(pair_queries, group, scales, head_size)
        for group in key_groups
        if group
    ]
    pair_attended = merge_parts(parts)
    token_count = spread.shape[1]
    own_part = pair_attended[:token_count]
    returned = lax.ppermute(pair_attended[token_count:], "lat", partner)
    attended_heads = jnp.where(
        core == 0,
        jnp.concatenate([own_part, returned], axis=1),
        jnp.concatenate([returned, own_part], axis=1),
    )
    token_block = attended_heads.shape[0] // lon_size
    attended = return_blocks(
        [attended_heads[d * token_block : (d + 1) * token_block] for d in range(lon_size)], "lon"
    )
    attended = attended.transpose(1, 0, 2).reshape(token_block, model_width)
    latent_two = (
        latent_wide + jnp.dot(attended, output_weight, preferred_element_type=jnp.float32)
    ).astype(jnp.bfloat16)
    latent_grid = latent_two.reshape(lat_rows // 4, lon_cols // 4, model_width)
    decoder_output = jax.nn.gelu(
        jnp.einsum("pqd,dabh->hpaqb", latent_grid, patch_out, preferred_element_type=jnp.float32)
    )
    decoder_output = decoder_output.reshape(conv_count, lat_rows, lon_cols).astype(jnp.bfloat16)
    decoder_output_padded = halo_padded(decoder_output, 1)
    estimated_maps = fields.astype(jnp.float32) + convolution_kernel_taps(
        decoder_output_padded, final_convolution_result
    )
    prediction = estimated_maps.astype(jnp.bfloat16)
    estimate_misfit = estimated_maps - goal_state.astype(jnp.float32)
    point_mismatch = (
        jnp.sum(estimate_misfit * estimate_misfit, axis=0)
        * meridian_area_factor(rows_total, row_first, lat_rows)[:, None]
    )
    region_count = region_class.shape[0]
    region_onehot = (
        region_mask.reshape(1, -1) == jnp.arange(region_count, dtype=jnp.int32)[:, None]
    ).astype(jnp.float32)
    factor = REG_DEV / (var_count * lat_rows * lon_cols)
    partial_loss = (
        jnp.dot(region_onehot, point_mismatch.reshape(-1), precision=lax.Precision.HIGHEST) * factor
    )
    region_loss = butterfly_sum(butterfly_sum(partial_loss, "lon"), "lat")
    class_onehot = (region_class[None, :] == jnp.arange(CLASSES, dtype=jnp.int32)[:, None]).astype(
        jnp.float32
    )
    class_loss = jnp.dot(class_onehot, region_loss, precision=lax.Precision.HIGHEST)
    return (prediction, region_loss, class_loss)


def solution(mesh):
    return jax.shard_map(
        on_device,
        mesh=mesh,
        in_specs=(
            P(None, "lat", "lon"),
            P(None, "lat", "lon"),
            P("lat", "lon"),
            P(),
            P(),
            P(),
            P(),
            P(),
            P(),
            P(),
            P(),
            P(),
            P(),
            P(),
            P(),
        ),
        out_specs=(P(None, "lat", "lon"), P(), P()),
        check_vma=False,
    )
```

```python
import functools
import math

import jax
import jax.numpy as jnp
from jax import lax
from jax.experimental import pallas as pl
from jax.experimental.pallas import tpu as pltpu
from jax.sharding import PartitionSpec as P

HEADS = 16
CLASSES = 8
REG_DEV = 2


def halo_padded(array, width):
    lat_size, lon_size = lax.axis_size("lat"), lax.axis_size("lon")
    down = [(i, i + 1) for i in range(lat_size - 1)]
    up = [(i + 1, i) for i in range(lat_size - 1)]
    from_above = lax.ppermute(array[:, -width:], "lat", down)
    from_below = lax.ppermute(array[:, :width], "lat", up)
    array = jnp.concatenate([from_above, array, from_below], axis=1)
    right = [(j, (j + 1) % lon_size) for j in range(lon_size)]
    left = [((j + 1) % lon_size, j) for j in range(lon_size)]
    from_left = lax.ppermute(array[:, :, -width:], "lon", right)
    from_right = lax.ppermute(array[:, :, :width], "lon", left)
    return jnp.concatenate([from_left, array, from_right], axis=2)


def butterfly_sum(value, axis):
    size, step = lax.axis_size(axis), 1
    while step < size:
        partner = [(i, i ^ step) for i in range(size) if (i ^ step) < size]
        value = value + lax.ppermute(value, axis, partner)
        step *= 2
    return value


def convolution_kernel_taps(padded, weight):
    row_count = padded.shape[1] - 2
    col_count = padded.shape[2] - 2
    result = jnp.zeros((weight.shape[1], row_count, col_count), jnp.float32)
    for tap_index in range(9):
        shift_row = tap_index // 3
        shift_col = tap_index % 3
        window = padded[:, shift_row : shift_row + row_count, shift_col : shift_col + col_count]
        result = result + jnp.einsum(
            "oc,cyx->oyx", weight[tap_index], window, preferred_element_type=jnp.float32
        )
    return result


def meridian_area_factor(rows_total, row_first, row_count):
    row_index = jnp.arange(row_count).astype(jnp.float32) + jnp.asarray(row_first).astype(
        jnp.float32
    )
    return jnp.cos(math.pi * ((row_index + 0.5) / rows_total - 0.5))


def attention_kernel(scale_ref, q_ref, *refs, head_size, chunk_count):
    key_refs, value_refs = refs[:chunk_count], refs[chunk_count : 2 * chunk_count]
    o_ref, m_ref, l_ref = refs[2 * chunk_count :]
    queries = q_ref[...]
    column_head = lax.broadcasted_iota(jnp.int32, queries.shape, 1) // head_size
    total = jnp.zeros(queries.shape, jnp.float32)
    maxima = jnp.zeros(queries.shape, jnp.float32)
    sums = jnp.zeros(queries.shape, jnp.float32)
    for head in range(queries.shape[1] // head_size):
        in_head = column_head == head
        masked = jnp.where(in_head, queries, jnp.zeros_like(queries))
        scores = [
            lax.dot_general(
                masked, key_ref[...], (((1,), (1,)), ((), ())), preferred_element_type=jnp.float32
            )
            * scale_ref[head]
            for key_ref in key_refs
        ]
        row_max = functools.reduce(
            jnp.maximum, [jnp.max(score, axis=1, keepdims=True) for score in scores]
        )
        weighted = None
        weight_sum = None
        for score, value_ref in zip(scores, value_refs):
            weights = jnp.exp(score - row_max)
            chunk_sum = jnp.sum(weights, axis=1, keepdims=True)
            chunk_weighted = jnp.dot(
                weights.astype(jnp.bfloat16), value_ref[...], preferred_element_type=jnp.float32
            )
            weight_sum = chunk_sum if weight_sum is None else weight_sum + chunk_sum
            weighted = chunk_weighted if weighted is None else weighted + chunk_weighted
        total = jnp.where(in_head, weighted, total)
        maxima = jnp.where(in_head, row_max, maxima)
        sums = jnp.where(in_head, weight_sum, sums)
    o_ref[...] = total
    m_ref[...] = maxima
    l_ref[...] = sums


def attend_part(queries, key_chunks, value_chunks, scales, head_size):
    query_count, width = queries.shape
    key_count = sum(chunk.shape[0] for chunk in key_chunks)
    cap = 1 << (max(8, (1 << 20) // key_count).bit_length() - 1)
    block = math.gcd(query_count, cap)
    heads = width // head_size
    part = jax.ShapeDtypeStruct((query_count, width), jnp.float32)
    part_spec = pl.BlockSpec((block, width), lambda i: (i, 0))
    chunk_specs = [
        pl.BlockSpec((chunk.shape[0], width), lambda i: (0, 0))
        for chunk in list(key_chunks) + list(value_chunks)
    ]
    return pl.pallas_call(
        functools.partial(attention_kernel, head_size=head_size, chunk_count=len(key_chunks)),
        out_shape=(part, part, part),
        grid=(query_count // block,),
        in_specs=[
            pl.BlockSpec(memory_space=pltpu.SMEM),
            pl.BlockSpec((block, width), lambda i: (i, 0)),
        ]
        + chunk_specs,
        out_specs=(part_spec, part_spec, part_spec),
        compiler_params=pltpu.CompilerParams(vmem_limit_bytes=48 * 1024 * 1024),
        cost_estimate=pl.CostEstimate(
            flops=4 * query_count * key_count * width,
            transcendentals=query_count * key_count * heads,
            bytes_accessed=2 * (query_count * width + 2 * key_count * width)
            + 12 * query_count * width,
        ),
    )(scales, queries, *key_chunks, *value_chunks)


def merge_parts(parts):
    joint = functools.reduce(jnp.maximum, [maxima for total, maxima, sums in parts])
    rescales = [jnp.exp(maxima - joint) for total, maxima, sums in parts]
    total = sum(part[0] * rescale for part, rescale in zip(parts, rescales))
    weight_sum = sum(part[2] * rescale for part, rescale in zip(parts, rescales))
    return (total / weight_sum).astype(jnp.bfloat16)


def exchange_blocks(blocks, axis):
    size, index = lax.axis_size(axis), lax.axis_index(axis)
    received = [lax.dynamic_index_in_dim(blocks, index, 0, keepdims=False)]
    for shift in range(1, size):
        outgoing = lax.dynamic_index_in_dim(blocks, (index + shift) % size, 0, keepdims=False)
        received.append(
            lax.ppermute(outgoing, axis, [(i, (i + shift) % size) for i in range(size)])
        )
    return received


def return_blocks(blocks, axis):
    size, index = lax.axis_size(axis), lax.axis_index(axis)
    received = [blocks[0]] + [
        lax.ppermute(blocks[shift], axis, [((i + shift) % size, i) for i in range(size)])
        for shift in range(1, size)
    ]
    rotated = jnp.stack(received + received)
    return lax.dynamic_slice_in_dim(rotated, size - index, size, axis=0)


def on_device(
    fields,
    goal_state,
    region_mask,
    region_class,
    entry_filter_stencil,
    conv_mid,
    patch_in,
    norm_gain,
    query_weight,
    key_weight,
    value_weight,
    output_weight,
    head_scale,
    patch_out,
    final_convolution_result,
):
    var_count, lat_rows, lon_cols = fields.shape
    conv_count = entry_filter_stencil.shape[1]
    model_width = query_weight.shape[0]
    head_size = model_width // HEADS
    row_first = lax.axis_index("lat") * lat_rows
    rows_total = lat_rows * lax.axis_size("lat")
    padded = halo_padded(fields, 2)
    hidden_one = jax.nn.gelu(convolution_kernel_taps(padded, entry_filter_stencil))
    extended_row = row_first - 1 + jnp.arange(lat_rows + 2, dtype=jnp.int32)
    inside = (extended_row >= 0) & (extended_row < rows_total)
    hidden_padded = jnp.where(inside[None, :, None], hidden_one, 0.0).astype(jnp.bfloat16)
    hidden_two = jax.nn.gelu(convolution_kernel_taps(hidden_padded, conv_mid)).astype(jnp.bfloat16)
    grouped = hidden_two.reshape(conv_count, lat_rows // 4, 4, lon_cols // 4, 4)
    latent = jnp.einsum(
        "hpaqb,abhd->pqd", grouped, patch_in, preferred_element_type=jnp.float32
    ).astype(jnp.bfloat16)
    latent_flat = latent.reshape(-1, model_width)
    latent_wide = latent_flat.astype(jnp.float32)
    normed = (
        latent_wide
        * lax.rsqrt(jnp.mean(latent_wide * latent_wide, axis=1, keepdims=True) + 1e-06)
        * norm_gain
    ).astype(jnp.bfloat16)
    lon_size = lax.axis_size("lon")
    group_width = model_width // lon_size
    projections = lax.optimization_barrier(
        tuple(
            jnp.dot(normed, weight, preferred_element_type=jnp.float32).astype(jnp.bfloat16)
            for weight in (query_weight, key_weight, value_weight)
        )
    )
    by_group = [p.reshape(-1, lon_size, group_width).transpose(1, 0, 2) for p in projections]
    spread = jnp.concatenate(exchange_blocks(jnp.stack(by_group, axis=1), "lon"), axis=1)
    lat_size = lax.axis_size("lat")
    core = lax.axis_index("lat") % 2
    half = group_width // 2
    partner = [(i, i ^ 1) for i in range(lat_size)]

    def with_partner(spread):
        low, high = spread[..., :half], spread[..., half:]
        mine = jnp.where(core == 0, low, high)
        theirs = jnp.where(core == 0, high, low)
        return jnp.concatenate([mine, lax.ppermute(theirs, "lat", partner)], axis=-2)

    pair_spread = with_partner(spread)
    pair_queries, key_value = pair_spread[0], pair_spread[1:]
    if lat_size == 8:
        across_x = [(i, i ^ 2) for i in range(lat_size)]
        across_y = [(i, i ^ 4) for i in range(lat_size)]
        from_x = lax.ppermute(key_value, "lat", across_x)
        from_y = lax.ppermute(key_value, "lat", across_y)
        middle = key_value.shape[1] // 2
        diagonal_low = lax.ppermute(from_y[:, :middle], "lat", across_x)
        diagonal_high = lax.ppermute(from_x[:, middle:], "lat", across_y)
        key_groups = [[key_value], [from_x, from_y], [diagonal_low, diagonal_high]]
    else:
        remote_chunks = [
            lax.ppermute(key_value, "lat", [(i, i ^ (2 * d)) for i in range(lat_size)])
            for d in range(1, lat_size // 2)
        ]
        key_groups = [[key_value]] + [[chunk] for chunk in remote_chunks]
    local_heads = half // head_size
    head_first = (lax.axis_index("lon") * 2 + core) * local_heads
    scales = lax.dynamic_slice_in_dim(head_scale, head_first, local_heads) / math.sqrt(head_size)
    parts = [
        attend_part(
            pair_queries,
            [chunk[0] for chunk in group],
            [chunk[1] for chunk in group],
            scales,
            head_size,
        )
        for group in key_groups
        if group
    ]
    pair_attended = merge_parts(parts)
    token_count = spread.shape[1]
    token_block = token_count // lon_size
    lon_index = lax.axis_index("lon")
    own_blocks = [pair_attended[d * token_block : (d + 1) * token_block] for d in range(lon_size)]
    partner_blocks = [
        pair_attended[token_count + d * token_block : token_count + (d + 1) * token_block]
        for d in range(lon_size)
    ]
    grid = ("lat", "lon")
    by_shift = []
    for shift in range(lon_size):
        own = own_blocks[0] if shift == 0 else lax.ppermute(
            own_blocks[shift], "lon", [((i + shift) % lon_size, i) for i in range(lon_size)]
        )
        other = lax.ppermute(
            partner_blocks[shift],
            grid,
            [
                (l * lon_size + j, (l ^ 1) * lon_size + (j - shift) % lon_size)
                for l in range(lat_size)
                for j in range(lon_size)
            ],
        )
        by_shift.append(
            jnp.where(
                core == 0,
                jnp.concatenate([own, other], axis=1),
                jnp.concatenate([other, own], axis=1),
            )
        )
    rotated = jnp.stack(by_shift + by_shift)
    attended = lax.dynamic_slice_in_dim(rotated, lon_size - lon_index, lon_size, axis=0)
    attended = attended.transpose(1, 0, 2).reshape(token_block, model_width)
    latent_two = (
        latent_wide + jnp.dot(attended, output_weight, preferred_element_type=jnp.float32)
    ).astype(jnp.bfloat16)
    latent_grid = latent_two.reshape(lat_rows // 4, lon_cols // 4, model_width)
    decoder_output = jax.nn.gelu(
        jnp.einsum("pqd,dabh->hpaqb", latent_grid, patch_out, preferred_element_type=jnp.float32)
    )
    decoder_output = decoder_output.reshape(conv_count, lat_rows, lon_cols).astype(jnp.bfloat16)
    decoder_output_padded = halo_padded(decoder_output, 1)
    estimated_maps = fields.astype(jnp.float32) + convolution_kernel_taps(
        decoder_output_padded, final_convolution_result
    )
    prediction = estimated_maps.astype(jnp.bfloat16)
    estimate_misfit = estimated_maps - goal_state.astype(jnp.float32)
    point_mismatch = (
        jnp.sum(estimate_misfit * estimate_misfit, axis=0)
        * meridian_area_factor(rows_total, row_first, lat_rows)[:, None]
    )
    region_count = region_class.shape[0]
    region_onehot = (
        region_mask.reshape(1, -1) == jnp.arange(region_count, dtype=jnp.int32)[:, None]
    ).astype(jnp.float32)
    factor = REG_DEV / (var_count * lat_rows * lon_cols)
    partial_loss = (
        jnp.dot(region_onehot, point_mismatch.reshape(-1), precision=lax.Precision.HIGHEST) * factor
    )
    region_loss = butterfly_sum(butterfly_sum(partial_loss, "lon"), "lat")
    class_onehot = (region_class[None, :] == jnp.arange(CLASSES, dtype=jnp.int32)[:, None]).astype(
        jnp.float32
    )
    class_loss = jnp.dot(class_onehot, region_loss, precision=lax.Precision.HIGHEST)
    return (prediction, region_loss, class_loss)


def solution(mesh):
    return jax.shard_map(
        on_device,
        mesh=mesh,
        in_specs=(
            P(None, "lat", "lon"),
            P(None, "lat", "lon"),
            P("lat", "lon"),
            P(),
            P(),
            P(),
            P(),
            P(),
            P(),
            P(),
            P(),
            P(),
            P(),
            P(),
            P(),
        ),
        out_specs=(P(None, "lat", "lon"), P(), P()),
        check_vma=False,
    )
```

```python
import functools
import math

import jax
import jax.numpy as jnp
from jax import lax
from jax.experimental import pallas as pl
from jax.experimental.pallas import tpu as pltpu
from jax.sharding import PartitionSpec as P

HEADS = 16
CLASSES = 8
REG_DEV = 2


def halo_padded(array, width):
    lat_size, lon_size = lax.axis_size("lat"), lax.axis_size("lon")
    down = [(i, i + 1) for i in range(lat_size - 1)]
    up = [(i + 1, i) for i in range(lat_size - 1)]
    from_above = lax.ppermute(array[:, -width:], "lat", down)
    from_below = lax.ppermute(array[:, :width], "lat", up)
    array = jnp.concatenate([from_above, array, from_below], axis=1)
    right = [(j, (j + 1) % lon_size) for j in range(lon_size)]
    left = [((j + 1) % lon_size, j) for j in range(lon_size)]
    from_left = lax.ppermute(array[:, :, -width:], "lon", right)
    from_right = lax.ppermute(array[:, :, :width], "lon", left)
    return jnp.concatenate([from_left, array, from_right], axis=2)


def butterfly_sum(value, axis):
    size, step = lax.axis_size(axis), 1
    while step < size:
        partner = [(i, i ^ step) for i in range(size) if (i ^ step) < size]
        value = value + lax.ppermute(value, axis, partner)
        step *= 2
    return value


def convolution_kernel_taps(padded, weight):
    row_count = padded.shape[1] - 2
    col_count = padded.shape[2] - 2
    result = jnp.zeros((weight.shape[1], row_count, col_count), jnp.float32)
    for tap_index in range(9):
        shift_row = tap_index // 3
        shift_col = tap_index % 3
        window = padded[:, shift_row : shift_row + row_count, shift_col : shift_col + col_count]
        result = result + jnp.einsum(
            "oc,cyx->oyx", weight[tap_index], window, preferred_element_type=jnp.float32
        )
    return result


def meridian_area_factor(rows_total, row_first, row_count):
    row_index = jnp.arange(row_count).astype(jnp.float32) + jnp.asarray(row_first).astype(
        jnp.float32
    )
    return jnp.cos(math.pi * ((row_index + 0.5) / rows_total - 0.5))


def attention_kernel(scale_ref, q_ref, *refs, head_size, chunk_count):
    key_refs, value_refs = refs[:chunk_count], refs[chunk_count : 2 * chunk_count]
    o_ref, m_ref, l_ref = refs[2 * chunk_count :]
    queries = q_ref[...]
    column_head = lax.broadcasted_iota(jnp.int32, queries.shape, 1) // head_size
    total = jnp.zeros(queries.shape, jnp.float32)
    maxima = jnp.zeros(queries.shape, jnp.float32)
    sums = jnp.zeros(queries.shape, jnp.float32)
    for head in range(queries.shape[1] // head_size):
        in_head = column_head == head
        masked = jnp.where(in_head, queries, jnp.zeros_like(queries))
        scores = [
            lax.dot_general(
                masked, key_ref[...], (((1,), (1,)), ((), ())), preferred_element_type=jnp.float32
            )
            * scale_ref[head]
            for key_ref in key_refs
        ]
        row_max = functools.reduce(
            jnp.maximum, [jnp.max(score, axis=1, keepdims=True) for score in scores]
        )
        weighted = None
        weight_sum = None
        for score, value_ref in zip(scores, value_refs):
            weights = jnp.exp(score - row_max)
            chunk_sum = jnp.sum(weights, axis=1, keepdims=True)
            chunk_weighted = jnp.dot(
                weights.astype(jnp.bfloat16), value_ref[...], preferred_element_type=jnp.float32
            )
            weight_sum = chunk_sum if weight_sum is None else weight_sum + chunk_sum
            weighted = chunk_weighted if weighted is None else weighted + chunk_weighted
        total = jnp.where(in_head, weighted, total)
        maxima = jnp.where(in_head, row_max, maxima)
        sums = jnp.where(in_head, weight_sum, sums)
    o_ref[...] = total
    m_ref[...] = maxima
    l_ref[...] = sums


def attend_part(queries, key_chunks, value_chunks, scales, head_size):
    query_count, width = queries.shape
    key_count = sum(chunk.shape[0] for chunk in key_chunks)
    cap = 1 << (max(8, (1 << 20) // key_count).bit_length() - 1)
    block = math.gcd(query_count, cap)
    heads = width // head_size
    part = jax.ShapeDtypeStruct((query_count, width), jnp.float32)
    part_spec = pl.BlockSpec((block, width), lambda i: (i, 0))
    chunk_specs = [
        pl.BlockSpec((chunk.shape[0], width), lambda i: (0, 0))
        for chunk in list(key_chunks) + list(value_chunks)
    ]
    return pl.pallas_call(
        functools.partial(attention_kernel, head_size=head_size, chunk_count=len(key_chunks)),
        out_shape=(part, part, part),
        grid=(query_count // block,),
        in_specs=[
            pl.BlockSpec(memory_space=pltpu.SMEM),
            pl.BlockSpec((block, width), lambda i: (i, 0)),
        ]
        + chunk_specs,
        out_specs=(part_spec, part_spec, part_spec),
        compiler_params=pltpu.CompilerParams(vmem_limit_bytes=48 * 1024 * 1024),
        cost_estimate=pl.CostEstimate(
            flops=4 * query_count * key_count * width,
            transcendentals=query_count * key_count * heads,
            bytes_accessed=2 * (query_count * width + 2 * key_count * width)
            + 12 * query_count * width,
        ),
    )(scales, queries, *key_chunks, *value_chunks)


def merge_parts(parts):
    joint = functools.reduce(jnp.maximum, [maxima for total, maxima, sums in parts])
    rescales = [jnp.exp(maxima - joint) for total, maxima, sums in parts]
    total = sum(part[0] * rescale for part, rescale in zip(parts, rescales))
    weight_sum = sum(part[2] * rescale for part, rescale in zip(parts, rescales))
    return (total / weight_sum).astype(jnp.bfloat16)


def exchange_blocks(blocks, axis):
    size, index = lax.axis_size(axis), lax.axis_index(axis)
    received = [lax.dynamic_index_in_dim(blocks, index, 0, keepdims=False)]
    for shift in range(1, size):
        outgoing = lax.dynamic_index_in_dim(blocks, (index + shift) % size, 0, keepdims=False)
        received.append(
            lax.ppermute(outgoing, axis, [(i, (i + shift) % size) for i in range(size)])
        )
    return received


def return_blocks(blocks, axis):
    size, index = lax.axis_size(axis), lax.axis_index(axis)
    received = [blocks[0]] + [
        lax.ppermute(blocks[shift], axis, [((i + shift) % size, i) for i in range(size)])
        for shift in range(1, size)
    ]
    rotated = jnp.stack(received + received)
    return lax.dynamic_slice_in_dim(rotated, size - index, size, axis=0)


def on_device(
    fields,
    goal_state,
    region_mask,
    region_class,
    entry_filter_stencil,
    conv_mid,
    patch_in,
    norm_gain,
    query_weight,
    key_weight,
    value_weight,
    output_weight,
    head_scale,
    patch_out,
    final_convolution_result,
):
    var_count, lat_rows, lon_cols = fields.shape
    conv_count = entry_filter_stencil.shape[1]
    model_width = query_weight.shape[0]
    head_size = model_width // HEADS
    row_first = lax.axis_index("lat") * lat_rows
    rows_total = lat_rows * lax.axis_size("lat")
    padded = halo_padded(fields, 2)
    hidden_one = jax.nn.gelu(convolution_kernel_taps(padded, entry_filter_stencil))
    extended_row = row_first - 1 + jnp.arange(lat_rows + 2, dtype=jnp.int32)
    inside = (extended_row >= 0) & (extended_row < rows_total)
    hidden_padded = jnp.where(inside[None, :, None], hidden_one, 0.0).astype(jnp.bfloat16)
    hidden_two = jax.nn.gelu(convolution_kernel_taps(hidden_padded, conv_mid)).astype(jnp.bfloat16)
    grouped = hidden_two.reshape(conv_count, lat_rows // 4, 4, lon_cols // 4, 4)
    latent = jnp.einsum(
        "hpaqb,abhd->pqd", grouped, patch_in, preferred_element_type=jnp.float32
    ).astype(jnp.bfloat16)
    latent_flat = latent.reshape(-1, model_width)
    latent_wide = latent_flat.astype(jnp.float32)
    normed = (
        latent_wide
        * lax.rsqrt(jnp.mean(latent_wide * latent_wide, axis=1, keepdims=True) + 1e-06)
        * norm_gain
    ).astype(jnp.bfloat16)
    lon_size = lax.axis_size("lon")
    group_width = model_width // lon_size
    projections = lax.optimization_barrier(
        tuple(
            jnp.dot(normed, weight, preferred_element_type=jnp.float32).astype(jnp.bfloat16)
            for weight in (query_weight, key_weight, value_weight)
        )
    )
    by_group = [p.reshape(-1, lon_size, group_width).transpose(1, 0, 2) for p in projections]
    spread = jnp.concatenate(exchange_blocks(jnp.stack(by_group, axis=1), "lon"), axis=1)
    lat_size = lax.axis_size("lat")
    core = lax.axis_index("lat") % 2
    half = group_width // 2
    partner = [(i, i ^ 1) for i in range(lat_size)]

    def with_partner(spread):
        low, high = spread[..., :half], spread[..., half:]
        mine = jnp.where(core == 0, low, high)
        theirs = jnp.where(core == 0, high, low)
        return jnp.concatenate([mine, lax.ppermute(theirs, "lat", partner)], axis=-2)

    pair_spread = with_partner(spread)
    pair_queries, key_value = pair_spread[0], pair_spread[1:]
    if lat_size == 8:
        across_x = [(i, i ^ 2) for i in range(lat_size)]
        across_y = [(i, i ^ 4) for i in range(lat_size)]
        from_x = lax.ppermute(key_value, "lat", across_x)
        from_y = lax.ppermute(key_value, "lat", across_y)
        middle = key_value.shape[1] // 2
        diagonal_low = lax.ppermute(from_y[:, :middle], "lat", across_x)
        diagonal_high = lax.ppermute(from_x[:, middle:], "lat", across_y)
        key_groups = [[key_value], [from_x, from_y], [diagonal_low, diagonal_high]]
    else:
        remote_chunks = [
            lax.ppermute(key_value, "lat", [(i, i ^ (2 * d)) for i in range(lat_size)])
            for d in range(1, lat_size // 2)
        ]
        key_groups = [[key_value]] + [[chunk] for chunk in remote_chunks]
    local_heads = half // head_size
    head_first = (lax.axis_index("lon") * 2 + core) * local_heads
    scales = lax.dynamic_slice_in_dim(head_scale, head_first, local_heads) / math.sqrt(head_size)
    parts = [
        attend_part(
            pair_queries,
            [chunk[0] for chunk in group],
            [chunk[1] for chunk in group],
            scales,
            head_size,
        )
        for group in key_groups
        if group
    ]
    half_rows = pair_queries.shape[0] // 2
    partner_rows = merge_parts([tuple(x[half_rows:] for x in part) for part in parts])
    own_rows = merge_parts([tuple(x[:half_rows] for x in part) for part in parts])
    pair_attended = jnp.concatenate([own_rows, partner_rows], axis=0)
    token_count = spread.shape[1]
    own_part = pair_attended[:token_count]
    returned = lax.ppermute(pair_attended[token_count:], "lat", partner)
    attended_heads = jnp.where(
        core == 0,
        jnp.concatenate([own_part, returned], axis=1),
        jnp.concatenate([returned, own_part], axis=1),
    )
    token_block = attended_heads.shape[0] // lon_size
    attended = return_blocks(
        [attended_heads[d * token_block : (d + 1) * token_block] for d in range(lon_size)], "lon"
    )
    attended = attended.transpose(1, 0, 2).reshape(token_block, model_width)
    latent_two = (
        latent_wide + jnp.dot(attended, output_weight, preferred_element_type=jnp.float32)
    ).astype(jnp.bfloat16)
    latent_grid = latent_two.reshape(lat_rows // 4, lon_cols // 4, model_width)
    decoder_output = jax.nn.gelu(
        jnp.einsum("pqd,dabh->hpaqb", latent_grid, patch_out, preferred_element_type=jnp.float32)
    )
    decoder_output = decoder_output.reshape(conv_count, lat_rows, lon_cols).astype(jnp.bfloat16)
    decoder_output_padded = halo_padded(decoder_output, 1)
    estimated_maps = fields.astype(jnp.float32) + convolution_kernel_taps(
        decoder_output_padded, final_convolution_result
    )
    prediction = estimated_maps.astype(jnp.bfloat16)
    estimate_misfit = estimated_maps - goal_state.astype(jnp.float32)
    point_mismatch = (
        jnp.sum(estimate_misfit * estimate_misfit, axis=0)
        * meridian_area_factor(rows_total, row_first, lat_rows)[:, None]
    )
    region_count = region_class.shape[0]
    region_onehot = (
        region_mask.reshape(1, -1) == jnp.arange(region_count, dtype=jnp.int32)[:, None]
    ).astype(jnp.float32)
    factor = REG_DEV / (var_count * lat_rows * lon_cols)
    partial_loss = (
        jnp.dot(region_onehot, point_mismatch.reshape(-1), precision=lax.Precision.HIGHEST) * factor
    )
    region_loss = butterfly_sum(butterfly_sum(partial_loss, "lon"), "lat")
    class_onehot = (region_class[None, :] == jnp.arange(CLASSES, dtype=jnp.int32)[:, None]).astype(
        jnp.float32
    )
    class_loss = jnp.dot(class_onehot, region_loss, precision=lax.Precision.HIGHEST)
    return (prediction, region_loss, class_loss)


def solution(mesh):
    return jax.shard_map(
        on_device,
        mesh=mesh,
        in_specs=(
            P(None, "lat", "lon"),
            P(None, "lat", "lon"),
            P("lat", "lon"),
            P(),
            P(),
            P(),
            P(),
            P(),
            P(),
            P(),
            P(),
            P(),
            P(),
            P(),
            P(),
        ),
        out_specs=(P(None, "lat", "lon"), P(), P()),
        check_vma=False,
    )
```
